32 devices in a mesh: seq: 8 (over z, x), head: 4 (over y, core).
Axes of the slice: x: 2, y: 2, z: 4, core: 2. Of those that a mesh axis runs over, the one named last changes fastest.
Arguments:
- queries: bfloat16 [16384, 4096], P(('seq', 'head')), may hold values from -6 to 6, as said below
- keys: bfloat16 [16384, 1024], P(('seq', 'head')), may hold values from -6 to 6, as said below
- values: bfloat16 [16384, 1024], P(('seq', 'head')), may hold values from -6 to 6, as said below
- gate_logit: float32 [32], replicated, may hold values from -3 to 3
Outputs:
- attended: bfloat16 [16384, 4096], P(('seq', 'head'))
The draws below stay inside these ranges and needn't reach their ends.
Inputs may be any that keep to these rules, and one draw needn't show every extreme that they name: queries are real-valued within the stated range. keys are real-valued within the stated range. values are real-valued within the stated range.
All inputs are finite; a program needn't handle non-finite values.
Results may differ from the reference program's by a relative error of at most 0.0034.
Values may be sent and summed in bfloat16 or wider, within the bound.
No kernel may reach another device: no remote copies, remote signals or barrier semaphores. Data moves between devices by JAX's collectives and lax.ppermute only.
A program may use at most 128 MiB of HBM per device.

```python
import jax
import jax.numpy as jnp
from jax import lax

HQ = 32
KVH = 8
HD = 128
SEG = 2048
GROUP = 4
TOKENS = 16384


def rough_base(key, shape):
    return jnp.clip(jax.random.normal(key, shape, jnp.float32), -4.0, 4.0)


def draw_queries(key, part):
    segment_count = TOKENS // SEG
    whole = rough_base(jax.random.fold_in(key, 31), (segment_count, SEG, KVH, GROUP, HD))
    return jnp.clip(whole, -6.0, 6.0).reshape(TOKENS, HQ * HD).astype(jnp.bfloat16)


def draw_keys(key, part):
    segment_count = TOKENS // SEG
    whole = rough_base(jax.random.fold_in(key, 11), (segment_count, SEG, KVH, HD))
    shifts = jax.random.uniform(jax.random.fold_in(key, 12), (segment_count, 1, KVH, HD), jnp.float32, -2.5, 2.5)
    whole = whole + shifts
    return jnp.clip(whole, -6.0, 6.0).reshape(TOKENS, KVH * HD).astype(jnp.bfloat16)


def draw_values(key, part):
    segment_count = TOKENS // SEG
    whole = rough_base(jax.random.fold_in(key, 21), (segment_count, SEG, KVH * HD))
    offsets = jax.random.uniform(jax.random.fold_in(key, 22), (segment_count, 1, KVH * HD), jnp.float32, -2.0, 2.0)
    return jnp.clip(whole + offsets, -6.0, 6.0).reshape(TOKENS, KVH * HD).astype(jnp.bfloat16)


def setup_inputs(seed: int = 0) -> dict:
    key_list = jax.random.split(jax.random.key(seed), 5)
    return {
        "queries": draw_queries(jax.random.fold_in(key_list[4], 71), 0),
        "keys": draw_keys(jax.random.fold_in(key_list[4], 71), 0),
        "values": draw_values(jax.random.fold_in(key_list[4], 71), 0),
        "gate_logit": jnp.clip(jax.random.uniform(key_list[3], (HQ,), jnp.float32, -3.0, 3.0), -3.0, 3.0),
    }


def feature(inputs):
    return jnp.where(inputs > 0, inputs + 1.0, jnp.exp(jnp.minimum(inputs, 0.0)))


def reference(queries, keys, values, gate_logit):
    segment_count = TOKENS // SEG
    highest = lax.Precision.HIGHEST
    key_feature = feature(keys.astype(jnp.float32)).reshape(segment_count, SEG, KVH, HD)
    value_data = values.astype(jnp.float32).reshape(segment_count, SEG, KVH, HD)
    memory_delta = jnp.einsum('stgd,stge->sgde', key_feature, value_data, precision=highest)
    normal_delta = jnp.sum(key_feature, axis=1)
    memory = jnp.concatenate([jnp.zeros_like(memory_delta[:1]), jnp.cumsum(memory_delta, axis=0)[:-1]], axis=0)
    normalizer = jnp.concatenate([jnp.zeros_like(normal_delta[:1]), jnp.cumsum(normal_delta, axis=0)[:-1]], axis=0)
    query_view = queries.reshape(segment_count, SEG, KVH, GROUP, HD)
    key_view = keys.reshape(segment_count, SEG, KVH, HD)
    value_view = values.reshape(segment_count, SEG, KVH, HD)
    gate_share = jax.nn.sigmoid(gate_logit).reshape(KVH, GROUP)
    causal = jnp.arange(SEG, dtype=jnp.int32)[:, None] >= jnp.arange(SEG, dtype=jnp.int32)[None, :]

    def one_item(item_index):
        segment_at = item_index // KVH
        head_at = item_index % KVH
        query_rows = query_view[segment_at, :, head_at].astype(jnp.float32)
        key_rows = key_view[segment_at, :, head_at].astype(jnp.float32)
        value_rows = value_view[segment_at, :, head_at].astype(jnp.float32)
        scores = jnp.einsum('tjd,ud->jtu', query_rows, key_rows, precision=highest) * (HD ** -0.5)
        scores = jnp.where(causal[None], scores, -1e30)
        row_top = jnp.max(scores, axis=-1, keepdims=True)
        exp_scores = jnp.exp(scores - row_top)
        weights = (exp_scores / jnp.sum(exp_scores, axis=-1, keepdims=True)).astype(jnp.bfloat16)
        weights = lax.optimization_barrier(weights).astype(jnp.float32)
        local_part = jnp.einsum('jtu,ud->tjd', weights, value_rows, precision=highest)
        query_feature = feature(query_rows)
        numerator = jnp.einsum('tjd,de->tje', query_feature, memory[segment_at, head_at], precision=highest)
        denominator = jnp.maximum(jnp.einsum('tjd,d->tj', query_feature, normalizer[segment_at, head_at], precision=highest), 1.0)
        retrieved = numerator / denominator[..., None]
        mixing = gate_share[head_at][None, :, None]
        return (mixing * retrieved + (1.0 - mixing) * local_part).astype(jnp.bfloat16)

    blocks = lax.map(one_item, jnp.arange(segment_count * KVH, dtype=jnp.int32))
    blocks = blocks.reshape(segment_count, KVH, SEG, GROUP, HD).transpose(0, 2, 1, 3, 4)
    return blocks.reshape(TOKENS, HQ * HD)
```

```python
import functools
import math

import jax
import jax.numpy as jnp
from jax import lax
from jax.experimental import pallas as pl
from jax.experimental.pallas import tpu as pltpu
from jax.sharding import PartitionSpec as P

HQ = 32
KVH = 8
HD = 128
SEG = 2048
BLOCK = 512


def feature(inputs):
    return jnp.where(inputs > 0, inputs + 1.0, jnp.exp(jnp.minimum(inputs, 0.0)))


def attention_kernel(
    gate_ref, q_ref, k_ref, v_ref, mem_ref, nrm_ref, o_ref, m_sc, l_sc, acc_sc, *, group_size
):
    head = pl.program_id(0)
    q_block = pl.program_id(1)
    k_block = pl.program_id(2)
    score_scale = HD ** (-0.5)

    @pl.when(k_block == 0)
    def _init():
        m_sc[...] = jnp.full(m_sc.shape, -jnp.inf, jnp.float32)
        l_sc[...] = jnp.zeros(l_sc.shape, jnp.float32)
        acc_sc[...] = jnp.zeros(acc_sc.shape, jnp.float32)

    def step(masked):
        scores = (
            lax.dot_general(
                q_ref[...], k_ref[...], (((1,), (1,)), ((), ())),
                preferred_element_type=jnp.float32,
            )
            * score_scale
        )
        if masked:
            rows = lax.broadcasted_iota(jnp.int32, scores.shape, 0)
            cols = lax.broadcasted_iota(jnp.int32, scores.shape, 1)
            scores = jnp.where(cols <= rows, scores, -1e30)
        m_prev = m_sc[...]
        m_new = jnp.maximum(m_prev, jnp.max(scores, axis=-1, keepdims=True))
        probs = jnp.exp(scores - m_new)
        alpha = jnp.exp(m_prev - m_new)
        l_sc[...] = alpha * l_sc[...] + jnp.sum(probs, axis=-1, keepdims=True)
        acc_sc[...] = alpha * acc_sc[...] + jnp.dot(
            probs.astype(jnp.bfloat16), v_ref[...], preferred_element_type=jnp.float32
        )
        m_sc[...] = m_new

    @pl.when(k_block < q_block)
    def _full():
        step(False)

    @pl.when(k_block == q_block)
    def _last():
        step(True)
        local_part = acc_sc[...] / l_sc[...]
        query_feature = feature(q_ref[...].astype(jnp.float32))
        numerator = jnp.dot(
            query_feature, mem_ref[0], precision=lax.Precision.HIGHEST,
            preferred_element_type=jnp.float32,
        )
        denominator = jnp.maximum(
            jnp.sum(query_feature * nrm_ref[0], axis=-1, keepdims=True), 1.0
        )
        mixing = gate_ref[head]
        o_ref[...] = (
            mixing * (numerator / denominator) + (1.0 - mixing) * local_part
        ).astype(o_ref.dtype)


def attention(query_local, key_local, value_local, memory, normalizer, mixing):
    tokens = query_local.shape[0]
    q_heads = query_local.shape[1] // HD
    kv_heads = key_local.shape[1] // HD
    group_size = q_heads // kv_heads
    blocks = tokens // BLOCK
    kernel = functools.partial(attention_kernel, group_size=group_size)
    return pl.pallas_call(
        kernel,
        grid=(q_heads, blocks, blocks),
        in_specs=[
            pl.BlockSpec(memory_space=pltpu.SMEM),
            pl.BlockSpec((BLOCK, HD), lambda h, i, j: (i, h)),
            pl.BlockSpec((BLOCK, HD), lambda h, i, j: (jnp.minimum(j, i), h // group_size)),
            pl.BlockSpec((BLOCK, HD), lambda h, i, j: (jnp.minimum(j, i), h // group_size)),
            pl.BlockSpec((1, HD, HD), lambda h, i, j: (h // group_size, 0, 0)),
            pl.BlockSpec((1, 1, HD), lambda h, i, j: (h // group_size, 0, 0)),
        ],
        out_specs=pl.BlockSpec((BLOCK, HD), lambda h, i, j: (i, h)),
        out_shape=jax.ShapeDtypeStruct(query_local.shape, jnp.bfloat16),
        scratch_shapes=[
            pltpu.VMEM((BLOCK, 1), jnp.float32),
            pltpu.VMEM((BLOCK, 1), jnp.float32),
            pltpu.VMEM((BLOCK, HD), jnp.float32),
        ],
        compiler_params=pltpu.CompilerParams(
            dimension_semantics=("arbitrary", "arbitrary", "arbitrary")
        ),
    )(mixing, query_local, key_local, value_local, memory, normalizer)


def before_states(key_local, value_local):
    kv_heads = key_local.shape[1] // HD
    key_feature = feature(key_local.astype(jnp.float32)).reshape(-1, kv_heads, HD)
    value_data = value_local.astype(jnp.float32).reshape(-1, kv_heads, HD)
    memory_delta = jnp.einsum(
        "tgd,tge->gde", key_feature, value_data, precision=lax.Precision.HIGHEST
    )
    normal_delta = jnp.sum(key_feature, axis=0)
    memory_all = lax.all_gather(memory_delta.astype(jnp.bfloat16), "seq").astype(jnp.float32)
    normal_all = lax.all_gather(normal_delta.astype(jnp.bfloat16), "seq").astype(jnp.float32)
    earlier = (
        jnp.arange(lax.axis_size("seq"), dtype=jnp.int32) < lax.axis_index("seq")
    ).astype(jnp.float32)
    memory = jnp.sum(memory_all * earlier[:, None, None, None], axis=0)
    normalizer = jnp.sum(normal_all * earlier[:, None, None], axis=0)
    return memory, normalizer[:, None, :]


def to_heads(rows, parts):
    tokens_here, cols = rows.shape
    split = rows.reshape(tokens_here, parts, cols // parts).transpose(1, 0, 2)
    gathered = lax.all_to_all(split, "head", split_axis=0, concat_axis=0, tiled=True)
    return gathered.reshape(parts * tokens_here, cols // parts)


def body(queries, keys, values, gate_logit):
    parts = lax.axis_size("head")
    head_place = lax.axis_index("head")
    key_local = to_heads(keys, parts)
    value_local = to_heads(values, parts)
    memory, normalizer = before_states(key_local, value_local)
    query_local = to_heads(queries, parts)
    q_heads = query_local.shape[1] // HD
    mixing = jax.nn.sigmoid(lax.dynamic_slice_in_dim(gate_logit, head_place * q_heads, q_heads))
    attended = attention(query_local, key_local, value_local, memory, normalizer, mixing)
    tokens_here = queries.shape[0]
    cols = attended.shape[1]
    split = attended.reshape(parts, tokens_here, cols)
    returned = lax.all_to_all(split, "head", split_axis=0, concat_axis=0, tiled=True)
    return returned.transpose(1, 0, 2).reshape(tokens_here, parts * cols)


def solution(mesh):
    in_specs = (P(("seq", "head"), None), P(("seq", "head"), None), P(("seq", "head"), None), P())
    out_specs = P(("seq", "head"), None)
    return jax.shard_map(body, mesh=mesh, in_specs=in_specs, out_specs=out_specs, check_vma=False)
```

```python
import functools

import jax
import jax.numpy as jnp
import numpy as np
from jax import lax
from jax.experimental import pallas as pl
from jax.experimental.pallas import tpu as pltpu
from jax.sharding import PartitionSpec as P

HQ = 32
KVH = 8
HD = 128
SEG = 2048
BLOCK = 512
LANES = 128


def feature(inputs):
    return jnp.where(inputs > 0, inputs + 1.0, jnp.exp(jnp.minimum(inputs, 0.0)))


def flash_kernel(qi_ref, kj_ref, q_ref, k_ref, v_ref, o_ref, m_sc, l_sc, acc_sc, *, group_size):
    step_at = pl.program_id(0)
    q_block = qi_ref[step_at]
    k_block = kj_ref[step_at]
    score_scale = HD ** (-0.5)

    @pl.when(k_block == 0)
    def _init():
        m_sc[...] = jnp.full(m_sc.shape, -jnp.inf, jnp.float32)
        l_sc[...] = jnp.zeros(l_sc.shape, jnp.float32)
        acc_sc[...] = jnp.zeros(acc_sc.shape, jnp.float32)

    def step(masked):
        key_rows = k_ref[...]
        value_rows = v_ref[...]
        if masked:
            rows = lax.broadcasted_iota(jnp.int32, (BLOCK, BLOCK), 0)
            cols = lax.broadcasted_iota(jnp.int32, (BLOCK, BLOCK), 1)
            allowed = cols <= rows
        for head in range(group_size):
            lanes = slice(head * HD, (head + 1) * HD)
            scores = (
                lax.dot_general(
                    q_ref[:, lanes], key_rows, (((1,), (1,)), ((), ())),
                    preferred_element_type=jnp.float32,
                )
                * score_scale
            )
            if masked:
                scores = jnp.where(allowed, scores, -1e30)
            m_prev = m_sc[head]
            m_new = jnp.maximum(m_prev, jnp.max(scores, axis=-1, keepdims=True))
            probs = jnp.exp(scores - m_new[:, :1])
            alpha = jnp.exp(m_prev - m_new)
            l_sc[head] = alpha * l_sc[head] + jnp.sum(probs, axis=-1, keepdims=True)
            acc_sc[:, lanes] = alpha * acc_sc[:, lanes] + jnp.dot(
                probs.astype(jnp.bfloat16), value_rows, preferred_element_type=jnp.float32
            )
            m_sc[head] = m_new

    @pl.when(k_block < q_block)
    def _full():
        step(False)

    @pl.when(k_block == q_block)
    def _last():
        step(True)
        for head in range(group_size):
            lanes = slice(head * HD, (head + 1) * HD)
            o_ref[:, lanes] = acc_sc[:, lanes] / l_sc[head]


def local_attention(query_rows, kv_rows, key_col, value_col):
    tokens, width = query_rows.shape
    group_size = width // HD
    blocks = tokens // BLOCK
    pairs = [(i, j) for i in range(blocks) for j in range(i + 1)]
    q_index = jnp.asarray(np.array([p[0] for p in pairs], np.int32))
    k_index = jnp.asarray(np.array([p[1] for p in pairs], np.int32))
    grid_spec = pltpu.PrefetchScalarGridSpec(
        num_scalar_prefetch=2,
        grid=(len(pairs),),
        in_specs=[
            pl.BlockSpec((BLOCK, width), lambda t, qi, kj: (qi[t], 0)),
            pl.BlockSpec((BLOCK, HD), lambda t, qi, kj: (kj[t], key_col)),
            pl.BlockSpec((BLOCK, HD), lambda t, qi, kj: (kj[t], value_col)),
        ],
        out_specs=pl.BlockSpec((BLOCK, width), lambda t, qi, kj: (qi[t], 0)),
        scratch_shapes=[
            pltpu.VMEM((group_size, BLOCK, LANES), jnp.float32),
            pltpu.VMEM((group_size, BLOCK, LANES), jnp.float32),
            pltpu.VMEM((BLOCK, width), jnp.float32),
        ],
    )
    return pl.pallas_call(
        functools.partial(flash_kernel, group_size=group_size),
        grid_spec=grid_spec,
        out_shape=jax.ShapeDtypeStruct((tokens, width), jnp.float32),
        compiler_params=pltpu.CompilerParams(dimension_semantics=("arbitrary",)),
    )(q_index, k_index, query_rows, kv_rows, kv_rows)


def mix(query_rows, local_part, state, mixing):
    tokens, width = query_rows.shape
    group_size = width // HD
    highest = lax.Precision.HIGHEST
    query_feature = feature(query_rows.astype(jnp.float32)).reshape(tokens, group_size, HD)
    numerator = jnp.einsum("tjd,de->tje", query_feature, state[:HD], precision=highest)
    denominator = jnp.maximum(
        jnp.einsum("tjd,d->tj", query_feature, state[HD], precision=highest), 1.0
    )
    retrieved = numerator / denominator[..., None]
    share = mixing[None, :, None]
    attended = share * retrieved + (1.0 - share) * local_part.reshape(tokens, group_size, HD)
    return attended.astype(jnp.bfloat16).reshape(tokens, width)


def before_states(key_local, value_local):
    kv_heads = key_local.shape[1] // HD
    key_feature = feature(key_local.astype(jnp.float32)).reshape(-1, kv_heads, HD)
    value_data = value_local.astype(jnp.float32).reshape(-1, kv_heads, HD)
    memory_delta = jnp.einsum(
        "tgd,tge->gde", key_feature, value_data, precision=lax.Precision.HIGHEST
    )
    normal_delta = jnp.sum(key_feature, axis=0)
    delta = jnp.concatenate([memory_delta, normal_delta[:, None, :]], axis=1)
    gathered = lax.all_gather(delta.astype(jnp.bfloat16), "seq").astype(jnp.float32)
    earlier = (
        jnp.arange(lax.axis_size("seq"), dtype=jnp.int32) < lax.axis_index("seq")
    ).astype(jnp.float32)
    return jnp.sum(gathered * earlier[:, None, None, None], axis=0)


def body(queries, keys, values, gate_logit):
    parts = lax.axis_size("head")
    head_place = lax.axis_index("head")
    tokens_here = queries.shape[0]
    kv_here = keys.shape[1] // (parts * HD)
    group_size = queries.shape[1] // (keys.shape[1])
    kv_split = jnp.stack(
        [keys.reshape(tokens_here, parts, kv_here * HD), values.reshape(tokens_here, parts, kv_here * HD)],
        axis=2,
    ).transpose(1, 0, 2, 3)
    kv_local = lax.all_to_all(kv_split, "head", split_axis=0, concat_axis=0, tiled=True)
    kv_local = kv_local.reshape(parts * tokens_here, 2 * kv_here * HD)
    state = before_states(kv_local[:, : kv_here * HD], kv_local[:, kv_here * HD :])
    mixing = jax.nn.sigmoid(
        lax.dynamic_slice_in_dim(gate_logit, head_place * kv_here * group_size, kv_here * group_size)
    ).reshape(kv_here, group_size)
    width = group_size * HD
    query_split = queries.reshape(tokens_here, parts, kv_here, width)
    returned = []
    for head in range(kv_here):
        query_rows = lax.all_to_all(
            query_split[:, :, head].transpose(1, 0, 2), "head", split_axis=0, concat_axis=0, tiled=True
        ).reshape(parts * tokens_here, width)
        local_part = local_attention(query_rows, kv_local, head, kv_here + head)
        attended = mix(query_rows, local_part, state[head], mixing[head])
        returned.append(
            lax.all_to_all(
                attended.reshape(parts, tokens_here, width), "head", split_axis=0, concat_axis=0, tiled=True
            )
        )
    stacked = jnp.stack(returned, axis=0).transpose(2, 1, 0, 3)
    return stacked.reshape(tokens_here, parts * kv_here * width)


def solution(mesh):
    in_specs = (P(("seq", "head"), None), P(("seq", "head"), None), P(("seq", "head"), None), P())
    out_specs = P(("seq", "head"), None)
    return jax.shard_map(body, mesh=mesh, in_specs=in_specs, out_specs=out_specs, check_vma=False)
```

```python
import functools

import jax
import jax.numpy as jnp
import numpy as np
from jax import lax
from jax.experimental import pallas as pl
from jax.experimental.pallas import tpu as pltpu
from jax.sharding import PartitionSpec as P

HQ = 32
KVH = 8
HD = 128
SEG = 2048
LANES = 128
STATE_ROWS = HD + 8


def feature(inputs):
    return jnp.where(inputs > 0, inputs + 1.0, jnp.exp(jnp.minimum(inputs, 0.0)))


def shifted(value, axis, steps):
    count = lax.axis_size(axis)
    return lax.ppermute(value, axis, [(source, source + steps) for source in range(count - steps)])


def split_kernel(q_ref, *out_refs):
    width = out_refs[0].shape[-1]
    for head, out_ref in enumerate(out_refs):
        out_ref[...] = q_ref[:, head * width : (head + 1) * width]


def split_queries(queries, parts, kv_here):
    tokens_here, cols = queries.shape
    group_cols = cols // parts
    width = group_cols // kv_here
    shape = jax.ShapeDtypeStruct((parts, tokens_here, width), queries.dtype)
    return pl.pallas_call(
        split_kernel,
        grid=(parts,),
        in_specs=[pl.BlockSpec((tokens_here, group_cols), lambda p: (0, p))],
        out_specs=[pl.BlockSpec((None, tokens_here, width), lambda p: (p, 0, 0))] * kv_here,
        out_shape=[shape] * kv_here,
    )(queries)


def pair_kernel(k_ref, v_ref, o_ref):
    width = k_ref.shape[-1]
    o_ref[:, :width] = k_ref[...]
    o_ref[:, width:] = v_ref[...]


def split_keys_values(keys, values, parts):
    tokens_here, cols = keys.shape
    group_cols = cols // parts
    return pl.pallas_call(
        pair_kernel,
        grid=(parts,),
        in_specs=[pl.BlockSpec((tokens_here, group_cols), lambda p: (0, p))] * 2,
        out_specs=pl.BlockSpec((None, tokens_here, 2 * group_cols), lambda p: (p, 0, 0)),
        out_shape=jax.ShapeDtypeStruct((parts, tokens_here, 2 * group_cols), keys.dtype),
    )(keys, values)


def delta_kernel(k_ref, v_ref, o_ref):
    @pl.when(pl.program_id(1) == 0)
    def _init():
        o_ref[...] = jnp.zeros(o_ref.shape, jnp.float32)

    key_feature = feature(k_ref[...].astype(jnp.float32))
    value_data = v_ref[...].astype(jnp.float32)
    o_ref[:HD, :] += jnp.dot(
        key_feature.T, value_data, precision=lax.Precision.HIGHEST,
        preferred_element_type=jnp.float32,
    )
    o_ref[HD : HD + 1, :] += jnp.sum(key_feature, axis=0, keepdims=True)


def segment_deltas(kv_local, kv_here):
    parts, tokens_here, _ = kv_local.shape
    return pl.pallas_call(
        delta_kernel,
        grid=(kv_here, parts),
        in_specs=[
            pl.BlockSpec((None, tokens_here, HD), lambda g, t: (t, 0, g)),
            pl.BlockSpec((None, tokens_here, HD), lambda g, t: (t, 0, kv_here + g)),
        ],
        out_specs=pl.BlockSpec((None, STATE_ROWS, HD), lambda g, t: (g, 0, 0)),
        out_shape=jax.ShapeDtypeStruct((kv_here, STATE_ROWS, HD), jnp.float32),
        compiler_params=pltpu.CompilerParams(dimension_semantics=("arbitrary", "arbitrary")),
    )(kv_local, kv_local)


def earlier_sum(delta):
    count = lax.axis_size("seq")
    total = delta
    steps = 1
    while steps < count:
        total = total + shifted(total, "seq", steps)
        steps *= 2
    return total - delta


def flash_kernel(
    qi_ref, kj_ref, gate_ref, q_ref, k_ref, v_ref, s_ref, o_ref, m_sc, l_sc, acc_sc, *, group_size
):
    step_at = pl.program_id(0)
    q_block = qi_ref[step_at]
    k_block = kj_ref[step_at]
    block = q_ref.shape[0]
    score_scale = HD ** (-0.5)

    @pl.when(k_block == 0)
    def _init():
        m_sc[...] = jnp.full(m_sc.shape, -jnp.inf, jnp.float32)
        l_sc[...] = jnp.zeros(l_sc.shape, jnp.float32)
        acc_sc[...] = jnp.zeros(acc_sc.shape, jnp.float32)

    def step(masked):
        key_rows = k_ref[...]
        value_rows = v_ref[...]
        if masked:
            rows = lax.broadcasted_iota(jnp.int32, (block, block), 0)
            cols = lax.broadcasted_iota(jnp.int32, (block, block), 1)
            allowed = cols <= rows
        for head in range(group_size):
            lanes = slice(head * HD, (head + 1) * HD)
            scores = (
                lax.dot_general(
                    q_ref[:, lanes], key_rows, (((1,), (1,)), ((), ())),
                    preferred_element_type=jnp.float32,
                )
                * score_scale
            )
            if masked:
                scores = jnp.where(allowed, scores, -1e30)
            m_prev = m_sc[head]
            m_new = jnp.maximum(m_prev, jnp.max(scores, axis=-1, keepdims=True))
            probs = jnp.exp(scores - m_new[:, :1])
            alpha = jnp.exp(m_prev - m_new)
            l_sc[head] = alpha * l_sc[head] + jnp.sum(probs, axis=-1, keepdims=True)
            acc_sc[:, lanes] = alpha * acc_sc[:, lanes] + jnp.dot(
                probs.astype(jnp.bfloat16), value_rows, preferred_element_type=jnp.float32
            )
            m_sc[head] = m_new

    @pl.when(k_block < q_block)
    def _full():
        step(False)

    @pl.when(k_block == q_block)
    def _last():
        step(True)
        memory = s_ref[:HD, :]
        normalizer = s_ref[HD : HD + 1, :]
        for head in range(group_size):
            lanes = slice(head * HD, (head + 1) * HD)
            local_part = acc_sc[:, lanes] / l_sc[head]
            query_feature = feature(q_ref[:, lanes].astype(jnp.float32))
            numerator = jnp.dot(
                query_feature, memory, precision=lax.Precision.HIGHEST,
                preferred_element_type=jnp.float32,
            )
            denominator = jnp.maximum(
                jnp.sum(query_feature * normalizer, axis=-1, keepdims=True), 1.0
            )
            mixing = gate_ref[head]
            o_ref[:, lanes] = (
                mixing * (numerator / denominator) + (1.0 - mixing) * local_part
            ).astype(o_ref.dtype)


def attend(query_rows, kv_local, state, mixing, head, kv_here):
    parts, block, width = query_rows.shape
    group_size = width // HD
    pairs = [(i, j) for i in range(parts) for j in range(i + 1)]
    q_index = jnp.asarray(np.array([p[0] for p in pairs], np.int32))
    k_index = jnp.asarray(np.array([p[1] for p in pairs], np.int32))
    grid_spec = pltpu.PrefetchScalarGridSpec(
        num_scalar_prefetch=2,
        grid=(len(pairs),),
        in_specs=[
            pl.BlockSpec(memory_space=pltpu.SMEM),
            pl.BlockSpec((None, block, width), lambda t, qi, kj: (qi[t], 0, 0)),
            pl.BlockSpec((None, block, HD), lambda t, qi, kj: (kj[t], 0, head)),
            pl.BlockSpec((None, block, HD), lambda t, qi, kj: (kj[t], 0, kv_here + head)),
            pl.BlockSpec((None, STATE_ROWS, HD), lambda t, qi, kj: (head, 0, 0)),
        ],
        out_specs=pl.BlockSpec((None, block, width), lambda t, qi, kj: (qi[t], 0, 0)),
        scratch_shapes=[
            pltpu.VMEM((group_size, block, LANES), jnp.float32),
            pltpu.VMEM((group_size, block, LANES), jnp.float32),
            pltpu.VMEM((block, width), jnp.float32),
        ],
    )
    return pl.pallas_call(
        functools.partial(flash_kernel, group_size=group_size),
        grid_spec=grid_spec,
        out_shape=jax.ShapeDtypeStruct(query_rows.shape, jnp.bfloat16),
        compiler_params=pltpu.CompilerParams(dimension_semantics=("arbitrary",)),
    )(q_index, k_index, mixing, query_rows, kv_local, kv_local, state)


def merge_kernel(*refs):
    in_refs, out_ref = refs[:-1], refs[-1]
    width = in_refs[0].shape[-1]
    for head, in_ref in enumerate(in_refs):
        out_ref[:, head * width : (head + 1) * width] = in_ref[...]


def merge_heads(returned):
    parts, tokens_here, width = returned[0].shape
    kv_here = len(returned)
    return pl.pallas_call(
        merge_kernel,
        grid=(parts,),
        in_specs=[pl.BlockSpec((None, tokens_here, width), lambda p: (p, 0, 0))] * kv_here,
        out_specs=pl.BlockSpec((tokens_here, kv_here * width), lambda p: (0, p)),
        out_shape=jax.ShapeDtypeStruct((tokens_here, parts * kv_here * width), returned[0].dtype),
    )(*returned)


def body(queries, keys, values, gate_logit):
    parts = lax.axis_size("head")
    head_place = lax.axis_index("head")
    kv_here = keys.shape[1] // (parts * HD)
    group_size = queries.shape[1] // keys.shape[1]

    def exchange(blocks):
        return lax.all_to_all(blocks, "head", split_axis=0, concat_axis=0, tiled=True)

    kv_local = exchange(split_keys_values(keys, values, parts))
    state = earlier_sum(segment_deltas(kv_local, kv_here))
    query_parts = split_queries(queries, parts, kv_here)
    gate_here = lax.dynamic_slice_in_dim(
        gate_logit, head_place * kv_here * group_size, kv_here * group_size
    )
    mixing = jax.nn.sigmoid(gate_here).reshape(kv_here, group_size)
    returned = []
    for head in range(kv_here):
        query_rows = exchange(query_parts[head])
        attended = attend(query_rows, kv_local, state, mixing[head], head, kv_here)
        returned.append(exchange(attended))
    return merge_heads(returned)


def solution(mesh):
    in_specs = (P(("seq", "head"), None), P(("seq", "head"), None), P(("seq", "head"), None), P())
    out_specs = P(("seq", "head"), None)
    return jax.shard_map(body, mesh=mesh, in_specs=in_specs, out_specs=out_specs, check_vma=False)
```

```python
import functools

import jax
import jax.numpy as jnp
import numpy as np
from jax import lax
from jax.experimental import pallas as pl
from jax.experimental.pallas import tpu as pltpu
from jax.sharding import PartitionSpec as P

HQ = 32
KVH = 8
HD = 128
SEG = 2048
LANES = 128
STATE_ROWS = HD + 8


def feature(inputs):
    return jnp.where(inputs > 0, inputs + 1.0, jnp.exp(jnp.minimum(inputs, 0.0)))


def shifted(value, axis, steps):
    count = lax.axis_size(axis)
    return lax.ppermute(value, axis, [(source, source + steps) for source in range(count - steps)])


def split_kernel(q_ref, k_ref, v_ref, first_ref, *out_refs):
    kv_cols = k_ref.shape[-1]
    width = out_refs[0].shape[-1] if out_refs else first_ref.shape[-1] - 2 * kv_cols
    first_ref[:, :kv_cols] = k_ref[...]
    first_ref[:, kv_cols : 2 * kv_cols] = v_ref[...]
    first_ref[:, 2 * kv_cols :] = q_ref[:, :width]
    for piece, out_ref in enumerate(out_refs):
        out_ref[...] = q_ref[:, (piece + 1) * width : (piece + 2) * width]


def split_inputs(queries, keys, values, parts, width):
    tokens_here, cols = queries.shape
    group_cols = cols // parts
    kv_cols = keys.shape[1] // parts
    pieces = group_cols // width
    first = jax.ShapeDtypeStruct((parts, tokens_here, 2 * kv_cols + width), queries.dtype)
    rest = jax.ShapeDtypeStruct((parts, tokens_here, width), queries.dtype)
    return pl.pallas_call(
        split_kernel,
        grid=(parts,),
        in_specs=[
            pl.BlockSpec((tokens_here, group_cols), lambda p: (0, p)),
            pl.BlockSpec((tokens_here, kv_cols), lambda p: (0, p)),
            pl.BlockSpec((tokens_here, kv_cols), lambda p: (0, p)),
        ],
        out_specs=[pl.BlockSpec((None, tokens_here, 2 * kv_cols + width), lambda p: (p, 0, 0))]
        + [pl.BlockSpec((None, tokens_here, width), lambda p: (p, 0, 0))] * (pieces - 1),
        out_shape=[first] + [rest] * (pieces - 1),
    )(queries, keys, values)


def delta_kernel(k_ref, v_ref, o_ref):
    @pl.when(pl.program_id(1) == 0)
    def _init():
        o_ref[...] = jnp.zeros(o_ref.shape, jnp.float32)

    key_feature = feature(k_ref[...].astype(jnp.float32))
    value_data = v_ref[...].astype(jnp.float32)
    o_ref[:HD, :] += jnp.dot(
        key_feature.T, value_data, precision=lax.Precision.HIGHEST,
        preferred_element_type=jnp.float32,
    )
    o_ref[HD : HD + 1, :] += jnp.sum(key_feature, axis=0, keepdims=True)


def local_deltas(keys, values):
    tokens_here, cols = keys.shape
    kv_heads = cols // HD
    return pl.pallas_call(
        delta_kernel,
        grid=(kv_heads, 1),
        in_specs=[pl.BlockSpec((tokens_here, HD), lambda g, t: (0, g))] * 2,
        out_specs=pl.BlockSpec((None, STATE_ROWS, HD), lambda g, t: (g, 0, 0)),
        out_shape=jax.ShapeDtypeStruct((kv_heads, STATE_ROWS, HD), jnp.float32),
        compiler_params=pltpu.CompilerParams(dimension_semantics=("arbitrary", "arbitrary")),
    )(keys, values)


def before_states(keys, values, kv_here):
    total = local_deltas(keys, values)
    parts = lax.axis_size("head")
    steps = 1
    while steps < parts:
        total = total + lax.ppermute(total, "head", [(p, p ^ steps) for p in range(parts)])
        steps *= 2
    delta = lax.dynamic_slice_in_dim(total, lax.axis_index("head") * kv_here, kv_here)
    count = lax.axis_size("seq")
    total = delta
    steps = 1
    while steps < count:
        total = total + shifted(total, "seq", steps)
        steps *= 2
    return total - delta


def flash_kernel(
    qi_ref, kj_ref, gate_ref, q_ref, k_ref, v_ref, s_ref, o_ref, m_sc, l_sc, acc_sc, *, group_size
):
    step_at = pl.program_id(0)
    q_block = qi_ref[step_at]
    k_block = kj_ref[step_at]
    block = q_ref.shape[0]
    score_scale = HD ** (-0.5)

    @pl.when(k_block == 0)
    def _init():
        m_sc[...] = jnp.full(m_sc.shape, -jnp.inf, jnp.float32)
        l_sc[...] = jnp.zeros(l_sc.shape, jnp.float32)
        acc_sc[...] = jnp.zeros(acc_sc.shape, jnp.float32)

    def step(masked):
        key_rows = k_ref[...]
        value_rows = v_ref[...]
        if masked:
            rows = lax.broadcasted_iota(jnp.int32, (block, block), 0)
            cols = lax.broadcasted_iota(jnp.int32, (block, block), 1)
            allowed = cols <= rows
        for head in range(group_size):
            lanes = slice(head * HD, (head + 1) * HD)
            scores = (
                lax.dot_general(
                    q_ref[:, lanes], key_rows, (((1,), (1,)), ((), ())),
                    preferred_element_type=jnp.float32,
                )
                * score_scale
            )
            if masked:
                scores = jnp.where(allowed, scores, -1e30)
            m_prev = m_sc[head]
            m_new = jnp.maximum(m_prev, jnp.max(scores, axis=-1, keepdims=True))
            probs = jnp.exp(scores - m_new[:, :1])
            alpha = jnp.exp(m_prev - m_new)
            l_sc[head] = alpha * l_sc[head] + jnp.sum(probs, axis=-1, keepdims=True)
            acc_sc[:, lanes] = alpha * acc_sc[:, lanes] + jnp.dot(
                probs.astype(jnp.bfloat16), value_rows, preferred_element_type=jnp.float32
            )
            m_sc[head] = m_new

    @pl.when(k_block < q_block)
    def _full():
        step(False)

    @pl.when(k_block == q_block)
    def _last():
        step(True)
        memory = s_ref[:HD, :]
        normalizer = s_ref[HD : HD + 1, :]
        for head in range(group_size):
            lanes = slice(head * HD, (head + 1) * HD)
            local_part = acc_sc[:, lanes] / l_sc[head]
            query_feature = feature(q_ref[:, lanes].astype(jnp.float32))
            numerator = jnp.dot(
                query_feature, memory, precision=lax.Precision.HIGHEST,
                preferred_element_type=jnp.float32,
            )
            denominator = jnp.maximum(
                jnp.sum(query_feature * normalizer, axis=-1, keepdims=True), 1.0
            )
            mixing = gate_ref[head]
            o_ref[:, lanes] = (
                mixing * (numerator / denominator) + (1.0 - mixing) * local_part
            ).astype(o_ref.dtype)


def attend(query_rows, q_col, kv_local, state, mixing, head, kv_here, width):
    parts, block, _ = query_rows.shape
    group_size = width // HD
    pairs = [(i, j) for i in range(parts) for j in range(i + 1)]
    q_index = jnp.asarray(np.array([p[0] for p in pairs], np.int32))
    k_index = jnp.asarray(np.array([p[1] for p in pairs], np.int32))
    grid_spec = pltpu.PrefetchScalarGridSpec(
        num_scalar_prefetch=2,
        grid=(len(pairs),),
        in_specs=[
            pl.BlockSpec(memory_space=pltpu.SMEM),
            pl.BlockSpec((None, block, width), lambda t, qi, kj: (qi[t], 0, q_col)),
            pl.BlockSpec((None, block, HD), lambda t, qi, kj: (kj[t], 0, head)),
            pl.BlockSpec((None, block, HD), lambda t, qi, kj: (kj[t], 0, kv_here + head)),
            pl.BlockSpec((None, STATE_ROWS, HD), lambda t, qi, kj: (head, 0, 0)),
        ],
        out_specs=pl.BlockSpec((None, block, width), lambda t, qi, kj: (qi[t], 0, 0)),
        scratch_shapes=[
            pltpu.VMEM((group_size, block, LANES), jnp.float32),
            pltpu.VMEM((group_size, block, LANES), jnp.float32),
            pltpu.VMEM((block, width), jnp.float32),
        ],
    )
    return pl.pallas_call(
        functools.partial(flash_kernel, group_size=group_size),
        grid_spec=grid_spec,
        out_shape=jax.ShapeDtypeStruct((parts, block, width), jnp.bfloat16),
        compiler_params=pltpu.CompilerParams(dimension_semantics=("arbitrary",)),
    )(q_index, k_index, mixing, query_rows, kv_local, kv_local, state)


def merge_kernel(*refs):
    in_refs, out_ref = refs[:-1], refs[-1]
    width = in_refs[0].shape[-1]
    for piece, in_ref in enumerate(in_refs):
        out_ref[:, piece * width : (piece + 1) * width] = in_ref[...]


def merge_pieces(returned):
    parts, tokens_here, width = returned[0].shape
    pieces = len(returned)
    return pl.pallas_call(
        merge_kernel,
        grid=(parts,),
        in_specs=[pl.BlockSpec((None, tokens_here, width), lambda p: (p, 0, 0))] * pieces,
        out_specs=pl.BlockSpec((tokens_here, pieces * width), lambda p: (0, p)),
        out_shape=jax.ShapeDtypeStruct((tokens_here, parts * pieces * width), returned[0].dtype),
    )(*returned)


def body(queries, keys, values, gate_logit):
    parts = lax.axis_size("head")
    head_place = lax.axis_index("head")
    kv_here = keys.shape[1] // (parts * HD)
    group_size = queries.shape[1] // keys.shape[1]
    width = 2 * HD if group_size % 2 == 0 else HD
    per_head = group_size * HD // width

    def exchange(blocks):
        return lax.all_to_all(blocks, "head", split_axis=0, concat_axis=0, tiled=True)

    state = before_states(keys, values, kv_here)
    sent = split_inputs(queries, keys, values, parts, width)
    kv_local = exchange(sent[0])
    gate_here = lax.dynamic_slice_in_dim(
        gate_logit, head_place * kv_here * group_size, kv_here * group_size
    )
    mixing = jax.nn.sigmoid(gate_here).reshape(kv_here * per_head, width // HD)
    kv_blocks = 2 * kv_here * HD // width
    returned = []
    for piece in range(kv_here * per_head):
        if piece == 0:
            query_rows, q_col = kv_local, kv_blocks
        else:
            query_rows, q_col = exchange(sent[piece]), 0
        attended = attend(
            query_rows, q_col, kv_local, state, mixing[piece], piece // per_head, kv_here, width
        )
        returned.append(exchange(attended))
    return merge_pieces(returned)


def solution(mesh):
    in_specs = (P(("seq", "head"), None), P(("seq", "head"), None), P(("seq", "head"), None), P())
    out_specs = P(("seq", "head"), None)
    return jax.shard_map(body, mesh=mesh, in_specs=in_specs, out_specs=out_specs, check_vma=False)
```

```python
import functools

import jax
import jax.numpy as jnp
import numpy as np
from jax import lax
from jax.experimental import pallas as pl
from jax.experimental.pallas import tpu as pltpu
from jax.sharding import PartitionSpec as P

HQ = 32
KVH = 8
HD = 128
SEG = 2048
LANES = 128
STATE_ROWS = HD + 8


def feature(inputs):
    return jnp.where(inputs > 0, inputs + 1.0, jnp.exp(jnp.minimum(inputs, 0.0)))


def shifted(value, axis, steps):
    count = lax.axis_size(axis)
    return lax.ppermute(value, axis, [(source, source + steps) for source in range(count - steps)])


def split_kernel(core_ref, q_keep, k_keep, v_keep, q_send, k_send, v_send, keep_ref, send_ref):
    q_cols = q_keep.shape[-1]
    k_cols = k_keep.shape[-1]
    for q_ref, k_ref, v_ref, o_ref in ((q_keep, k_keep, v_keep, keep_ref), (q_send, k_send, v_send, send_ref)):
        o_ref[:, :q_cols] = q_ref[...]
        o_ref[:, q_cols : q_cols + k_cols] = k_ref[...]
        o_ref[:, q_cols + k_cols :] = v_ref[...]


def split_inputs(queries, keys, values, core):
    tokens_here, q_all = queries.shape
    q_cols = q_all // 2
    k_cols = keys.shape[1] // 2
    keep_map = lambda i, c: (0, c[0])
    send_map = lambda i, c: (0, 1 - c[0])
    shape = jax.ShapeDtypeStruct((tokens_here, q_cols + 2 * k_cols), queries.dtype)
    grid_spec = pltpu.PrefetchScalarGridSpec(
        num_scalar_prefetch=1,
        grid=(1,),
        in_specs=[
            pl.BlockSpec((tokens_here, q_cols), keep_map),
            pl.BlockSpec((tokens_here, k_cols), keep_map),
            pl.BlockSpec((tokens_here, k_cols), keep_map),
            pl.BlockSpec((tokens_here, q_cols), send_map),
            pl.BlockSpec((tokens_here, k_cols), send_map),
            pl.BlockSpec((tokens_here, k_cols), send_map),
        ],
        out_specs=[pl.BlockSpec((tokens_here, q_cols + 2 * k_cols), lambda i, c: (0, 0))] * 2,
    )
    return pl.pallas_call(
        split_kernel, grid_spec=grid_spec, out_shape=[shape, shape]
    )(core.reshape(1), queries, keys, values, queries, keys, values)


def delta_kernel(k_ref, v_ref, o_ref):
    @pl.when(pl.program_id(1) == 0)
    def _init():
        o_ref[...] = jnp.zeros(o_ref.shape, jnp.float32)

    key_feature = feature(k_ref[...].astype(jnp.float32))
    value_data = v_ref[...].astype(jnp.float32)
    o_ref[:HD, :] += jnp.dot(
        key_feature.T, value_data, precision=lax.Precision.HIGHEST,
        preferred_element_type=jnp.float32,
    )
    o_ref[HD : HD + 1, :] += jnp.sum(key_feature, axis=0, keepdims=True)


def local_deltas(keys, values):
    tokens_here, cols = keys.shape
    kv_heads = cols // HD
    return pl.pallas_call(
        delta_kernel,
        grid=(kv_heads, 1),
        in_specs=[pl.BlockSpec((tokens_here, HD), lambda g, t: (0, g))] * 2,
        out_specs=pl.BlockSpec((None, STATE_ROWS, HD), lambda g, t: (g, 0, 0)),
        out_shape=jax.ShapeDtypeStruct((kv_heads, STATE_ROWS, HD), jnp.float32),
        compiler_params=pltpu.CompilerParams(dimension_semantics=("arbitrary", "arbitrary")),
    )(keys, values)


def before_states(keys, values, core, kv_group):
    total = local_deltas(keys, values)
    parts = lax.axis_size("head")
    keep = lax.dynamic_slice_in_dim(total, core * kv_group, kv_group)
    send = lax.dynamic_slice_in_dim(total, (1 - core) * kv_group, kv_group)
    total = keep + lax.ppermute(send, "head", [(p, p ^ 1) for p in range(parts)])
    steps = 2
    while steps < parts:
        total = total + lax.ppermute(total, "head", [(p, p ^ steps) for p in range(parts)])
        steps *= 2
    delta = total
    count = lax.axis_size("seq")
    steps = 1
    while steps < count:
        total = total + shifted(total, "seq", steps)
        steps *= 2
    return total - delta


def flash_kernel(
    qp_ref, kp_ref, op_ref, first_ref, last_ref, valid_ref, gate_ref, q_ref, k_ref, v_ref, s_ref,
    o_ref, m_sc, l_sc, acc_sc, *, group_size
):
    kv_head = pl.program_id(0)
    step_at = pl.program_id(1)
    first = first_ref[step_at] == 1
    last = last_ref[step_at] == 1
    valid = valid_ref[step_at] == 1
    block = q_ref.shape[0]
    score_scale = HD ** (-0.5)

    @pl.when(valid & first)
    def _init():
        m_sc[...] = jnp.full(m_sc.shape, -jnp.inf, jnp.float32)
        l_sc[...] = jnp.zeros(l_sc.shape, jnp.float32)
        acc_sc[...] = jnp.zeros(acc_sc.shape, jnp.float32)

    def step(masked):
        key_rows = k_ref[...]
        value_rows = v_ref[...]
        if masked:
            rows = lax.broadcasted_iota(jnp.int32, (block, block), 0)
            cols = lax.broadcasted_iota(jnp.int32, (block, block), 1)
            allowed = cols <= rows
        for head in range(group_size):
            lanes = slice(head * HD, (head + 1) * HD)
            scores = (
                lax.dot_general(
                    q_ref[:, lanes], key_rows, (((1,), (1,)), ((), ())),
                    preferred_element_type=jnp.float32,
                )
                * score_scale
            )
            if masked:
                scores = jnp.where(allowed, scores, -1e30)
            m_prev = m_sc[head]
            m_new = jnp.maximum(m_prev, jnp.max(scores, axis=-1, keepdims=True))
            probs = jnp.exp(scores - m_new[:, :1])
            alpha = jnp.exp(m_prev - m_new)
            l_sc[head] = alpha * l_sc[head] + jnp.sum(probs, axis=-1, keepdims=True)
            acc_sc[:, lanes] = alpha * acc_sc[:, lanes] + jnp.dot(
                probs.astype(jnp.bfloat16), value_rows, preferred_element_type=jnp.float32
            )
            m_sc[head] = m_new

    @pl.when(valid & jnp.logical_not(last))
    def _full():
        step(False)

    @pl.when(valid & last)
    def _last():
        step(True)
        memory = s_ref[:HD, :]
        normalizer = s_ref[HD : HD + 1, :]
        for head in range(group_size):
            lanes = slice(head * HD, (head + 1) * HD)
            local_part = acc_sc[:, lanes] / l_sc[head]
            query_feature = feature(q_ref[:, lanes].astype(jnp.float32))
            numerator = jnp.dot(
                query_feature, memory, precision=lax.Precision.HIGHEST,
                preferred_element_type=jnp.float32,
            )
            denominator = jnp.maximum(
                jnp.sum(query_feature * normalizer, axis=-1, keepdims=True), 1.0
            )
            mixing = gate_ref[kv_head * group_size + head]
            o_ref[:, lanes] = (
                mixing * (numerator / denominator) + (1.0 - mixing) * local_part
            ).astype(o_ref.dtype)


def pair_tables(chips, chip, core):
    longest = 4 * chips - 1
    tables = np.zeros((chips, 2, 6, longest), np.int32)
    for y in range(chips):
        for c in range(2):
            steps = []
            for a in range(2):
                for j in range(2 * y + a + 1):
                    k_pos = 2 * (chips - 1 - y + j // 2) + ((j % 2) ^ c)
                    steps.append((a ^ c, k_pos, a ^ c, int(j == 0), int(j == 2 * y + a), 1))
            while len(steps) < longest:
                steps.append(steps[-1][:5] + (0,))
            tables[y, c] = np.array(steps, np.int32).T
    return jnp.asarray(tables)[chip, core]


def attend(query_rows, kv_rows, state, mixing, tables, group_size):
    _, block, q_cols = query_rows.shape
    kv_group = kv_rows.shape[-1] // (2 * HD)
    width = group_size * HD
    steps = tables.shape[-1]
    grid_spec = pltpu.PrefetchScalarGridSpec(
        num_scalar_prefetch=6,
        grid=(kv_group, steps),
        in_specs=[
            pl.BlockSpec(memory_space=pltpu.SMEM),
            pl.BlockSpec((None, block, width), lambda g, t, qp, kp, op, f, l, v: (qp[t], 0, g)),
            pl.BlockSpec((None, block, HD), lambda g, t, qp, kp, op, f, l, v: (kp[t], 0, g)),
            pl.BlockSpec(
                (None, block, HD), lambda g, t, qp, kp, op, f, l, v: (kp[t], 0, kv_group + g)
            ),
            pl.BlockSpec((None, STATE_ROWS, HD), lambda g, t, qp, kp, op, f, l, v: (g, 0, 0)),
        ],
        out_specs=pl.BlockSpec((None, block, width), lambda g, t, qp, kp, op, f, l, v: (op[t], 0, g)),
        scratch_shapes=[
            pltpu.VMEM((group_size, block, LANES), jnp.float32),
            pltpu.VMEM((group_size, block, LANES), jnp.float32),
            pltpu.VMEM((block, width), jnp.float32),
        ],
    )
    return pl.pallas_call(
        functools.partial(flash_kernel, group_size=group_size),
        grid_spec=grid_spec,
        out_shape=jax.ShapeDtypeStruct((2, block, q_cols), jnp.bfloat16),
        compiler_params=pltpu.CompilerParams(dimension_semantics=("arbitrary", "arbitrary")),
    )(*[tables[i] for i in range(6)], mixing, query_rows, kv_rows, kv_rows, state)


def merge_kernel(core_ref, own_ref, back_ref, o_ref):
    @pl.when(pl.program_id(0) == core_ref[0])
    def _own():
        o_ref[...] = own_ref[...]

    @pl.when(pl.program_id(0) != core_ref[0])
    def _back():
        o_ref[...] = back_ref[...]


def merge_halves(own, back, core):
    tokens_here, q_cols = back.shape
    grid_spec = pltpu.PrefetchScalarGridSpec(
        num_scalar_prefetch=1,
        grid=(2,),
        in_specs=[
            pl.BlockSpec((None, tokens_here, q_cols), lambda h, c: (0, 0, 0)),
            pl.BlockSpec((tokens_here, q_cols), lambda h, c: (0, 0)),
        ],
        out_specs=pl.BlockSpec((tokens_here, q_cols), lambda h, c: (0, h)),
    )
    return pl.pallas_call(
        merge_kernel,
        grid_spec=grid_spec,
        out_shape=jax.ShapeDtypeStruct((tokens_here, 2 * q_cols), back.dtype),
    )(core.reshape(1), own, back)


def body(queries, keys, values, gate_logit):
    parts = lax.axis_size("head")
    chips = parts // 2
    place = lax.axis_index("head")
    chip = place // 2
    core = place % 2
    q_cols = queries.shape[1] // 2
    k_cols = keys.shape[1] // 2
    kv_group = k_cols // HD
    group_size = queries.shape[1] // keys.shape[1]
    sibling = [(p, p ^ 1) for p in range(parts)]

    state = before_states(keys, values, core, kv_group)
    keep, send = split_inputs(queries, keys, values, core)
    recv = lax.ppermute(send, "head", sibling)
    query_rows = jnp.stack([keep[:, :q_cols], recv[:, :q_cols]])
    kv_chip = jnp.stack([keep[:, q_cols:], recv[:, q_cols:]])
    kv_parts = [
        lax.ppermute(kv_chip, "head", [(p, p + 2 * s) for p in range(parts - 2 * s)])
        for s in range(chips - 1, 0, -1)
    ]
    kv_rows = jnp.concatenate(kv_parts + [kv_chip], axis=0)
    gate_here = lax.dynamic_slice_in_dim(gate_logit, core * kv_group * group_size, kv_group * group_size)
    mixing = jax.nn.sigmoid(gate_here)
    attended = attend(query_rows, kv_rows, state, mixing, pair_tables(chips, chip, core), group_size)
    back = lax.ppermute(attended[1], "head", sibling)
    return merge_halves(attended, back, core)


def solution(mesh):
    in_specs = (P(("seq", "head"), None), P(("seq", "head"), None), P(("seq", "head"), None), P())
    out_specs = P(("seq", "head"), None)
    return jax.shard_map(body, mesh=mesh, in_specs=in_specs, out_specs=out_specs, check_vma=False)
```

```python
import functools

import jax
import jax.numpy as jnp
import numpy as np
from jax import lax
from jax.experimental import pallas as pl
from jax.experimental.pallas import tpu as pltpu
from jax.sharding import PartitionSpec as P

HQ = 32
KVH = 8
HD = 128
SEG = 2048
LANES = 128
STATE_ROWS = HD + 8


def feature(inputs):
    return jnp.where(inputs > 0, inputs + 1.0, jnp.exp(jnp.minimum(inputs, 0.0)))


def shifted(value, axis, steps):
    count = lax.axis_size(axis)
    return lax.ppermute(value, axis, [(source, source + steps) for source in range(count - steps)])


def split_kernel(core_ref, q_keep, k_keep, v_keep, q_send, k_send, v_send, *out_refs):
    k_cols = k_keep.shape[-1]
    keep_q, keep_kv, send_q, send_kv = out_refs
    keep_q[...] = q_keep[...]
    keep_kv[:, :k_cols] = k_keep[...]
    keep_kv[:, k_cols:] = v_keep[...]
    send_q[...] = q_send[...]
    send_kv[:, :k_cols] = k_send[...]
    send_kv[:, k_cols:] = v_send[...]


def split_inputs(queries, keys, values, core):
    tokens_here, q_all = queries.shape
    q_cols = q_all // 2
    k_cols = keys.shape[1] // 2
    keep_map = lambda i, c: (0, c[0])
    send_map = lambda i, c: (0, 1 - c[0])
    q_shape = jax.ShapeDtypeStruct((tokens_here, q_cols), queries.dtype)
    kv_shape = jax.ShapeDtypeStruct((tokens_here, 2 * k_cols), keys.dtype)
    grid_spec = pltpu.PrefetchScalarGridSpec(
        num_scalar_prefetch=1,
        grid=(1,),
        in_specs=[
            pl.BlockSpec((tokens_here, q_cols), keep_map),
            pl.BlockSpec((tokens_here, k_cols), keep_map),
            pl.BlockSpec((tokens_here, k_cols), keep_map),
            pl.BlockSpec((tokens_here, q_cols), send_map),
            pl.BlockSpec((tokens_here, k_cols), send_map),
            pl.BlockSpec((tokens_here, k_cols), send_map),
        ],
        out_specs=[
            pl.BlockSpec((tokens_here, q_cols), lambda i, c: (0, 0)),
            pl.BlockSpec((tokens_here, 2 * k_cols), lambda i, c: (0, 0)),
        ]
        * 2,
    )
    return pl.pallas_call(
        split_kernel, grid_spec=grid_spec, out_shape=[q_shape, kv_shape] * 2
    )(core.reshape(1), queries, keys, values, queries, keys, values)


def delta_kernel(k_ref, v_ref, o_ref):
    @pl.when(pl.program_id(1) == 0)
    def _init():
        o_ref[...] = jnp.zeros(o_ref.shape, jnp.float32)

    key_feature = feature(k_ref[...].astype(jnp.float32))
    value_data = v_ref[...].astype(jnp.float32)
    o_ref[:HD, :] += jnp.dot(
        key_feature.T, value_data, precision=lax.Precision.HIGHEST,
        preferred_element_type=jnp.float32,
    )
    o_ref[HD : HD + 1, :] += jnp.sum(key_feature, axis=0, keepdims=True)


def local_deltas(keys, values):
    tokens_here, cols = keys.shape
    kv_heads = cols // HD
    return pl.pallas_call(
        delta_kernel,
        grid=(kv_heads, 1),
        in_specs=[pl.BlockSpec((tokens_here, HD), lambda g, t: (0, g))] * 2,
        out_specs=pl.BlockSpec((None, STATE_ROWS, HD), lambda g, t: (g, 0, 0)),
        out_shape=jax.ShapeDtypeStruct((kv_heads, STATE_ROWS, HD), jnp.float32),
        compiler_params=pltpu.CompilerParams(dimension_semantics=("arbitrary", "arbitrary")),
    )(keys, values)


def before_states(keys, values, core, kv_group):
    total = local_deltas(keys, values)
    parts = lax.axis_size("head")
    keep = lax.dynamic_slice_in_dim(total, core * kv_group, kv_group)
    send = lax.dynamic_slice_in_dim(total, (1 - core) * kv_group, kv_group)
    total = keep + lax.ppermute(send, "head", [(p, p ^ 1) for p in range(parts)])
    steps = 2
    while steps < parts:
        total = total + lax.ppermute(total, "head", [(p, p ^ steps) for p in range(parts)])
        steps *= 2
    delta = total
    count = lax.axis_size("seq")
    steps = 1
    while steps < count:
        total = total + shifted(total, "seq", steps)
        steps *= 2
    return total - delta


def flash_kernel(
    qp_ref, kp_ref, op_ref, first_ref, last_ref, valid_ref, gate_ref, q_ref, k_ref, v_ref, s_ref,
    o_ref, m_sc, l_sc, acc_sc, *, group_size
):
    kv_head = pl.program_id(0)
    step_at = pl.program_id(1)
    first = first_ref[step_at] == 1
    last = last_ref[step_at] == 1
    valid = valid_ref[step_at] == 1
    block = q_ref.shape[0]
    score_scale = HD ** (-0.5)

    @pl.when(valid & first)
    def _init():
        m_sc[...] = jnp.full(m_sc.shape, -jnp.inf, jnp.float32)
        l_sc[...] = jnp.zeros(l_sc.shape, jnp.float32)
        acc_sc[...] = jnp.zeros(acc_sc.shape, jnp.float32)

    def step(masked):
        key_rows = k_ref[...]
        value_rows = v_ref[...]
        if masked:
            rows = lax.broadcasted_iota(jnp.int32, (block, block), 0)
            cols = lax.broadcasted_iota(jnp.int32, (block, block), 1)
            allowed = cols <= rows
        for head in range(group_size):
            lanes = slice(head * HD, (head + 1) * HD)
            scores = (
                lax.dot_general(
                    q_ref[:, lanes], key_rows, (((1,), (1,)), ((), ())),
                    preferred_element_type=jnp.float32,
                )
                * score_scale
            )
            if masked:
                scores = jnp.where(allowed, scores, -1e30)
            m_prev = m_sc[head]
            m_new = jnp.maximum(m_prev, jnp.max(scores, axis=-1, keepdims=True))
            probs = jnp.exp(scores - m_new[:, :1])
            alpha = jnp.exp(m_prev - m_new)
            l_sc[head] = alpha * l_sc[head] + jnp.sum(probs, axis=-1, keepdims=True)
            acc_sc[:, lanes] = alpha * acc_sc[:, lanes] + jnp.dot(
                probs.astype(jnp.bfloat16), value_rows, preferred_element_type=jnp.float32
            )
            m_sc[head] = m_new

    @pl.when(valid & jnp.logical_not(last))
    def _full():
        step(False)

    @pl.when(valid & last)
    def _last():
        step(True)
        memory = s_ref[:HD, :]
        normalizer = s_ref[HD : HD + 1, :]
        for head in range(group_size):
            lanes = slice(head * HD, (head + 1) * HD)
            local_part = acc_sc[:, lanes] / l_sc[head]
            query_feature = feature(q_ref[:, lanes].astype(jnp.float32))
            numerator = jnp.dot(
                query_feature, memory, precision=lax.Precision.HIGHEST,
                preferred_element_type=jnp.float32,
            )
            denominator = jnp.maximum(
                jnp.sum(query_feature * normalizer, axis=-1, keepdims=True), 1.0
            )
            mixing = gate_ref[kv_head * group_size + head]
            o_ref[:, lanes] = (
                mixing * (numerator / denominator) + (1.0 - mixing) * local_part
            ).astype(o_ref.dtype)


def pair_tables(chips, chip, core):
    longest = 4 * chips - 1
    tables = np.zeros((chips, 2, 6, longest), np.int32)
    for y in range(chips):
        for c in range(2):
            steps = []
            for a in range(2):
                for j in range(2 * y + a + 1):
                    k_pos = 2 * (chips - 1 - y + j // 2) + ((j % 2) ^ c)
                    steps.append((a ^ c, k_pos, a ^ c, int(j == 0), int(j == 2 * y + a), 1))
            while len(steps) < longest:
                steps.append(steps[-1][:5] + (0,))
            tables[y, c] = np.array(steps, np.int32).T
    return jnp.asarray(tables)[chip, core]


def attend(query_rows, kv_rows, state, mixing, tables, group_size):
    _, block, q_cols = query_rows.shape
    kv_group = kv_rows.shape[-1] // (2 * HD)
    width = group_size * HD
    steps = tables.shape[-1]
    grid_spec = pltpu.PrefetchScalarGridSpec(
        num_scalar_prefetch=6,
        grid=(kv_group, steps),
        in_specs=[
            pl.BlockSpec(memory_space=pltpu.SMEM),
            pl.BlockSpec((None, block, width), lambda g, t, qp, kp, op, f, l, v: (qp[t], 0, g)),
            pl.BlockSpec((None, block, HD), lambda g, t, qp, kp, op, f, l, v: (kp[t], 0, g)),
            pl.BlockSpec(
                (None, block, HD), lambda g, t, qp, kp, op, f, l, v: (kp[t], 0, kv_group + g)
            ),
            pl.BlockSpec((None, STATE_ROWS, HD), lambda g, t, qp, kp, op, f, l, v: (g, 0, 0)),
        ],
        out_specs=pl.BlockSpec((None, block, width), lambda g, t, qp, kp, op, f, l, v: (op[t], 0, g)),
        scratch_shapes=[
            pltpu.VMEM((group_size, block, LANES), jnp.float32),
            pltpu.VMEM((group_size, block, LANES), jnp.float32),
            pltpu.VMEM((block, width), jnp.float32),
        ],
    )
    return pl.pallas_call(
        functools.partial(flash_kernel, group_size=group_size),
        grid_spec=grid_spec,
        out_shape=jax.ShapeDtypeStruct((2, block, q_cols), jnp.bfloat16),
        compiler_params=pltpu.CompilerParams(dimension_semantics=("arbitrary", "arbitrary")),
    )(*[tables[i] for i in range(6)], mixing, query_rows, kv_rows, kv_rows, state)


def merge_kernel(core_ref, own_ref, back_ref, o_ref):
    @pl.when(pl.program_id(0) == core_ref[0])
    def _own():
        o_ref[...] = own_ref[...]

    @pl.when(pl.program_id(0) != core_ref[0])
    def _back():
        o_ref[...] = back_ref[...]


def merge_halves(own, back, core):
    tokens_here, q_cols = back.shape
    grid_spec = pltpu.PrefetchScalarGridSpec(
        num_scalar_prefetch=1,
        grid=(2,),
        in_specs=[
            pl.BlockSpec((None, tokens_here, q_cols), lambda h, c: (0, 0, 0)),
            pl.BlockSpec((tokens_here, q_cols), lambda h, c: (0, 0)),
        ],
        out_specs=pl.BlockSpec((tokens_here, q_cols), lambda h, c: (0, h)),
    )
    return pl.pallas_call(
        merge_kernel,
        grid_spec=grid_spec,
        out_shape=jax.ShapeDtypeStruct((tokens_here, 2 * q_cols), back.dtype),
    )(core.reshape(1), own, back)


def body(queries, keys, values, gate_logit):
    parts = lax.axis_size("head")
    chips = parts // 2
    place = lax.axis_index("head")
    chip = place // 2
    core = place % 2
    k_cols = keys.shape[1] // 2
    kv_group = k_cols // HD
    group_size = queries.shape[1] // keys.shape[1]
    sibling = [(p, p ^ 1) for p in range(parts)]

    state = before_states(keys, values, core, kv_group)
    keep_q, keep_kv, send_q, send_kv = split_inputs(queries, keys, values, core)
    kv_parts = []
    for s in range(chips - 1, 0, -1):
        kv_parts.append(lax.ppermute(keep_kv, "head", [(p, p + 2 * s) for p in range(parts - 2 * s)]))
        kv_parts.append(
            lax.ppermute(send_kv, "head", [(p, (p + 2 * s) ^ 1) for p in range(parts - 2 * s)])
        )
    recv_q = lax.ppermute(send_q, "head", sibling)
    recv_kv = lax.ppermute(send_kv, "head", sibling)
    query_rows = jnp.stack([keep_q, recv_q])
    kv_rows = jnp.stack(kv_parts + [keep_kv, recv_kv])
    gate_here = lax.dynamic_slice_in_dim(gate_logit, core * kv_group * group_size, kv_group * group_size)
    mixing = jax.nn.sigmoid(gate_here)
    attended = attend(query_rows, kv_rows, state, mixing, pair_tables(chips, chip, core), group_size)
    back = lax.ppermute(attended[1], "head", sibling)
    return merge_halves(attended, back, core)


def solution(mesh):
    in_specs = (P(("seq", "head"), None), P(("seq", "head"), None), P(("seq", "head"), None), P())
    out_specs = P(("seq", "head"), None)
    return jax.shard_map(body, mesh=mesh, in_specs=in_specs, out_specs=out_specs, check_vma=False)
```

```python
import functools

import jax
import jax.numpy as jnp
import numpy as np
from jax import lax
from jax.experimental import pallas as pl
from jax.experimental.pallas import tpu as pltpu
from jax.sharding import PartitionSpec as P

HQ = 32
KVH = 8
HD = 128
SEG = 2048
LANES = 128
STATE_ROWS = HD + 8


def feature(inputs):
    return jnp.where(inputs > 0, inputs + 1.0, jnp.exp(jnp.minimum(inputs, 0.0)))


def shifted(value, axis, steps):
    count = lax.axis_size(axis)
    return lax.ppermute(value, axis, [(source, source + steps) for source in range(count - steps)])


def split_kernel(core_ref, q_keep, k_keep, v_keep, q_send, k_send, v_send, *out_refs):
    k_cols = k_keep.shape[-1]
    keep_q, keep_kv, send_q, send_kv = out_refs
    keep_q[...] = q_keep[...]
    keep_kv[:, :k_cols] = k_keep[...]
    keep_kv[:, k_cols:] = v_keep[...]
    send_q[...] = q_send[...]
    send_kv[:, :k_cols] = k_send[...]
    send_kv[:, k_cols:] = v_send[...]


def split_inputs(queries, keys, values, core):
    tokens_here, q_all = queries.shape
    q_cols = q_all // 2
    k_cols = keys.shape[1] // 2
    keep_map = lambda i, c: (0, c[0])
    send_map = lambda i, c: (0, 1 - c[0])
    q_shape = jax.ShapeDtypeStruct((tokens_here, q_cols), queries.dtype)
    kv_shape = jax.ShapeDtypeStruct((tokens_here, 2 * k_cols), keys.dtype)
    grid_spec = pltpu.PrefetchScalarGridSpec(
        num_scalar_prefetch=1,
        grid=(1,),
        in_specs=[
            pl.BlockSpec((tokens_here, q_cols), keep_map),
            pl.BlockSpec((tokens_here, k_cols), keep_map),
            pl.BlockSpec((tokens_here, k_cols), keep_map),
            pl.BlockSpec((tokens_here, q_cols), send_map),
            pl.BlockSpec((tokens_here, k_cols), send_map),
            pl.BlockSpec((tokens_here, k_cols), send_map),
        ],
        out_specs=[
            pl.BlockSpec((tokens_here, q_cols), lambda i, c: (0, 0)),
            pl.BlockSpec((tokens_here, 2 * k_cols), lambda i, c: (0, 0)),
        ]
        * 2,
    )
    return pl.pallas_call(
        split_kernel, grid_spec=grid_spec, out_shape=[q_shape, kv_shape] * 2
    )(core.reshape(1), queries, keys, values, queries, keys, values)


def delta_kernel(k_ref, v_ref, o_ref):
    @pl.when(pl.program_id(1) == 0)
    def _init():
        o_ref[...] = jnp.zeros(o_ref.shape, jnp.float32)

    key_feature = feature(k_ref[...].astype(jnp.float32))
    value_data = v_ref[...].astype(jnp.float32)
    o_ref[:HD, :] += jnp.dot(
        key_feature.T, value_data, precision=lax.Precision.HIGHEST,
        preferred_element_type=jnp.float32,
    )
    o_ref[HD : HD + 1, :] += jnp.sum(key_feature, axis=0, keepdims=True)


def local_deltas(keys, values):
    tokens_here, cols = keys.shape
    kv_heads = cols // HD
    return pl.pallas_call(
        delta_kernel,
        grid=(kv_heads, 1),
        in_specs=[pl.BlockSpec((tokens_here, HD), lambda g, t: (0, g))] * 2,
        out_specs=pl.BlockSpec((None, STATE_ROWS, HD), lambda g, t: (g, 0, 0)),
        out_shape=jax.ShapeDtypeStruct((kv_heads, STATE_ROWS, HD), jnp.float32),
        compiler_params=pltpu.CompilerParams(dimension_semantics=("arbitrary", "arbitrary")),
    )(keys, values)


def before_states(keys, values, core, kv_group):
    total = local_deltas(keys, values)
    parts = lax.axis_size("head")
    keep = lax.dynamic_slice_in_dim(total, core * kv_group, kv_group)
    send = lax.dynamic_slice_in_dim(total, (1 - core) * kv_group, kv_group)
    total = keep + lax.ppermute(send, "head", [(p, p ^ 1) for p in range(parts)])
    steps = 2
    while steps < parts:
        total = total + lax.ppermute(total, "head", [(p, p ^ steps) for p in range(parts)])
        steps *= 2
    delta = total
    count = lax.axis_size("seq")
    steps = 1
    while steps < count:
        total = total + shifted(total, "seq", steps)
        steps *= 2
    return total - delta


def flash_kernel(
    qp_ref, kp_ref, op_ref, first_ref, last_ref, valid_ref, q_ref, k_ref, v_ref,
    o_ref, m_sc, l_sc, acc_sc, *, group_size
):
    step_at = pl.program_id(1)
    first = first_ref[step_at] == 1
    last = last_ref[step_at] == 1
    valid = valid_ref[step_at] == 1
    block = q_ref.shape[0]
    score_scale = HD ** (-0.5)

    @pl.when(valid & first)
    def _init():
        m_sc[...] = jnp.full(m_sc.shape, -jnp.inf, jnp.float32)
        l_sc[...] = jnp.zeros(l_sc.shape, jnp.float32)
        acc_sc[...] = jnp.zeros(acc_sc.shape, jnp.float32)

    def step(masked):
        key_rows = k_ref[...]
        value_rows = v_ref[...]
        if masked:
            rows = lax.broadcasted_iota(jnp.int32, (block, block), 0)
            cols = lax.broadcasted_iota(jnp.int32, (block, block), 1)
            allowed = cols <= rows
        for head in range(group_size):
            lanes = slice(head * HD, (head + 1) * HD)
            scores = (
                lax.dot_general(
                    q_ref[:, lanes], key_rows, (((1,), (1,)), ((), ())),
                    preferred_element_type=jnp.float32,
                )
                * score_scale
            )
            if masked:
                scores = jnp.where(allowed, scores, -1e30)
            m_prev = m_sc[head]
            m_new = jnp.maximum(m_prev, jnp.max(scores, axis=-1, keepdims=True))
            probs = jnp.exp(scores - m_new[:, :1])
            alpha = jnp.exp(m_prev - m_new)
            l_sc[head] = alpha * l_sc[head] + jnp.sum(probs, axis=-1, keepdims=True)
            acc_sc[:, lanes] = alpha * acc_sc[:, lanes] + jnp.dot(
                probs.astype(jnp.bfloat16), value_rows, preferred_element_type=jnp.float32
            )
            m_sc[head] = m_new

    @pl.when(valid & jnp.logical_not(last))
    def _full():
        step(False)

    @pl.when(valid & last)
    def _last():
        step(True)
        for head in range(group_size):
            lanes = slice(head * HD, (head + 1) * HD)
            o_ref[:, lanes] = acc_sc[:, lanes] / l_sc[head]


def mix_kernel(gate_ref, q_ref, local_ref, s_ref, o_ref, *, group_size):
    kv_head = pl.program_id(1)
    memory = s_ref[:HD, :]
    normalizer = s_ref[HD : HD + 1, :]
    for head in range(group_size):
        lanes = slice(head * HD, (head + 1) * HD)
        query_feature = feature(q_ref[:, lanes].astype(jnp.float32))
        numerator = jnp.dot(
            query_feature, memory, precision=lax.Precision.HIGHEST,
            preferred_element_type=jnp.float32,
        )
        denominator = jnp.maximum(
            jnp.sum(query_feature * normalizer, axis=-1, keepdims=True), 1.0
        )
        mixing = gate_ref[kv_head * group_size + head]
        o_ref[:, lanes] = (
            mixing * (numerator / denominator) + (1.0 - mixing) * local_ref[:, lanes]
        ).astype(o_ref.dtype)


def mix(query_rows, local_part, state, mixing, group_size):
    positions, block, q_cols = query_rows.shape
    width = group_size * HD
    kv_group = q_cols // width
    row_map = lambda a, g: (a, 0, g)
    return pl.pallas_call(
        functools.partial(mix_kernel, group_size=group_size),
        grid=(positions, kv_group),
        in_specs=[
            pl.BlockSpec(memory_space=pltpu.SMEM),
            pl.BlockSpec((None, block, width), row_map),
            pl.BlockSpec((None, block, width), row_map),
            pl.BlockSpec((None, STATE_ROWS, HD), lambda a, g: (g, 0, 0)),
        ],
        out_specs=pl.BlockSpec((None, block, width), row_map),
        out_shape=jax.ShapeDtypeStruct(query_rows.shape, jnp.bfloat16),
    )(mixing, query_rows, local_part, state)


def pair_tables(chips, chip, core):
    longest = 4 * chips - 1
    tables = np.zeros((chips, 2, 6, longest), np.int32)
    for y in range(chips):
        for c in range(2):
            steps = []
            for a in range(2):
                for j in range(2 * y + a + 1):
                    k_pos = 2 * (chips - 1 - y + j // 2) + ((j % 2) ^ c)
                    steps.append((a ^ c, k_pos, a ^ c, int(j == 0), int(j == 2 * y + a), 1))
            while len(steps) < longest:
                steps.append(steps[-1][:5] + (0,))
            tables[y, c] = np.array(steps, np.int32).T
    return jnp.asarray(tables)[chip, core]


def attend(query_rows, kv_rows, tables, group_size):
    _, block, q_cols = query_rows.shape
    kv_group = kv_rows.shape[-1] // (2 * HD)
    width = group_size * HD
    steps = tables.shape[-1]
    grid_spec = pltpu.PrefetchScalarGridSpec(
        num_scalar_prefetch=6,
        grid=(kv_group, steps),
        in_specs=[
            pl.BlockSpec((None, block, width), lambda g, t, qp, kp, op, f, l, v: (qp[t], 0, g)),
            pl.BlockSpec((None, block, HD), lambda g, t, qp, kp, op, f, l, v: (kp[t], 0, g)),
            pl.BlockSpec(
                (None, block, HD), lambda g, t, qp, kp, op, f, l, v: (kp[t], 0, kv_group + g)
            ),
        ],
        out_specs=pl.BlockSpec((None, block, width), lambda g, t, qp, kp, op, f, l, v: (op[t], 0, g)),
        scratch_shapes=[
            pltpu.VMEM((group_size, block, LANES), jnp.float32),
            pltpu.VMEM((group_size, block, LANES), jnp.float32),
            pltpu.VMEM((block, width), jnp.float32),
        ],
    )
    return pl.pallas_call(
        functools.partial(flash_kernel, group_size=group_size),
        grid_spec=grid_spec,
        out_shape=jax.ShapeDtypeStruct((2, block, q_cols), jnp.float32),
        compiler_params=pltpu.CompilerParams(dimension_semantics=("arbitrary", "arbitrary")),
    )(*[tables[i] for i in range(6)], query_rows, kv_rows, kv_rows)


def merge_kernel(core_ref, own_ref, back_ref, o_ref):
    @pl.when(pl.program_id(0) == core_ref[0])
    def _own():
        o_ref[...] = own_ref[...]

    @pl.when(pl.program_id(0) != core_ref[0])
    def _back():
        o_ref[...] = back_ref[...]


def merge_halves(own, back, core):
    tokens_here, q_cols = back.shape
    grid_spec = pltpu.PrefetchScalarGridSpec(
        num_scalar_prefetch=1,
        grid=(2,),
        in_specs=[
            pl.BlockSpec((None, tokens_here, q_cols), lambda h, c: (0, 0, 0)),
            pl.BlockSpec((tokens_here, q_cols), lambda h, c: (0, 0)),
        ],
        out_specs=pl.BlockSpec((tokens_here, q_cols), lambda h, c: (0, h)),
    )
    return pl.pallas_call(
        merge_kernel,
        grid_spec=grid_spec,
        out_shape=jax.ShapeDtypeStruct((tokens_here, 2 * q_cols), back.dtype),
    )(core.reshape(1), own, back)


def body(queries, keys, values, gate_logit):
    parts = lax.axis_size("head")
    chips = parts // 2
    place = lax.axis_index("head")
    chip = place // 2
    core = place % 2
    k_cols = keys.shape[1] // 2
    kv_group = k_cols // HD
    group_size = queries.shape[1] // keys.shape[1]
    sibling = [(p, p ^ 1) for p in range(parts)]

    state = before_states(keys, values, core, kv_group)
    keep_q, keep_kv, send_q, send_kv = split_inputs(queries, keys, values, core)
    kv_parts = []
    for s in range(chips - 1, 0, -1):
        kv_parts.append(lax.ppermute(keep_kv, "head", [(p, p + 2 * s) for p in range(parts - 2 * s)]))
        kv_parts.append(
            lax.ppermute(send_kv, "head", [(p, (p + 2 * s) ^ 1) for p in range(parts - 2 * s)])
        )
    recv_q = lax.ppermute(send_q, "head", sibling)
    recv_kv = lax.ppermute(send_kv, "head", sibling)
    query_rows = jnp.stack([keep_q, recv_q])
    kv_rows = jnp.stack(kv_parts + [keep_kv, recv_kv])
    gate_here = lax.dynamic_slice_in_dim(gate_logit, core * kv_group * group_size, kv_group * group_size)
    mixing = jax.nn.sigmoid(gate_here)
    local_part = attend(query_rows, kv_rows, pair_tables(chips, chip, core), group_size)
    attended = mix(query_rows, local_part, state, mixing, group_size)
    back = lax.ppermute(attended[1], "head", sibling)
    return merge_halves(attended, back, core)


def solution(mesh):
    in_specs = (P(("seq", "head"), None), P(("seq", "head"), None), P(("seq", "head"), None), P())
    out_specs = P(("seq", "head"), None)
    return jax.shard_map(body, mesh=mesh, in_specs=in_specs, out_specs=out_specs, check_vma=False)
```

```python
import functools

import jax
import jax.numpy as jnp
import numpy as np
from jax import lax
from jax.experimental import pallas as pl
from jax.experimental.pallas import tpu as pltpu
from jax.sharding import PartitionSpec as P

HQ = 32
KVH = 8
HD = 128
SEG = 2048
LANES = 128
STATE_ROWS = HD + 8


def feature(inputs):
    return jnp.where(inputs > 0, inputs + 1.0, jnp.exp(jnp.minimum(inputs, 0.0)))


def shifted(value, axis, steps):
    count = lax.axis_size(axis)
    return lax.ppermute(value, axis, [(source, source + steps) for source in range(count - steps)])


def split_kernel(core_ref, q_keep, k_keep, v_keep, q_send, k_send, v_send, *out_refs):
    k_cols = k_keep.shape[-1]
    keep_q, keep_kv, send_q, send_kv = out_refs
    keep_q[...] = q_keep[...]
    keep_kv[:, :k_cols] = k_keep[...]
    keep_kv[:, k_cols:] = v_keep[...]
    send_q[...] = q_send[...]
    send_kv[:, :k_cols] = k_send[...]
    send_kv[:, k_cols:] = v_send[...]


def split_inputs(queries, keys, values, core):
    tokens_here, q_all = queries.shape
    q_cols = q_all // 2
    k_cols = keys.shape[1] // 2
    keep_map = lambda i, c: (0, c[0])
    send_map = lambda i, c: (0, 1 - c[0])
    q_shape = jax.ShapeDtypeStruct((tokens_here, q_cols), queries.dtype)
    kv_shape = jax.ShapeDtypeStruct((tokens_here, 2 * k_cols), keys.dtype)
    grid_spec = pltpu.PrefetchScalarGridSpec(
        num_scalar_prefetch=1,
        grid=(1,),
        in_specs=[
            pl.BlockSpec((tokens_here, q_cols), keep_map),
            pl.BlockSpec((tokens_here, k_cols), keep_map),
            pl.BlockSpec((tokens_here, k_cols), keep_map),
            pl.BlockSpec((tokens_here, q_cols), send_map),
            pl.BlockSpec((tokens_here, k_cols), send_map),
            pl.BlockSpec((tokens_here, k_cols), send_map),
        ],
        out_specs=[
            pl.BlockSpec((tokens_here, q_cols), lambda i, c: (0, 0)),
            pl.BlockSpec((tokens_here, 2 * k_cols), lambda i, c: (0, 0)),
        ]
        * 2,
    )
    return pl.pallas_call(
        split_kernel, grid_spec=grid_spec, out_shape=[q_shape, kv_shape] * 2
    )(core.reshape(1), queries, keys, values, queries, keys, values)


def delta_kernel(k_ref, v_ref, o_ref):
    @pl.when(pl.program_id(1) == 0)
    def _init():
        o_ref[...] = jnp.zeros(o_ref.shape, jnp.float32)

    key_feature = feature(k_ref[...].astype(jnp.float32))
    value_data = v_ref[...].astype(jnp.float32)
    o_ref[:HD, :] += jnp.dot(
        key_feature.T, value_data, precision=lax.Precision.HIGHEST,
        preferred_element_type=jnp.float32,
    )
    o_ref[HD : HD + 1, :] += jnp.sum(key_feature, axis=0, keepdims=True)


def local_deltas(keys, values):
    tokens_here, cols = keys.shape
    kv_heads = cols // HD
    return pl.pallas_call(
        delta_kernel,
        grid=(kv_heads, 1),
        in_specs=[pl.BlockSpec((tokens_here, HD), lambda g, t: (0, g))] * 2,
        out_specs=pl.BlockSpec((None, STATE_ROWS, HD), lambda g, t: (g, 0, 0)),
        out_shape=jax.ShapeDtypeStruct((kv_heads, STATE_ROWS, HD), jnp.float32),
        compiler_params=pltpu.CompilerParams(dimension_semantics=("arbitrary", "arbitrary")),
    )(keys, values)


def chip_states(keys, values, core, kv_group):
    total = local_deltas(keys, values)
    parts = lax.axis_size("head")
    keep = lax.dynamic_slice_in_dim(total, core * kv_group, kv_group)
    send = lax.dynamic_slice_in_dim(total, (1 - core) * kv_group, kv_group)
    total = keep + lax.ppermute(send, "head", [(p, p ^ 1) for p in range(parts)])
    steps = 2
    while steps < parts:
        total = total + lax.ppermute(total, "head", [(p, p ^ steps) for p in range(parts)])
        steps *= 2
    return total


def earlier_states(delta):
    count = lax.axis_size("seq")
    total = delta
    steps = 1
    while steps < count:
        total = total + shifted(total, "seq", steps)
        steps *= 2
    return total - delta


def flash_kernel(
    qp_ref, kp_ref, op_ref, first_ref, last_ref, valid_ref, gate_ref, q_ref, k_ref, v_ref, s_ref,
    o_ref, m_sc, l_sc, acc_sc, *, group_size
):
    kv_head = pl.program_id(0)
    step_at = pl.program_id(1)
    first = first_ref[step_at] == 1
    last = last_ref[step_at] == 1
    valid = valid_ref[step_at] == 1
    block = q_ref.shape[0]
    score_scale = HD ** (-0.5)

    @pl.when(valid & first)
    def _init():
        m_sc[...] = jnp.full(m_sc.shape, -jnp.inf, jnp.float32)
        l_sc[...] = jnp.zeros(l_sc.shape, jnp.float32)
        acc_sc[...] = jnp.zeros(acc_sc.shape, jnp.float32)

    def step(masked):
        key_rows = k_ref[...]
        value_rows = v_ref[...]
        if masked:
            rows = lax.broadcasted_iota(jnp.int32, (block, block), 0)
            cols = lax.broadcasted_iota(jnp.int32, (block, block), 1)
            allowed = cols <= rows
        for head in range(group_size):
            lanes = slice(head * HD, (head + 1) * HD)
            scores = (
                lax.dot_general(
                    q_ref[:, lanes], key_rows, (((1,), (1,)), ((), ())),
                    preferred_element_type=jnp.float32,
                )
                * score_scale
            )
            if masked:
                scores = jnp.where(allowed, scores, -1e30)
            m_prev = m_sc[head]
            m_new = jnp.maximum(m_prev, jnp.max(scores, axis=-1, keepdims=True))
            probs = jnp.exp(scores - m_new[:, :1])
            alpha = jnp.exp(m_prev - m_new)
            l_sc[head] = alpha * l_sc[head] + jnp.sum(probs, axis=-1, keepdims=True)
            acc_sc[:, lanes] = alpha * acc_sc[:, lanes] + jnp.dot(
                probs.astype(jnp.bfloat16), value_rows, preferred_element_type=jnp.float32
            )
            m_sc[head] = m_new

    @pl.when(valid & jnp.logical_not(last))
    def _full():
        step(False)

    @pl.when(valid & last)
    def _last():
        step(True)
        memory = s_ref[:HD, :]
        normalizer = s_ref[HD : HD + 1, :]
        for head in range(group_size):
            lanes = slice(head * HD, (head + 1) * HD)
            local_part = acc_sc[:, lanes] / l_sc[head]
            query_feature = feature(q_ref[:, lanes].astype(jnp.float32))
            numerator = jnp.dot(
                query_feature, memory, precision=lax.Precision.HIGHEST,
                preferred_element_type=jnp.float32,
            )
            denominator = jnp.maximum(
                jnp.sum(query_feature * normalizer, axis=-1, keepdims=True), 1.0
            )
            mixing = gate_ref[kv_head * group_size + head]
            o_ref[:, lanes] = (
                mixing * (numerator / denominator) + (1.0 - mixing) * local_part
            ).astype(o_ref.dtype)


def pair_tables(chips, chip, core):
    longest = 4 * chips - 1
    tables = np.zeros((chips, 2, 6, longest), np.int32)
    for y in range(chips):
        for c in range(2):
            steps = []
            for a in range(2):
                for j in range(2 * y + a + 1):
                    k_pos = 2 * (chips - 1 - y + j // 2) + ((j % 2) ^ c)
                    steps.append((a ^ c, k_pos, a ^ c, int(j == 0), int(j == 2 * y + a), 1))
            while len(steps) < longest:
                steps.append(steps[-1][:5] + (0,))
            tables[y, c] = np.array(steps, np.int32).T
    return jnp.asarray(tables)[chip, core]


def attend(query_rows, kv_rows, state, mixing, tables, group_size):
    _, block, q_cols = query_rows.shape
    kv_group = kv_rows.shape[-1] // (2 * HD)
    width = group_size * HD
    steps = tables.shape[-1]
    grid_spec = pltpu.PrefetchScalarGridSpec(
        num_scalar_prefetch=6,
        grid=(kv_group, steps),
        in_specs=[
            pl.BlockSpec(memory_space=pltpu.SMEM),
            pl.BlockSpec((None, block, width), lambda g, t, qp, kp, op, f, l, v: (qp[t], 0, g)),
            pl.BlockSpec((None, block, HD), lambda g, t, qp, kp, op, f, l, v: (kp[t], 0, g)),
            pl.BlockSpec(
                (None, block, HD), lambda g, t, qp, kp, op, f, l, v: (kp[t], 0, kv_group + g)
            ),
            pl.BlockSpec((None, STATE_ROWS, HD), lambda g, t, qp, kp, op, f, l, v: (g, 0, 0)),
        ],
        out_specs=pl.BlockSpec((None, block, width), lambda g, t, qp, kp, op, f, l, v: (op[t], 0, g)),
        scratch_shapes=[
            pltpu.VMEM((group_size, block, LANES), jnp.float32),
            pltpu.VMEM((group_size, block, LANES), jnp.float32),
            pltpu.VMEM((block, width), jnp.float32),
        ],
    )
    return pl.pallas_call(
        functools.partial(flash_kernel, group_size=group_size),
        grid_spec=grid_spec,
        out_shape=jax.ShapeDtypeStruct((2, block, q_cols), jnp.bfloat16),
        compiler_params=pltpu.CompilerParams(dimension_semantics=("arbitrary", "arbitrary")),
    )(*[tables[i] for i in range(6)], mixing, query_rows, kv_rows, kv_rows, state)


def merge_kernel(core_ref, own_ref, back_ref, o_ref):
    @pl.when(pl.program_id(0) == core_ref[0])
    def _own():
        o_ref[...] = own_ref[...]

    @pl.when(pl.program_id(0) != core_ref[0])
    def _back():
        o_ref[...] = back_ref[...]


def merge_halves(own, back, core):
    tokens_here, q_cols = back.shape
    grid_spec = pltpu.PrefetchScalarGridSpec(
        num_scalar_prefetch=1,
        grid=(2,),
        in_specs=[
            pl.BlockSpec((None, tokens_here, q_cols), lambda h, c: (0, 0, 0)),
            pl.BlockSpec((tokens_here, q_cols), lambda h, c: (0, 0)),
        ],
        out_specs=pl.BlockSpec((tokens_here, q_cols), lambda h, c: (0, h)),
    )
    return pl.pallas_call(
        merge_kernel,
        grid_spec=grid_spec,
        out_shape=jax.ShapeDtypeStruct((tokens_here, 2 * q_cols), back.dtype),
    )(core.reshape(1), own, back)


def body(queries, keys, values, gate_logit):
    parts = lax.axis_size("head")
    chips = parts // 2
    place = lax.axis_index("head")
    chip = place // 2
    core = place % 2
    k_cols = keys.shape[1] // 2
    kv_group = k_cols // HD
    group_size = queries.shape[1] // keys.shape[1]
    sibling = [(p, p ^ 1) for p in range(parts)]

    delta = chip_states(keys, values, core, kv_group)
    keep_q, keep_kv, send_q, send_kv = split_inputs(queries, keys, values, core)
    delta, keep_kv, send_kv = lax.optimization_barrier((delta, keep_kv, send_kv))
    state = earlier_states(delta)
    kv_parts = []
    for s in range(chips - 1, 0, -1):
        kv_parts.append(lax.ppermute(keep_kv, "head", [(p, p + 2 * s) for p in range(parts - 2 * s)]))
        kv_parts.append(
            lax.ppermute(send_kv, "head", [(p, (p + 2 * s) ^ 1) for p in range(parts - 2 * s)])
        )
    recv_q = lax.ppermute(send_q, "head", sibling)
    recv_kv = lax.ppermute(send_kv, "head", sibling)
    query_rows = jnp.stack([keep_q, recv_q])
    kv_rows = jnp.stack(kv_parts + [keep_kv, recv_kv])
    gate_here = lax.dynamic_slice_in_dim(gate_logit, core * kv_group * group_size, kv_group * group_size)
    mixing = jax.nn.sigmoid(gate_here)
    attended = attend(query_rows, kv_rows, state, mixing, pair_tables(chips, chip, core), group_size)
    back = lax.ppermute(attended[1], "head", sibling)
    return merge_halves(attended, back, core)


def solution(mesh):
    in_specs = (P(("seq", "head"), None), P(("seq", "head"), None), P(("seq", "head"), None), P())
    out_specs = P(("seq", "head"), None)
    return jax.shard_map(body, mesh=mesh, in_specs=in_specs, out_specs=out_specs, check_vma=False)
```

```python
import functools

import jax
import jax.numpy as jnp
import numpy as np
from jax import lax
from jax.experimental import pallas as pl
from jax.experimental.pallas import tpu as pltpu
from jax.sharding import PartitionSpec as P

HQ = 32
KVH = 8
HD = 128
SEG = 2048
LANES = 128
STATE_ROWS = HD + 8


def feature(inputs):
    return jnp.where(inputs > 0, inputs + 1.0, jnp.exp(jnp.minimum(inputs, 0.0)))


def shifted(value, axis, steps):
    count = lax.axis_size(axis)
    return lax.ppermute(value, axis, [(source, source + steps) for source in range(count - steps)])


def split_kernel(core_ref, q_keep, k_keep, v_keep, q_send, k_send, v_send, *out_refs):
    k_cols = k_keep.shape[-1]
    keep_q, keep_kv, send_q, send_kv = out_refs
    keep_q[...] = q_keep[...]
    keep_kv[:, :k_cols] = k_keep[...]
    keep_kv[:, k_cols:] = v_keep[...]
    send_q[...] = q_send[...]
    send_kv[:, :k_cols] = k_send[...]
    send_kv[:, k_cols:] = v_send[...]


def split_inputs(queries, keys, values, core):
    tokens_here, q_all = queries.shape
    q_cols = q_all // 2
    k_cols = keys.shape[1] // 2
    keep_map = lambda i, c: (0, c[0])
    send_map = lambda i, c: (0, 1 - c[0])
    q_shape = jax.ShapeDtypeStruct((tokens_here, q_cols), queries.dtype)
    kv_shape = jax.ShapeDtypeStruct((tokens_here, 2 * k_cols), keys.dtype)
    grid_spec = pltpu.PrefetchScalarGridSpec(
        num_scalar_prefetch=1,
        grid=(1,),
        in_specs=[
            pl.BlockSpec((tokens_here, q_cols), keep_map),
            pl.BlockSpec((tokens_here, k_cols), keep_map),
            pl.BlockSpec((tokens_here, k_cols), keep_map),
            pl.BlockSpec((tokens_here, q_cols), send_map),
            pl.BlockSpec((tokens_here, k_cols), send_map),
            pl.BlockSpec((tokens_here, k_cols), send_map),
        ],
        out_specs=[
            pl.BlockSpec((tokens_here, q_cols), lambda i, c: (0, 0)),
            pl.BlockSpec((tokens_here, 2 * k_cols), lambda i, c: (0, 0)),
        ]
        * 2,
    )
    return pl.pallas_call(
        split_kernel, grid_spec=grid_spec, out_shape=[q_shape, kv_shape] * 2
    )(core.reshape(1), queries, keys, values, queries, keys, values)


def delta_kernel(k_ref, v_ref, o_ref):
    @pl.when(pl.program_id(1) == 0)
    def _init():
        o_ref[...] = jnp.zeros(o_ref.shape, jnp.float32)

    key_feature = feature(k_ref[...].astype(jnp.float32))
    value_data = v_ref[...].astype(jnp.float32)
    o_ref[:HD, :] += jnp.dot(
        key_feature.T, value_data, precision=lax.Precision.HIGHEST,
        preferred_element_type=jnp.float32,
    )
    o_ref[HD : HD + 1, :] += jnp.sum(key_feature, axis=0, keepdims=True)


def local_deltas(keys, values):
    tokens_here, cols = keys.shape
    kv_heads = cols // HD
    return pl.pallas_call(
        delta_kernel,
        grid=(kv_heads, 1),
        in_specs=[pl.BlockSpec((tokens_here, HD), lambda g, t: (0, g))] * 2,
        out_specs=pl.BlockSpec((None, STATE_ROWS, HD), lambda g, t: (g, 0, 0)),
        out_shape=jax.ShapeDtypeStruct((kv_heads, STATE_ROWS, HD), jnp.float32),
        compiler_params=pltpu.CompilerParams(dimension_semantics=("arbitrary", "arbitrary")),
    )(keys, values)


def chip_states(keys, values, core, kv_group):
    total = local_deltas(keys, values)
    parts = lax.axis_size("head")
    keep = lax.dynamic_slice_in_dim(total, core * kv_group, kv_group)
    send = lax.dynamic_slice_in_dim(total, (1 - core) * kv_group, kv_group)
    total = keep + lax.ppermute(send, "head", [(p, p ^ 1) for p in range(parts)])
    steps = 2
    while steps < parts:
        total = total + lax.ppermute(total, "head", [(p, p ^ steps) for p in range(parts)])
        steps *= 2
    return total


def earlier_states(delta):
    count = lax.axis_size("seq")
    total = delta
    steps = 1
    while steps < count:
        total = total + shifted(total, "seq", steps)
        steps *= 2
    return total - delta


def online_step(q_ref, k_ref, v_ref, m_sc, l_sc, acc_sc, group_size, masked):
    block = q_ref.shape[0]
    score_scale = HD ** (-0.5)
    key_rows = k_ref[...]
    value_rows = v_ref[...]
    if masked:
        rows = lax.broadcasted_iota(jnp.int32, (block, block), 0)
        cols = lax.broadcasted_iota(jnp.int32, (block, block), 1)
        allowed = cols <= rows
    for head in range(group_size):
        lanes = slice(head * HD, (head + 1) * HD)
        scores = (
            lax.dot_general(
                q_ref[:, lanes], key_rows, (((1,), (1,)), ((), ())),
                preferred_element_type=jnp.float32,
            )
            * score_scale
        )
        if masked:
            scores = jnp.where(allowed, scores, -1e30)
        m_prev = m_sc[head]
        m_new = jnp.maximum(m_prev, jnp.max(scores, axis=-1, keepdims=True))
        probs = jnp.exp(scores - m_new[:, :1])
        alpha = jnp.exp(m_prev - m_new)
        l_sc[head] = alpha * l_sc[head] + jnp.sum(probs, axis=-1, keepdims=True)
        acc_sc[:, lanes] = alpha * acc_sc[:, lanes] + jnp.dot(
            probs.astype(jnp.bfloat16), value_rows, preferred_element_type=jnp.float32
        )
        m_sc[head] = m_new


def near_kernel(qp_ref, kp_ref, first_ref, diag_ref, q_ref, k_ref, v_ref, acc_ref, ml_ref,
                m_sc, l_sc, acc_sc, *, group_size):
    step_at = pl.program_id(1)

    @pl.when(first_ref[step_at] == 1)
    def _init():
        m_sc[...] = jnp.full(m_sc.shape, -jnp.inf, jnp.float32)
        l_sc[...] = jnp.zeros(l_sc.shape, jnp.float32)
        acc_sc[...] = jnp.zeros(acc_sc.shape, jnp.float32)

    @pl.when(diag_ref[step_at] == 0)
    def _full():
        online_step(q_ref, k_ref, v_ref, m_sc, l_sc, acc_sc, group_size, False)

    @pl.when(diag_ref[step_at] == 1)
    def _diag():
        online_step(q_ref, k_ref, v_ref, m_sc, l_sc, acc_sc, group_size, True)
        acc_ref[...] = acc_sc[...]
        lane = lax.broadcasted_iota(jnp.int32, ml_ref.shape, 1)
        packed = jnp.zeros(ml_ref.shape, jnp.float32)
        for head in range(group_size):
            packed = jnp.where(lane == head, m_sc[head], packed)
            packed = jnp.where(lane == group_size + head, l_sc[head], packed)
        ml_ref[...] = packed


def far_kernel(qp_ref, kp_ref, first_ref, last_ref, valid_ref, gate_ref, q_ref, k_ref, v_ref,
               s_ref, acc_in, ml_in, o_ref, m_sc, l_sc, acc_sc, *, group_size):
    kv_head = pl.program_id(0)
    step_at = pl.program_id(1)

    @pl.when(first_ref[step_at] == 1)
    def _init():
        packed = ml_in[...]
        for head in range(group_size):
            m_sc[head] = jnp.broadcast_to(packed[:, head : head + 1], m_sc.shape[1:])
            l_sc[head] = jnp.broadcast_to(
                packed[:, group_size + head : group_size + head + 1], l_sc.shape[1:]
            )
        acc_sc[...] = acc_in[...]

    @pl.when(valid_ref[step_at] == 1)
    def _step():
        online_step(q_ref, k_ref, v_ref, m_sc, l_sc, acc_sc, group_size, False)

    @pl.when(last_ref[step_at] == 1)
    def _last():
        memory = s_ref[:HD, :]
        normalizer = s_ref[HD : HD + 1, :]
        for head in range(group_size):
            lanes = slice(head * HD, (head + 1) * HD)
            local_part = acc_sc[:, lanes] / l_sc[head]
            query_feature = feature(q_ref[:, lanes].astype(jnp.float32))
            numerator = jnp.dot(
                query_feature, memory, precision=lax.Precision.HIGHEST,
                preferred_element_type=jnp.float32,
            )
            denominator = jnp.maximum(
                jnp.sum(query_feature * normalizer, axis=-1, keepdims=True), 1.0
            )
            mixing = gate_ref[kv_head * group_size + head]
            o_ref[:, lanes] = (
                mixing * (numerator / denominator) + (1.0 - mixing) * local_part
            ).astype(o_ref.dtype)


def near_tables(core):
    tables = np.array(
        [[[c, 1 ^ c, 1 ^ c], [c, c, 1 ^ c], [1, 1, 0], [1, 0, 1]] for c in range(2)], np.int32
    )
    return jnp.asarray(tables)[core]


def far_tables(chips, chip, core):
    per_block = max(1, 2 * (chips - 1))
    tables = np.zeros((chips, 2, 5, 2 * per_block), np.int32)
    for y in range(chips):
        for c in range(2):
            steps = []
            for a in range(2):
                k_pos = 0
                for j in range(per_block):
                    valid = int(j < 2 * y)
                    if valid:
                        k_pos = 2 * (chips - 1 - y + j // 2) + ((j % 2) ^ c)
                    steps.append((a ^ c, k_pos, int(j == 0), int(j == per_block - 1), valid))
            tables[y, c] = np.array(steps, np.int32).T
    return jnp.asarray(tables)[chip, core]


def attend(query_rows, near_kv, far_kv, state, mixing, chips, chip, core, group_size):
    _, block, q_cols = query_rows.shape
    kv_group = near_kv.shape[-1] // (2 * HD)
    width = group_size * HD
    scratch = [
        pltpu.VMEM((group_size, block, LANES), jnp.float32),
        pltpu.VMEM((group_size, block, LANES), jnp.float32),
        pltpu.VMEM((block, width), jnp.float32),
    ]
    params = pltpu.CompilerParams(dimension_semantics=("arbitrary", "arbitrary"))
    near = near_tables(core)
    near_spec = pltpu.PrefetchScalarGridSpec(
        num_scalar_prefetch=4,
        grid=(kv_group, near.shape[-1]),
        in_specs=[
            pl.BlockSpec((None, block, width), lambda g, t, qp, kp, f, d: (qp[t], 0, g)),
            pl.BlockSpec((None, block, HD), lambda g, t, qp, kp, f, d: (kp[t], 0, g)),
            pl.BlockSpec((None, block, HD), lambda g, t, qp, kp, f, d: (kp[t], 0, kv_group + g)),
        ],
        out_specs=[
            pl.BlockSpec((None, block, width), lambda g, t, qp, kp, f, d: (qp[t], 0, g)),
            pl.BlockSpec((None, None, block, LANES), lambda g, t, qp, kp, f, d: (g, qp[t], 0, 0)),
        ],
        scratch_shapes=scratch,
    )
    acc, ml = pl.pallas_call(
        functools.partial(near_kernel, group_size=group_size),
        grid_spec=near_spec,
        out_shape=[
            jax.ShapeDtypeStruct((2, block, q_cols), jnp.float32),
            jax.ShapeDtypeStruct((kv_group, 2, block, LANES), jnp.float32),
        ],
        compiler_params=params,
    )(*[near[i] for i in range(4)], query_rows, near_kv, near_kv)
    far = far_tables(chips, chip, core)
    far_spec = pltpu.PrefetchScalarGridSpec(
        num_scalar_prefetch=5,
        grid=(kv_group, far.shape[-1]),
        in_specs=[
            pl.BlockSpec(memory_space=pltpu.SMEM),
            pl.BlockSpec((None, block, width), lambda g, t, qp, kp, f, l, v: (qp[t], 0, g)),
            pl.BlockSpec((None, block, HD), lambda g, t, qp, kp, f, l, v: (kp[t], 0, g)),
            pl.BlockSpec((None, block, HD), lambda g, t, qp, kp, f, l, v: (kp[t], 0, kv_group + g)),
            pl.BlockSpec((None, STATE_ROWS, HD), lambda g, t, qp, kp, f, l, v: (g, 0, 0)),
            pl.BlockSpec((None, block, width), lambda g, t, qp, kp, f, l, v: (qp[t], 0, g)),
            pl.BlockSpec((None, None, block, LANES), lambda g, t, qp, kp, f, l, v: (g, qp[t], 0, 0)),
        ],
        out_specs=pl.BlockSpec((None, block, width), lambda g, t, qp, kp, f, l, v: (qp[t], 0, g)),
        scratch_shapes=scratch,
    )
    return pl.pallas_call(
        functools.partial(far_kernel, group_size=group_size),
        grid_spec=far_spec,
        out_shape=jax.ShapeDtypeStruct((2, block, q_cols), jnp.bfloat16),
        compiler_params=params,
    )(*[far[i] for i in range(5)], mixing, query_rows, far_kv, far_kv, state, acc, ml)


def merge_kernel(core_ref, own_ref, back_ref, o_ref):
    @pl.when(pl.program_id(0) == core_ref[0])
    def _own():
        o_ref[...] = own_ref[...]

    @pl.when(pl.program_id(0) != core_ref[0])
    def _back():
        o_ref[...] = back_ref[...]


def merge_halves(own, back, core):
    tokens_here, q_cols = back.shape
    grid_spec = pltpu.PrefetchScalarGridSpec(
        num_scalar_prefetch=1,
        grid=(2,),
        in_specs=[
            pl.BlockSpec((None, tokens_here, q_cols), lambda h, c: (0, 0, 0)),
            pl.BlockSpec((tokens_here, q_cols), lambda h, c: (0, 0)),
        ],
        out_specs=pl.BlockSpec((tokens_here, q_cols), lambda h, c: (0, h)),
    )
    return pl.pallas_call(
        merge_kernel,
        grid_spec=grid_spec,
        out_shape=jax.ShapeDtypeStruct((tokens_here, 2 * q_cols), back.dtype),
    )(core.reshape(1), own, back)


def body(queries, keys, values, gate_logit):
    parts = lax.axis_size("head")
    chips = parts // 2
    place = lax.axis_index("head")
    chip = place // 2
    core = place % 2
    k_cols = keys.shape[1] // 2
    kv_group = k_cols // HD
    group_size = queries.shape[1] // keys.shape[1]
    sibling = [(p, p ^ 1) for p in range(parts)]

    delta = chip_states(keys, values, core, kv_group)
    keep_q, keep_kv, send_q, send_kv = split_inputs(queries, keys, values, core)
    delta, keep_kv, send_kv = lax.optimization_barrier((delta, keep_kv, send_kv))
    state = earlier_states(delta)
    kv_parts = []
    for s in range(chips - 1, 0, -1):
        kv_parts.append(lax.ppermute(keep_kv, "head", [(p, p + 2 * s) for p in range(parts - 2 * s)]))
        kv_parts.append(
            lax.ppermute(send_kv, "head", [(p, (p + 2 * s) ^ 1) for p in range(parts - 2 * s)])
        )
    recv_q = lax.ppermute(send_q, "head", sibling)
    recv_kv = lax.ppermute(send_kv, "head", sibling)
    query_rows = jnp.stack([keep_q, recv_q])
    near_kv = jnp.stack([keep_kv, recv_kv])
    far_kv = jnp.stack(kv_parts) if kv_parts else near_kv
    gate_here = lax.dynamic_slice_in_dim(gate_logit, core * kv_group * group_size, kv_group * group_size)
    mixing = jax.nn.sigmoid(gate_here)
    attended = attend(query_rows, near_kv, far_kv, state, mixing, chips, chip, core, group_size)
    back = lax.ppermute(attended[1], "head", sibling)
    return merge_halves(attended, back, core)


def solution(mesh):
    in_specs = (P(("seq", "head"), None), P(("seq", "head"), None), P(("seq", "head"), None), P())
    out_specs = P(("seq", "head"), None)
    return jax.shard_map(body, mesh=mesh, in_specs=in_specs, out_specs=out_specs, check_vma=False)
```

```python
import functools

import jax
import jax.numpy as jnp
import numpy as np
from jax import lax
from jax.experimental import pallas as pl
from jax.experimental.pallas import tpu as pltpu
from jax.sharding import PartitionSpec as P

HQ = 32
KVH = 8
HD = 128
SEG = 2048
LANES = 128
STATE_ROWS = HD + 8


def feature(inputs):
    return jnp.where(inputs > 0, inputs + 1.0, jnp.exp(jnp.minimum(inputs, 0.0)))


def shifted(value, axis, steps):
    count = lax.axis_size(axis)
    return lax.ppermute(value, axis, [(source, source + steps) for source in range(count - steps)])


def split_kernel(core_ref, q_keep, k_keep, v_keep, q_send, k_send, v_send, *out_refs):
    k_cols = k_keep.shape[-1]
    keep_q, keep_kv, send_q, send_kv = out_refs
    keep_q[...] = q_keep[...]
    keep_kv[:, :k_cols] = k_keep[...]
    keep_kv[:, k_cols:] = v_keep[...]
    send_q[...] = q_send[...]
    send_kv[:, :k_cols] = k_send[...]
    send_kv[:, k_cols:] = v_send[...]


def split_inputs(queries, keys, values, core):
    tokens_here, q_all = queries.shape
    q_cols = q_all // 2
    k_cols = keys.shape[1] // 2
    keep_map = lambda i, c: (0, c[0])
    send_map = lambda i, c: (0, 1 - c[0])
    q_shape = jax.ShapeDtypeStruct((tokens_here, q_cols), queries.dtype)
    kv_shape = jax.ShapeDtypeStruct((tokens_here, 2 * k_cols), keys.dtype)
    grid_spec = pltpu.PrefetchScalarGridSpec(
        num_scalar_prefetch=1,
        grid=(1,),
        in_specs=[
            pl.BlockSpec((tokens_here, q_cols), keep_map),
            pl.BlockSpec((tokens_here, k_cols), keep_map),
            pl.BlockSpec((tokens_here, k_cols), keep_map),
            pl.BlockSpec((tokens_here, q_cols), send_map),
            pl.BlockSpec((tokens_here, k_cols), send_map),
            pl.BlockSpec((tokens_here, k_cols), send_map),
        ],
        out_specs=[
            pl.BlockSpec((tokens_here, q_cols), lambda i, c: (0, 0)),
            pl.BlockSpec((tokens_here, 2 * k_cols), lambda i, c: (0, 0)),
        ]
        * 2,
    )
    return pl.pallas_call(
        split_kernel, grid_spec=grid_spec, out_shape=[q_shape, kv_shape] * 2
    )(core.reshape(1), queries, keys, values, queries, keys, values)


def delta_kernel(k_ref, v_ref, o_ref):
    @pl.when(pl.program_id(1) == 0)
    def _init():
        o_ref[...] = jnp.zeros(o_ref.shape, jnp.float32)

    key_feature = feature(k_ref[...].astype(jnp.float32))
    value_data = v_ref[...].astype(jnp.float32)
    o_ref[:HD, :] += jnp.dot(
        key_feature.T, value_data, precision=lax.Precision.HIGHEST,
        preferred_element_type=jnp.float32,
    )
    o_ref[HD : HD + 1, :] += jnp.sum(key_feature, axis=0, keepdims=True)


def local_deltas(keys, values):
    tokens_here, cols = keys.shape
    kv_heads = cols // HD
    return pl.pallas_call(
        delta_kernel,
        grid=(kv_heads, 1),
        in_specs=[pl.BlockSpec((tokens_here, HD), lambda g, t: (0, g))] * 2,
        out_specs=pl.BlockSpec((None, STATE_ROWS, HD), lambda g, t: (g, 0, 0)),
        out_shape=jax.ShapeDtypeStruct((kv_heads, STATE_ROWS, HD), jnp.float32),
        compiler_params=pltpu.CompilerParams(dimension_semantics=("arbitrary", "arbitrary")),
    )(keys, values)


def chip_states(keys, values, core, kv_group):
    total = local_deltas(keys, values)
    parts = lax.axis_size("head")
    keep = lax.dynamic_slice_in_dim(total, core * kv_group, kv_group)
    send = lax.dynamic_slice_in_dim(total, (1 - core) * kv_group, kv_group)
    total = keep + lax.ppermute(send, "head", [(p, p ^ 1) for p in range(parts)])
    steps = 2
    while steps < parts:
        total = total + lax.ppermute(total, "head", [(p, p ^ steps) for p in range(parts)])
        steps *= 2
    return total


def earlier_states(delta):
    count = lax.axis_size("seq")
    total = delta
    steps = 1
    while steps < count:
        total = total + shifted(total, "seq", steps)
        steps *= 2
    return total - delta


def online_step(q_ref, k_ref, v_ref, m_sc, l_sc, acc_sc, group_size, masked):
    block = q_ref.shape[0]
    score_scale = HD ** (-0.5)
    key_rows = k_ref[...]
    value_rows = v_ref[...]
    if masked:
        rows = lax.broadcasted_iota(jnp.int32, (block, block), 0)
        cols = lax.broadcasted_iota(jnp.int32, (block, block), 1)
        allowed = cols <= rows
    for head in range(group_size):
        lanes = slice(head * HD, (head + 1) * HD)
        scores = (
            lax.dot_general(
                q_ref[:, lanes], key_rows, (((1,), (1,)), ((), ())),
                preferred_element_type=jnp.float32,
            )
            * score_scale
        )
        if masked:
            scores = jnp.where(allowed, scores, -1e30)
        m_prev = m_sc[head]
        m_new = jnp.maximum(m_prev, jnp.max(scores, axis=-1, keepdims=True))
        probs = jnp.exp(scores - m_new[:, :1])
        alpha = jnp.exp(m_prev - m_new)
        l_sc[head] = alpha * l_sc[head] + jnp.sum(probs, axis=-1, keepdims=True)
        acc_sc[:, lanes] = alpha * acc_sc[:, lanes] + jnp.dot(
            probs.astype(jnp.bfloat16), value_rows, preferred_element_type=jnp.float32
        )
        m_sc[head] = m_new


def near_kernel(qp_ref, kp_ref, first_ref, diag_ref, q_ref, k_ref, v_ref, acc_ref, ml_ref,
                m_sc, l_sc, acc_sc, *, group_size):
    step_at = pl.program_id(1)

    @pl.when(first_ref[step_at] == 1)
    def _init():
        m_sc[...] = jnp.full(m_sc.shape, -jnp.inf, jnp.float32)
        l_sc[...] = jnp.zeros(l_sc.shape, jnp.float32)
        acc_sc[...] = jnp.zeros(acc_sc.shape, jnp.float32)

    @pl.when(diag_ref[step_at] == 0)
    def _full():
        online_step(q_ref, k_ref, v_ref, m_sc, l_sc, acc_sc, group_size, False)

    @pl.when(diag_ref[step_at] == 1)
    def _diag():
        online_step(q_ref, k_ref, v_ref, m_sc, l_sc, acc_sc, group_size, True)
        acc_ref[...] = acc_sc[...]
        lane = lax.broadcasted_iota(jnp.int32, ml_ref.shape, 1)
        packed = jnp.zeros(ml_ref.shape, jnp.float32)
        for head in range(group_size):
            packed = jnp.where(lane == head, m_sc[head], packed)
            packed = jnp.where(lane == group_size + head, l_sc[head], packed)
        ml_ref[...] = packed


def far_kernel(qp_ref, kp_ref, first_ref, last_ref, valid_ref, gate_ref, q_ref, k_ref, v_ref,
               s_ref, acc_in, ml_in, o_ref, m_sc, l_sc, acc_sc, *, group_size):
    kv_head = pl.program_id(0)
    step_at = pl.program_id(1)

    @pl.when(first_ref[step_at] == 1)
    def _init():
        packed = ml_in[...]
        for head in range(group_size):
            m_sc[head] = jnp.broadcast_to(packed[:, head : head + 1], m_sc.shape[1:])
            l_sc[head] = jnp.broadcast_to(
                packed[:, group_size + head : group_size + head + 1], l_sc.shape[1:]
            )
        acc_sc[...] = acc_in[...]

    @pl.when(valid_ref[step_at] == 1)
    def _step():
        online_step(q_ref, k_ref, v_ref, m_sc, l_sc, acc_sc, group_size, False)

    @pl.when(last_ref[step_at] == 1)
    def _last():
        memory = s_ref[:HD, :]
        normalizer = s_ref[HD : HD + 1, :]
        for head in range(group_size):
            lanes = slice(head * HD, (head + 1) * HD)
            local_part = acc_sc[:, lanes] / l_sc[head]
            query_feature = feature(q_ref[:, lanes].astype(jnp.float32))
            numerator = jnp.dot(
                query_feature, memory, precision=lax.Precision.HIGHEST,
                preferred_element_type=jnp.float32,
            )
            denominator = jnp.maximum(
                jnp.sum(query_feature * normalizer, axis=-1, keepdims=True), 1.0
            )
            mixing = gate_ref[kv_head * group_size + head]
            o_ref[:, lanes] = (
                mixing * (numerator / denominator) + (1.0 - mixing) * local_part
            ).astype(o_ref.dtype)


def near_tables(core):
    tables = np.array(
        [[[c, 1 ^ c, 1 ^ c], [c, c, 1 ^ c], [1, 1, 0], [1, 0, 1]] for c in range(2)], np.int32
    )
    return jnp.asarray(tables)[core]


def far_tables(chips, chip, core):
    per_block = max(1, 2 * (chips - 1))
    tables = np.zeros((chips, 2, 5, 2 * per_block), np.int32)
    for y in range(chips):
        for c in range(2):
            steps = []
            for a in range(2):
                k_pos = 0
                for j in range(per_block):
                    valid = int(j < 2 * y)
                    if valid:
                        k_pos = 2 * (chips - 1 - y + j // 2) + ((j % 2) ^ c)
                    steps.append((a ^ c, k_pos, int(j == 0), int(j == per_block - 1), valid))
            tables[y, c] = np.array(steps, np.int32).T
    return jnp.asarray(tables)[chip, core]


def attend(query_rows, near_kv, far_kv, state, mixing, chips, chip, core, group_size):
    _, block, q_cols = query_rows.shape
    kv_group = near_kv.shape[-1] // (2 * HD)
    width = group_size * HD
    scratch = [
        pltpu.VMEM((group_size, block, LANES), jnp.float32),
        pltpu.VMEM((group_size, block, LANES), jnp.float32),
        pltpu.VMEM((block, width), jnp.float32),
    ]
    params = pltpu.CompilerParams(dimension_semantics=("arbitrary", "arbitrary"))
    near = near_tables(core)
    near_spec = pltpu.PrefetchScalarGridSpec(
        num_scalar_prefetch=4,
        grid=(kv_group, near.shape[-1]),
        in_specs=[
            pl.BlockSpec((None, block, width), lambda g, t, qp, kp, f, d: (qp[t], 0, g)),
            pl.BlockSpec((None, block, HD), lambda g, t, qp, kp, f, d: (kp[t], 0, g)),
            pl.BlockSpec((None, block, HD), lambda g, t, qp, kp, f, d: (kp[t], 0, kv_group + g)),
        ],
        out_specs=[
            pl.BlockSpec((None, block, width), lambda g, t, qp, kp, f, d: (qp[t], 0, g)),
            pl.BlockSpec((None, None, block, LANES), lambda g, t, qp, kp, f, d: (g, qp[t], 0, 0)),
        ],
        scratch_shapes=scratch,
    )
    pair_flops = 4 * block * block * HD * group_size * kv_group
    pair_exps = block * block * group_size * kv_group
    acc, ml = pl.pallas_call(
        functools.partial(near_kernel, group_size=group_size),
        grid_spec=near_spec,
        cost_estimate=pl.CostEstimate(
            flops=3 * pair_flops, transcendentals=3 * pair_exps,
            bytes_accessed=int(query_rows.size * 6 + near_kv.size * 2),
        ),
        out_shape=[
            jax.ShapeDtypeStruct((2, block, q_cols), jnp.float32),
            jax.ShapeDtypeStruct((kv_group, 2, block, LANES), jnp.float32),
        ],
        compiler_params=params,
    )(*[near[i] for i in range(4)], query_rows, near_kv, near_kv)
    far = far_tables(chips, chip, core)
    far_spec = pltpu.PrefetchScalarGridSpec(
        num_scalar_prefetch=5,
        grid=(kv_group, far.shape[-1]),
        in_specs=[
            pl.BlockSpec(memory_space=pltpu.SMEM),
            pl.BlockSpec((None, block, width), lambda g, t, qp, kp, f, l, v: (qp[t], 0, g)),
            pl.BlockSpec((None, block, HD), lambda g, t, qp, kp, f, l, v: (kp[t], 0, g)),
            pl.BlockSpec((None, block, HD), lambda g, t, qp, kp, f, l, v: (kp[t], 0, kv_group + g)),
            pl.BlockSpec((None, STATE_ROWS, HD), lambda g, t, qp, kp, f, l, v: (g, 0, 0)),
            pl.BlockSpec((None, block, width), lambda g, t, qp, kp, f, l, v: (qp[t], 0, g)),
            pl.BlockSpec((None, None, block, LANES), lambda g, t, qp, kp, f, l, v: (g, qp[t], 0, 0)),
        ],
        out_specs=pl.BlockSpec((None, block, width), lambda g, t, qp, kp, f, l, v: (qp[t], 0, g)),
        scratch_shapes=scratch,
    )
    far_pairs = far.shape[-1]
    return pl.pallas_call(
        functools.partial(far_kernel, group_size=group_size),
        grid_spec=far_spec,
        cost_estimate=pl.CostEstimate(
            flops=far_pairs * pair_flops, transcendentals=far_pairs * pair_exps,
            bytes_accessed=int(query_rows.size * 8 + far_kv.size * 2),
        ),
        out_shape=jax.ShapeDtypeStruct((2, block, q_cols), jnp.bfloat16),
        compiler_params=params,
    )(*[far[i] for i in range(5)], mixing, query_rows, far_kv, far_kv, state, acc, ml)


def merge_kernel(core_ref, own_ref, back_ref, o_ref):
    @pl.when(pl.program_id(0) == core_ref[0])
    def _own():
        o_ref[...] = own_ref[...]

    @pl.when(pl.program_id(0) != core_ref[0])
    def _back():
        o_ref[...] = back_ref[...]


def merge_halves(own, back, core):
    tokens_here, q_cols = back.shape
    grid_spec = pltpu.PrefetchScalarGridSpec(
        num_scalar_prefetch=1,
        grid=(2,),
        in_specs=[
            pl.BlockSpec((None, tokens_here, q_cols), lambda h, c: (0, 0, 0)),
            pl.BlockSpec((tokens_here, q_cols), lambda h, c: (0, 0)),
        ],
        out_specs=pl.BlockSpec((tokens_here, q_cols), lambda h, c: (0, h)),
    )
    return pl.pallas_call(
        merge_kernel,
        grid_spec=grid_spec,
        out_shape=jax.ShapeDtypeStruct((tokens_here, 2 * q_cols), back.dtype),
    )(core.reshape(1), own, back)


def body(queries, keys, values, gate_logit):
    parts = lax.axis_size("head")
    chips = parts // 2
    place = lax.axis_index("head")
    chip = place // 2
    core = place % 2
    k_cols = keys.shape[1] // 2
    kv_group = k_cols // HD
    group_size = queries.shape[1] // keys.shape[1]
    sibling = [(p, p ^ 1) for p in range(parts)]

    delta = chip_states(keys, values, core, kv_group)
    keep_q, keep_kv, send_q, send_kv = split_inputs(queries, keys, values, core)
    recv_q = lax.ppermute(send_q, "head", sibling)
    recv_kv = lax.ppermute(send_kv, "head", sibling)
    delta, keep_kv, send_kv, recv_q, recv_kv = lax.optimization_barrier(
        (delta, keep_kv, send_kv, recv_q, recv_kv)
    )
    state = earlier_states(delta)
    kv_parts = []
    for s in range(chips - 1, 0, -1):
        kv_parts.append(lax.ppermute(keep_kv, "head", [(p, p + 2 * s) for p in range(parts - 2 * s)]))
        kv_parts.append(
            lax.ppermute(send_kv, "head", [(p, (p + 2 * s) ^ 1) for p in range(parts - 2 * s)])
        )
    query_rows = jnp.stack([keep_q, recv_q])
    near_kv = jnp.stack([keep_kv, recv_kv])
    far_kv = jnp.stack(kv_parts) if kv_parts else near_kv
    gate_here = lax.dynamic_slice_in_dim(gate_logit, core * kv_group * group_size, kv_group * group_size)
    mixing = jax.nn.sigmoid(gate_here)
    attended = attend(query_rows, near_kv, far_kv, state, mixing, chips, chip, core, group_size)
    back = lax.ppermute(attended[1], "head", sibling)
    return merge_halves(attended, back, core)


def solution(mesh):
    in_specs = (P(("seq", "head"), None), P(("seq", "head"), None), P(("seq", "head"), None), P())
    out_specs = P(("seq", "head"), None)
    return jax.shard_map(body, mesh=mesh, in_specs=in_specs, out_specs=out_specs, check_vma=False)
```

```python
import functools

import jax
import jax.numpy as jnp
import numpy as np
from jax import lax
from jax.experimental import pallas as pl
from jax.experimental.pallas import tpu as pltpu
from jax.sharding import PartitionSpec as P

HQ = 32
KVH = 8
HD = 128
SEG = 2048
LANES = 128
STATE_ROWS = HD + 8


def feature(inputs):
    return jnp.where(inputs > 0, inputs + 1.0, jnp.exp(jnp.minimum(inputs, 0.0)))


def shifted(value, axis, steps):
    count = lax.axis_size(axis)
    return lax.ppermute(value, axis, [(source, source + steps) for source in range(count - steps)])


def split_kernel(core_ref, q_keep, k_keep, v_keep, q_send, k_send, v_send, *out_refs):
    k_cols = k_keep.shape[-1]
    keep_q, keep_kv, send_q, send_kv = out_refs
    keep_q[...] = q_keep[...]
    keep_kv[:, :k_cols] = k_keep[...]
    keep_kv[:, k_cols:] = v_keep[...]
    send_q[...] = q_send[...]
    send_kv[:, :k_cols] = k_send[...]
    send_kv[:, k_cols:] = v_send[...]


def split_inputs(queries, keys, values, core):
    tokens_here, q_all = queries.shape
    q_cols = q_all // 2
    k_cols = keys.shape[1] // 2
    keep_map = lambda i, c: (0, c[0])
    send_map = lambda i, c: (0, 1 - c[0])
    q_shape = jax.ShapeDtypeStruct((tokens_here, q_cols), queries.dtype)
    kv_shape = jax.ShapeDtypeStruct((tokens_here, 2 * k_cols), keys.dtype)
    grid_spec = pltpu.PrefetchScalarGridSpec(
        num_scalar_prefetch=1,
        grid=(1,),
        in_specs=[
            pl.BlockSpec((tokens_here, q_cols), keep_map),
            pl.BlockSpec((tokens_here, k_cols), keep_map),
            pl.BlockSpec((tokens_here, k_cols), keep_map),
            pl.BlockSpec((tokens_here, q_cols), send_map),
            pl.BlockSpec((tokens_here, k_cols), send_map),
            pl.BlockSpec((tokens_here, k_cols), send_map),
        ],
        out_specs=[
            pl.BlockSpec((tokens_here, q_cols), lambda i, c: (0, 0)),
            pl.BlockSpec((tokens_here, 2 * k_cols), lambda i, c: (0, 0)),
        ]
        * 2,
    )
    return pl.pallas_call(
        split_kernel, grid_spec=grid_spec, out_shape=[q_shape, kv_shape] * 2
    )(core.reshape(1), queries, keys, values, queries, keys, values)


def delta_kernel(k_ref, v_ref, o_ref):
    @pl.when(pl.program_id(1) == 0)
    def _init():
        o_ref[...] = jnp.zeros(o_ref.shape, jnp.float32)

    key_feature = feature(k_ref[...].astype(jnp.float32))
    value_data = v_ref[...].astype(jnp.float32)
    o_ref[:HD, :] += jnp.dot(
        key_feature.T, value_data, precision=lax.Precision.HIGHEST,
        preferred_element_type=jnp.float32,
    )
    o_ref[HD : HD + 1, :] += jnp.sum(key_feature, axis=0, keepdims=True)


def local_deltas(keys, values):
    tokens_here, cols = keys.shape
    kv_heads = cols // HD
    return pl.pallas_call(
        delta_kernel,
        grid=(kv_heads, 1),
        in_specs=[pl.BlockSpec((tokens_here, HD), lambda g, t: (0, g))] * 2,
        out_specs=pl.BlockSpec((None, STATE_ROWS, HD), lambda g, t: (g, 0, 0)),
        out_shape=jax.ShapeDtypeStruct((kv_heads, STATE_ROWS, HD), jnp.float32),
        compiler_params=pltpu.CompilerParams(dimension_semantics=("arbitrary", "arbitrary")),
    )(keys, values)


def chip_states(keys, values, core, kv_group):
    total = local_deltas(keys, values)
    parts = lax.axis_size("head")
    keep = lax.dynamic_slice_in_dim(total, core * kv_group, kv_group)
    send = lax.dynamic_slice_in_dim(total, (1 - core) * kv_group, kv_group)
    total = keep + lax.ppermute(send, "head", [(p, p ^ 1) for p in range(parts)])
    steps = 2
    while steps < parts:
        total = total + lax.ppermute(total, "head", [(p, p ^ steps) for p in range(parts)])
        steps *= 2
    return total


def earlier_states(delta):
    count = lax.axis_size("seq")
    total = delta
    steps = 1
    while steps < count:
        total = total + shifted(total, "seq", steps)
        steps *= 2
    return total - delta


def online_step(q_ref, k_ref, v_ref, m_sc, l_sc, acc_sc, group_size, masked):
    block = q_ref.shape[0]
    score_scale = HD ** (-0.5)
    key_rows = k_ref[...]
    value_rows = jnp.concatenate([v_ref[...], jnp.ones((block, LANES), v_ref.dtype)], axis=1)
    if masked:
        rows = lax.broadcasted_iota(jnp.int32, (block, block), 0)
        cols = lax.broadcasted_iota(jnp.int32, (block, block), 1)
        allowed = cols <= rows
    for head in range(group_size):
        lanes = slice(head * HD, (head + 1) * HD)
        scores = lax.dot_general(
            q_ref[:, lanes], key_rows, (((1,), (1,)), ((), ())),
            preferred_element_type=jnp.float32,
        )
        if masked:
            scores = jnp.where(allowed, scores, -1e30)
        m_prev = m_sc[head]
        m_new = jnp.maximum(m_prev, jnp.max(scores, axis=-1, keepdims=True) * score_scale)
        probs = jnp.exp(scores * score_scale - m_new[:, :1])
        alpha = jnp.exp(m_prev - m_new)
        both = jnp.dot(probs.astype(jnp.bfloat16), value_rows, preferred_element_type=jnp.float32)
        l_sc[head] = alpha * l_sc[head] + both[:, HD:]
        acc_sc[:, lanes] = alpha * acc_sc[:, lanes] + both[:, :HD]
        m_sc[head] = m_new


def near_kernel(qp_ref, kp_ref, first_ref, diag_ref, q_ref, k_ref, v_ref, acc_ref, ml_ref,
                m_sc, l_sc, acc_sc, *, group_size):
    step_at = pl.program_id(1)

    @pl.when(first_ref[step_at] == 1)
    def _init():
        m_sc[...] = jnp.full(m_sc.shape, -jnp.inf, jnp.float32)
        l_sc[...] = jnp.zeros(l_sc.shape, jnp.float32)
        acc_sc[...] = jnp.zeros(acc_sc.shape, jnp.float32)

    @pl.when(diag_ref[step_at] == 0)
    def _full():
        online_step(q_ref, k_ref, v_ref, m_sc, l_sc, acc_sc, group_size, False)

    @pl.when(diag_ref[step_at] == 1)
    def _diag():
        online_step(q_ref, k_ref, v_ref, m_sc, l_sc, acc_sc, group_size, True)
        acc_ref[...] = acc_sc[...]
        lane = lax.broadcasted_iota(jnp.int32, ml_ref.shape, 1)
        packed = jnp.zeros(ml_ref.shape, jnp.float32)
        for head in range(group_size):
            packed = jnp.where(lane == head, m_sc[head], packed)
            packed = jnp.where(lane == group_size + head, l_sc[head], packed)
        ml_ref[...] = packed


def far_kernel(qp_ref, kp_ref, first_ref, last_ref, valid_ref, gate_ref, q_ref, k_ref, v_ref,
               s_ref, acc_in, ml_in, o_ref, m_sc, l_sc, acc_sc, *, group_size):
    kv_head = pl.program_id(0)
    step_at = pl.program_id(1)

    @pl.when(first_ref[step_at] == 1)
    def _init():
        packed = ml_in[...]
        for head in range(group_size):
            m_sc[head] = jnp.broadcast_to(packed[:, head : head + 1], m_sc.shape[1:])
            l_sc[head] = jnp.broadcast_to(
                packed[:, group_size + head : group_size + head + 1], l_sc.shape[1:]
            )
        acc_sc[...] = acc_in[...]

    @pl.when(valid_ref[step_at] == 1)
    def _step():
        online_step(q_ref, k_ref, v_ref, m_sc, l_sc, acc_sc, group_size, False)

    @pl.when(last_ref[step_at] == 1)
    def _last():
        memory = s_ref[:HD, :]
        normalizer = s_ref[HD : HD + 1, :]
        for head in range(group_size):
            lanes = slice(head * HD, (head + 1) * HD)
            local_part = acc_sc[:, lanes] / l_sc[head]
            query_feature = feature(q_ref[:, lanes].astype(jnp.float32))
            numerator = jnp.dot(
                query_feature, memory, precision=lax.Precision.HIGHEST,
                preferred_element_type=jnp.float32,
            )
            denominator = jnp.maximum(
                jnp.sum(query_feature * normalizer, axis=-1, keepdims=True), 1.0
            )
            mixing = gate_ref[kv_head * group_size + head]
            o_ref[:, lanes] = (
                mixing * (numerator / denominator) + (1.0 - mixing) * local_part
            ).astype(o_ref.dtype)


def near_tables(core):
    tables = np.array(
        [[[c, 1 ^ c, 1 ^ c], [c, c, 1 ^ c], [1, 1, 0], [1, 0, 1]] for c in range(2)], np.int32
    )
    return jnp.asarray(tables)[core]


def far_tables(chips, chip, core):
    per_block = max(1, 2 * (chips - 1))
    tables = np.zeros((chips, 2, 5, 2 * per_block), np.int32)
    for y in range(chips):
        for c in range(2):
            steps = []
            for a in range(2):
                k_pos = 0
                for j in range(per_block):
                    valid = int(j < 2 * y)
                    if valid:
                        k_pos = 2 * (chips - 1 - y + j // 2) + ((j % 2) ^ c)
                    steps.append((a ^ c, k_pos, int(j == 0), int(j == per_block - 1), valid))
            tables[y, c] = np.array(steps, np.int32).T
    return jnp.asarray(tables)[chip, core]


def attend(query_rows, near_kv, far_kv, state, mixing, chips, chip, core, group_size):
    _, block, q_cols = query_rows.shape
    kv_group = near_kv.shape[-1] // (2 * HD)
    width = group_size * HD
    scratch = [
        pltpu.VMEM((group_size, block, LANES), jnp.float32),
        pltpu.VMEM((group_size, block, LANES), jnp.float32),
        pltpu.VMEM((block, width), jnp.float32),
    ]
    params = pltpu.CompilerParams(dimension_semantics=("arbitrary", "arbitrary"))
    near = near_tables(core)
    near_spec = pltpu.PrefetchScalarGridSpec(
        num_scalar_prefetch=4,
        grid=(kv_group, near.shape[-1]),
        in_specs=[
            pl.BlockSpec((None, block, width), lambda g, t, qp, kp, f, d: (qp[t], 0, g)),
            pl.BlockSpec((None, block, HD), lambda g, t, qp, kp, f, d: (kp[t], 0, g)),
            pl.BlockSpec((None, block, HD), lambda g, t, qp, kp, f, d: (kp[t], 0, kv_group + g)),
        ],
        out_specs=[
            pl.BlockSpec((None, block, width), lambda g, t, qp, kp, f, d: (qp[t], 0, g)),
            pl.BlockSpec((None, None, block, LANES), lambda g, t, qp, kp, f, d: (g, qp[t], 0, 0)),
        ],
        scratch_shapes=scratch,
    )
    pair_flops = 4 * block * block * HD * group_size * kv_group
    pair_exps = block * block * group_size * kv_group
    acc, ml = pl.pallas_call(
        functools.partial(near_kernel, group_size=group_size),
        grid_spec=near_spec,
        cost_estimate=pl.CostEstimate(
            flops=3 * pair_flops, transcendentals=3 * pair_exps,
            bytes_accessed=int(query_rows.size * 6 + near_kv.size * 2),
        ),
        out_shape=[
            jax.ShapeDtypeStruct((2, block, q_cols), jnp.float32),
            jax.ShapeDtypeStruct((kv_group, 2, block, LANES), jnp.float32),
        ],
        compiler_params=params,
    )(*[near[i] for i in range(4)], query_rows, near_kv, near_kv)
    far = far_tables(chips, chip, core)
    far_spec = pltpu.PrefetchScalarGridSpec(
        num_scalar_prefetch=5,
        grid=(kv_group, far.shape[-1]),
        in_specs=[
            pl.BlockSpec(memory_space=pltpu.SMEM),
            pl.BlockSpec((None, block, width), lambda g, t, qp, kp, f, l, v: (qp[t], 0, g)),
            pl.BlockSpec((None, block, HD), lambda g, t, qp, kp, f, l, v: (kp[t], 0, g)),
            pl.BlockSpec((None, block, HD), lambda g, t, qp, kp, f, l, v: (kp[t], 0, kv_group + g)),
            pl.BlockSpec((None, STATE_ROWS, HD), lambda g, t, qp, kp, f, l, v: (g, 0, 0)),
            pl.BlockSpec((None, block, width), lambda g, t, qp, kp, f, l, v: (qp[t], 0, g)),
            pl.BlockSpec((None, None, block, LANES), lambda g, t, qp, kp, f, l, v: (g, qp[t], 0, 0)),
        ],
        out_specs=pl.BlockSpec((None, block, width), lambda g, t, qp, kp, f, l, v: (qp[t], 0, g)),
        scratch_shapes=scratch,
    )
    far_pairs = far.shape[-1]
    return pl.pallas_call(
        functools.partial(far_kernel, group_size=group_size),
        grid_spec=far_spec,
        cost_estimate=pl.CostEstimate(
            flops=far_pairs * pair_flops, transcendentals=far_pairs * pair_exps,
            bytes_accessed=int(query_rows.size * 8 + far_kv.size * 2),
        ),
        out_shape=jax.ShapeDtypeStruct((2, block, q_cols), jnp.bfloat16),
        compiler_params=params,
    )(*[far[i] for i in range(5)], mixing, query_rows, far_kv, far_kv, state, acc, ml)


def merge_kernel(core_ref, own_ref, back_ref, o_ref):
    @pl.when(pl.program_id(0) == core_ref[0])
    def _own():
        o_ref[...] = own_ref[...]

    @pl.when(pl.program_id(0) != core_ref[0])
    def _back():
        o_ref[...] = back_ref[...]


def merge_halves(own, back, core):
    tokens_here, q_cols = back.shape
    grid_spec = pltpu.PrefetchScalarGridSpec(
        num_scalar_prefetch=1,
        grid=(2,),
        in_specs=[
            pl.BlockSpec((None, tokens_here, q_cols), lambda h, c: (0, 0, 0)),
            pl.BlockSpec((tokens_here, q_cols), lambda h, c: (0, 0)),
        ],
        out_specs=pl.BlockSpec((tokens_here, q_cols), lambda h, c: (0, h)),
    )
    return pl.pallas_call(
        merge_kernel,
        grid_spec=grid_spec,
        out_shape=jax.ShapeDtypeStruct((tokens_here, 2 * q_cols), back.dtype),
    )(core.reshape(1), own, back)


def body(queries, keys, values, gate_logit):
    parts = lax.axis_size("head")
    chips = parts // 2
    place = lax.axis_index("head")
    chip = place // 2
    core = place % 2
    k_cols = keys.shape[1] // 2
    kv_group = k_cols // HD
    group_size = queries.shape[1] // keys.shape[1]
    sibling = [(p, p ^ 1) for p in range(parts)]

    delta = chip_states(keys, values, core, kv_group)
    keep_q, keep_kv, send_q, send_kv = split_inputs(queries, keys, values, core)
    recv_q = lax.ppermute(send_q, "head", sibling)
    recv_kv = lax.ppermute(send_kv, "head", sibling)
    delta, keep_kv, send_kv, recv_q, recv_kv = lax.optimization_barrier(
        (delta, keep_kv, send_kv, recv_q, recv_kv)
    )
    state = earlier_states(delta)
    kv_parts = []
    for s in range(chips - 1, 0, -1):
        kv_parts.append(lax.ppermute(keep_kv, "head", [(p, p + 2 * s) for p in range(parts - 2 * s)]))
        kv_parts.append(
            lax.ppermute(send_kv, "head", [(p, (p + 2 * s) ^ 1) for p in range(parts - 2 * s)])
        )
    query_rows = jnp.stack([keep_q, recv_q])
    near_kv = jnp.stack([keep_kv, recv_kv])
    far_kv = jnp.stack(kv_parts) if kv_parts else near_kv
    gate_here = lax.dynamic_slice_in_dim(gate_logit, core * kv_group * group_size, kv_group * group_size)
    mixing = jax.nn.sigmoid(gate_here)
    attended = attend(query_rows, near_kv, far_kv, state, mixing, chips, chip, core, group_size)
    back = lax.ppermute(attended[1], "head", sibling)
    return merge_halves(attended, back, core)


def solution(mesh):
    in_specs = (P(("seq", "head"), None), P(("seq", "head"), None), P(("seq", "head"), None), P())
    out_specs = P(("seq", "head"), None)
    return jax.shard_map(body, mesh=mesh, in_specs=in_specs, out_specs=out_specs, check_vma=False)
```

```python
import functools

import jax
import jax.numpy as jnp
import numpy as np
from jax import lax
from jax.experimental import pallas as pl
from jax.experimental.pallas import tpu as pltpu
from jax.sharding import PartitionSpec as P

HQ = 32
KVH = 8
HD = 128
SEG = 2048
LANES = 128
STATE_ROWS = HD + 8


def feature(inputs):
    return jnp.where(inputs > 0, inputs + 1.0, jnp.exp(jnp.minimum(inputs, 0.0)))


def shifted(value, axis, steps):
    count = lax.axis_size(axis)
    return lax.ppermute(value, axis, [(source, source + steps) for source in range(count - steps)])


def split_kernel(core_ref, q_keep, k_keep, v_keep, q_send, k_send, v_send, *out_refs):
    k_cols = k_keep.shape[-1]
    keep_q, keep_kv, send_q, send_kv = out_refs
    keep_q[...] = q_keep[...]
    keep_kv[:, :k_cols] = k_keep[...]
    keep_kv[:, k_cols:] = v_keep[...]
    send_q[...] = q_send[...]
    send_kv[:, :k_cols] = k_send[...]
    send_kv[:, k_cols:] = v_send[...]


def split_inputs(queries, keys, values, core):
    tokens_here, q_all = queries.shape
    q_cols = q_all // 2
    k_cols = keys.shape[1] // 2
    keep_map = lambda i, c: (0, c[0])
    send_map = lambda i, c: (0, 1 - c[0])
    q_shape = jax.ShapeDtypeStruct((tokens_here, q_cols), queries.dtype)
    kv_shape = jax.ShapeDtypeStruct((tokens_here, 2 * k_cols), keys.dtype)
    grid_spec = pltpu.PrefetchScalarGridSpec(
        num_scalar_prefetch=1,
        grid=(1,),
        in_specs=[
            pl.BlockSpec((tokens_here, q_cols), keep_map),
            pl.BlockSpec((tokens_here, k_cols), keep_map),
            pl.BlockSpec((tokens_here, k_cols), keep_map),
            pl.BlockSpec((tokens_here, q_cols), send_map),
            pl.BlockSpec((tokens_here, k_cols), send_map),
            pl.BlockSpec((tokens_here, k_cols), send_map),
        ],
        out_specs=[
            pl.BlockSpec((tokens_here, q_cols), lambda i, c: (0, 0)),
            pl.BlockSpec((tokens_here, 2 * k_cols), lambda i, c: (0, 0)),
        ]
        * 2,
    )
    return pl.pallas_call(
        split_kernel, grid_spec=grid_spec, out_shape=[q_shape, kv_shape] * 2
    )(core.reshape(1), queries, keys, values, queries, keys, values)


def delta_kernel(k_ref, v_ref, o_ref):
    for head in range(o_ref.shape[0]):
        lanes = slice(head * HD, (head + 1) * HD)
        key_feature = feature(k_ref[:, lanes].astype(jnp.float32))
        value_data = v_ref[:, lanes].astype(jnp.float32)
        o_ref[head, :HD, :] = jnp.dot(
            key_feature.T, value_data, precision=lax.Precision.HIGHEST,
            preferred_element_type=jnp.float32,
        )
        o_ref[head, HD:, :] = jnp.zeros((STATE_ROWS - HD, HD), jnp.float32)
        o_ref[head, HD : HD + 1, :] = jnp.sum(key_feature, axis=0, keepdims=True)


def local_deltas(keys, values):
    kv_heads = keys.shape[1] // HD
    return pl.pallas_call(
        delta_kernel,
        out_shape=jax.ShapeDtypeStruct((kv_heads, STATE_ROWS, HD), jnp.float32),
    )(keys, values)


def chip_states(keys, values, core, kv_group):
    total = local_deltas(keys, values)
    parts = lax.axis_size("head")
    keep = lax.dynamic_slice_in_dim(total, core * kv_group, kv_group)
    send = lax.dynamic_slice_in_dim(total, (1 - core) * kv_group, kv_group)
    total = keep + lax.ppermute(send, "head", [(p, p ^ 1) for p in range(parts)])
    steps = 2
    while steps < parts:
        total = total + lax.ppermute(total, "head", [(p, p ^ steps) for p in range(parts)])
        steps *= 2
    return total


def earlier_states(delta):
    count = lax.axis_size("seq")
    total = delta
    steps = 1
    while steps < count:
        total = total + shifted(total, "seq", steps)
        steps *= 2
    return total - delta


def online_step(q_ref, k_ref, v_ref, m_sc, l_sc, acc_sc, group_size, masked):
    block = q_ref.shape[0]
    score_scale = HD ** (-0.5)
    key_rows = k_ref[...]
    value_rows = jnp.concatenate([v_ref[...], jnp.ones((block, LANES), v_ref.dtype)], axis=1)
    if masked:
        rows = lax.broadcasted_iota(jnp.int32, (block, block), 0)
        cols = lax.broadcasted_iota(jnp.int32, (block, block), 1)
        allowed = cols <= rows
    for head in range(group_size):
        lanes = slice(head * HD, (head + 1) * HD)
        scores = lax.dot_general(
            q_ref[:, lanes], key_rows, (((1,), (1,)), ((), ())),
            preferred_element_type=jnp.float32,
        )
        if masked:
            scores = jnp.where(allowed, scores, -1e30)
        m_prev = m_sc[head]
        m_new = jnp.maximum(m_prev, jnp.max(scores, axis=-1, keepdims=True) * score_scale)
        probs = jnp.exp(scores * score_scale - m_new[:, :1])
        alpha = jnp.exp(m_prev - m_new)
        both = jnp.dot(probs.astype(jnp.bfloat16), value_rows, preferred_element_type=jnp.float32)
        l_sc[head] = alpha * l_sc[head] + both[:, HD:]
        acc_sc[:, lanes] = alpha * acc_sc[:, lanes] + both[:, :HD]
        m_sc[head] = m_new


def near_kernel(qs_ref, ks_ref, first_ref, diag_ref, q_keep, q_recv, k_keep, v_keep, k_recv,
                v_recv, acc_ref, ml_ref, m_sc, l_sc, acc_sc, *, group_size):
    step_at = pl.program_id(1)
    q_src = qs_ref[step_at]
    k_src = ks_ref[step_at]
    diag = diag_ref[step_at] == 1

    @pl.when(first_ref[step_at] == 1)
    def _init():
        m_sc[...] = jnp.full(m_sc.shape, -jnp.inf, jnp.float32)
        l_sc[...] = jnp.zeros(l_sc.shape, jnp.float32)
        acc_sc[...] = jnp.zeros(acc_sc.shape, jnp.float32)

    sources = ((q_keep, k_keep, v_keep), (q_recv, k_recv, v_recv))
    for q_at in range(2):
        for k_at in range(2):
            masked = q_at == k_at

            @pl.when((q_src == q_at) & (k_src == k_at) & (diag == masked))
            def _step():
                q_ref = sources[q_at][0]
                online_step(q_ref, sources[k_at][1], sources[k_at][2], m_sc, l_sc, acc_sc,
                            group_size, masked)

    @pl.when(diag)
    def _save():
        acc_ref[...] = acc_sc[...]
        lane = lax.broadcasted_iota(jnp.int32, ml_ref.shape, 1)
        packed = jnp.zeros(ml_ref.shape, jnp.float32)
        for head in range(group_size):
            packed = jnp.where(lane == head, m_sc[head], packed)
            packed = jnp.where(lane == group_size + head, l_sc[head], packed)
        ml_ref[...] = packed


def far_kernel(qp_ref, kp_ref, first_ref, last_ref, valid_ref, gate_ref, q_keep, q_recv, k_ref,
               v_ref, s_ref, acc_in, ml_in, o_ref, m_sc, l_sc, acc_sc, *, group_size):
    kv_head = pl.program_id(0)
    step_at = pl.program_id(1)

    @pl.when(first_ref[step_at] == 1)
    def _init():
        packed = ml_in[...]
        for head in range(group_size):
            m_sc[head] = jnp.broadcast_to(packed[:, head : head + 1], m_sc.shape[1:])
            l_sc[head] = jnp.broadcast_to(
                packed[:, group_size + head : group_size + head + 1], l_sc.shape[1:]
            )
        acc_sc[...] = acc_in[...]

    for q_at, q_ref in enumerate((q_keep, q_recv)):
        chosen = qp_ref[step_at] == q_at

        @pl.when(chosen & (valid_ref[step_at] == 1))
        def _step():
            online_step(q_ref, k_ref, v_ref, m_sc, l_sc, acc_sc, group_size, False)

        @pl.when(chosen & (last_ref[step_at] == 1))
        def _last():
            finish(q_ref, s_ref, gate_ref, o_ref, acc_sc, l_sc, kv_head, group_size)


def finish(q_ref, s_ref, gate_ref, o_ref, acc_sc, l_sc, kv_head, group_size):
    memory = s_ref[:HD, :]
    normalizer = s_ref[HD : HD + 1, :]
    for head in range(group_size):
        lanes = slice(head * HD, (head + 1) * HD)
        local_part = acc_sc[:, lanes] / l_sc[head]
        query_feature = feature(q_ref[:, lanes].astype(jnp.float32))
        numerator = jnp.dot(
            query_feature, memory, precision=lax.Precision.HIGHEST,
            preferred_element_type=jnp.float32,
        )
        denominator = jnp.maximum(
            jnp.sum(query_feature * normalizer, axis=-1, keepdims=True), 1.0
        )
        mixing = gate_ref[kv_head * group_size + head]
        o_ref[:, lanes] = (
            mixing * (numerator / denominator) + (1.0 - mixing) * local_part
        ).astype(o_ref.dtype)


def near_tables(core):
    tables = np.array(
        [[[c, 1 ^ c, 1 ^ c], [c, c, 1 ^ c], [1, 1, 0], [1, 0, 1]] for c in range(2)], np.int32
    )
    return jnp.asarray(tables)[core]


def far_tables(chips, chip, core):
    per_block = max(1, 2 * (chips - 1))
    tables = np.zeros((chips, 2, 5, 2 * per_block), np.int32)
    for y in range(chips):
        for c in range(2):
            steps = []
            for a in range(2):
                k_pos = 0
                for j in range(per_block):
                    valid = int(j < 2 * y)
                    if valid:
                        k_pos = 2 * (chips - 1 - y + j // 2) + ((j % 2) ^ c)
                    steps.append((a ^ c, k_pos, int(j == 0), int(j == per_block - 1), valid))
            tables[y, c] = np.array(steps, np.int32).T
    return jnp.asarray(tables)[chip, core]


def attend(keep_q, recv_q, keep_kv, recv_kv, far_kv, state, mixing, chips, chip, core, group_size):
    block, q_cols = keep_q.shape
    kv_group = keep_kv.shape[-1] // (2 * HD)
    width = group_size * HD
    scratch = [
        pltpu.VMEM((group_size, block, LANES), jnp.float32),
        pltpu.VMEM((group_size, block, LANES), jnp.float32),
        pltpu.VMEM((block, width), jnp.float32),
    ]
    params = pltpu.CompilerParams(dimension_semantics=("arbitrary", "arbitrary"))
    near = near_tables(core)
    q_spec = pl.BlockSpec((block, width), lambda g, t, *_: (0, g))
    k_spec = pl.BlockSpec((block, HD), lambda g, t, *_: (0, g))
    v_spec = pl.BlockSpec((block, HD), lambda g, t, *_: (0, kv_group + g))
    near_spec = pltpu.PrefetchScalarGridSpec(
        num_scalar_prefetch=4,
        grid=(kv_group, near.shape[-1]),
        in_specs=[q_spec, q_spec, k_spec, v_spec, k_spec, v_spec],
        out_specs=[
            pl.BlockSpec((None, block, width), lambda g, t, qs, ks, f, d: (qs[t], 0, g)),
            pl.BlockSpec((None, None, block, LANES), lambda g, t, qs, ks, f, d: (g, qs[t], 0, 0)),
        ],
        scratch_shapes=scratch,
    )
    pair_flops = 4 * block * block * HD * group_size * kv_group
    pair_exps = block * block * group_size * kv_group
    acc, ml = pl.pallas_call(
        functools.partial(near_kernel, group_size=group_size),
        grid_spec=near_spec,
        cost_estimate=pl.CostEstimate(
            flops=3 * pair_flops, transcendentals=3 * pair_exps,
            bytes_accessed=int(keep_q.size * 12 + keep_kv.size * 4),
        ),
        out_shape=[
            jax.ShapeDtypeStruct((2, block, q_cols), jnp.float32),
            jax.ShapeDtypeStruct((kv_group, 2, block, LANES), jnp.float32),
        ],
        compiler_params=params,
    )(*[near[i] for i in range(4)], keep_q, recv_q, keep_kv, keep_kv, recv_kv, recv_kv)
    far = far_tables(chips, chip, core)
    far_spec = pltpu.PrefetchScalarGridSpec(
        num_scalar_prefetch=5,
        grid=(kv_group, far.shape[-1]),
        in_specs=[
            pl.BlockSpec(memory_space=pltpu.SMEM),
            q_spec,
            q_spec,
            pl.BlockSpec((None, block, HD), lambda g, t, qp, kp, f, l, v: (kp[t], 0, g)),
            pl.BlockSpec((None, block, HD), lambda g, t, qp, kp, f, l, v: (kp[t], 0, kv_group + g)),
            pl.BlockSpec((None, STATE_ROWS, HD), lambda g, t, qp, kp, f, l, v: (g, 0, 0)),
            pl.BlockSpec((None, block, width), lambda g, t, qp, kp, f, l, v: (qp[t], 0, g)),
            pl.BlockSpec((None, None, block, LANES), lambda g, t, qp, kp, f, l, v: (g, qp[t], 0, 0)),
        ],
        out_specs=pl.BlockSpec((None, block, width), lambda g, t, qp, kp, f, l, v: (qp[t], 0, g)),
        scratch_shapes=scratch,
    )
    far_pairs = far.shape[-1]
    return pl.pallas_call(
        functools.partial(far_kernel, group_size=group_size),
        grid_spec=far_spec,
        cost_estimate=pl.CostEstimate(
            flops=far_pairs * pair_flops, transcendentals=far_pairs * pair_exps,
            bytes_accessed=int(keep_q.size * 16 + far_kv.size * 2),
        ),
        out_shape=jax.ShapeDtypeStruct((2, block, q_cols), jnp.bfloat16),
        compiler_params=params,
    )(*[far[i] for i in range(5)], mixing, keep_q, recv_q, far_kv, far_kv, state, acc, ml)


def merge_kernel(core_ref, own_ref, back_ref, o_ref):
    @pl.when(pl.program_id(0) == core_ref[0])
    def _own():
        o_ref[...] = own_ref[...]

    @pl.when(pl.program_id(0) != core_ref[0])
    def _back():
        o_ref[...] = back_ref[...]


def merge_halves(own, back, core):
    tokens_here, q_cols = back.shape
    grid_spec = pltpu.PrefetchScalarGridSpec(
        num_scalar_prefetch=1,
        grid=(2,),
        in_specs=[
            pl.BlockSpec((None, tokens_here, q_cols), lambda h, c: (0, 0, 0)),
            pl.BlockSpec((tokens_here, q_cols), lambda h, c: (0, 0)),
        ],
        out_specs=pl.BlockSpec((tokens_here, q_cols), lambda h, c: (0, h)),
    )
    return pl.pallas_call(
        merge_kernel,
        grid_spec=grid_spec,
        out_shape=jax.ShapeDtypeStruct((tokens_here, 2 * q_cols), back.dtype),
    )(core.reshape(1), own, back)


def body(queries, keys, values, gate_logit):
    parts = lax.axis_size("head")
    chips = parts // 2
    place = lax.axis_index("head")
    chip = place // 2
    core = place % 2
    k_cols = keys.shape[1] // 2
    kv_group = k_cols // HD
    group_size = queries.shape[1] // keys.shape[1]
    sibling = [(p, p ^ 1) for p in range(parts)]

    delta = chip_states(keys, values, core, kv_group)
    keep_q, keep_kv, send_q, send_kv = split_inputs(queries, keys, values, core)
    recv_q = lax.ppermute(send_q, "head", sibling)
    recv_kv = lax.ppermute(send_kv, "head", sibling)
    delta, keep_kv, send_kv, recv_q, recv_kv = lax.optimization_barrier(
        (delta, keep_kv, send_kv, recv_q, recv_kv)
    )
    state = earlier_states(delta)
    kv_parts = []
    for s in range(chips - 1, 0, -1):
        kv_parts.append(lax.ppermute(keep_kv, "head", [(p, p + 2 * s) for p in range(parts - 2 * s)]))
        kv_parts.append(
            lax.ppermute(send_kv, "head", [(p, (p + 2 * s) ^ 1) for p in range(parts - 2 * s)])
        )
    far_kv = jnp.stack(kv_parts) if kv_parts else jnp.stack([keep_kv, recv_kv])
    gate_here = lax.dynamic_slice_in_dim(gate_logit, core * kv_group * group_size, kv_group * group_size)
    mixing = jax.nn.sigmoid(gate_here)
    attended = attend(
        keep_q, recv_q, keep_kv, recv_kv, far_kv, state, mixing, chips, chip, core, group_size
    )
    back = lax.ppermute(attended[1], "head", sibling)
    return merge_halves(attended, back, core)


def solution(mesh):
    in_specs = (P(("seq", "head"), None), P(("seq", "head"), None), P(("seq", "head"), None), P())
    out_specs = P(("seq", "head"), None)
    return jax.shard_map(body, mesh=mesh, in_specs=in_specs, out_specs=out_specs, check_vma=False)
```

```python
import functools

import jax
import jax.numpy as jnp
import numpy as np
from jax import lax
from jax.experimental import pallas as pl
from jax.experimental.pallas import tpu as pltpu
from jax.sharding import PartitionSpec as P

HQ = 32
KVH = 8
HD = 128
SEG = 2048
LANES = 128
STATE_ROWS = HD + 8


def feature(inputs):
    return jnp.where(inputs > 0, inputs + 1.0, jnp.exp(jnp.minimum(inputs, 0.0)))


def shifted(value, axis, steps):
    count = lax.axis_size(axis)
    return lax.ppermute(value, axis, [(source, source + steps) for source in range(count - steps)])


def split_kernel(core_ref, q_keep, k_keep, v_keep, q_send, k_send, v_send, *out_refs):
    k_cols = k_keep.shape[-1]
    keep_q, keep_kv, send_q, send_kv = out_refs
    keep_q[...] = q_keep[...]
    keep_kv[:, :k_cols] = k_keep[...]
    keep_kv[:, k_cols:] = v_keep[...]
    send_q[...] = q_send[...]
    send_kv[:, :k_cols] = k_send[...]
    send_kv[:, k_cols:] = v_send[...]


def split_inputs(queries, keys, values, core):
    tokens_here, q_all = queries.shape
    q_cols = q_all // 2
    k_cols = keys.shape[1] // 2
    keep_map = lambda i, c: (0, c[0])
    send_map = lambda i, c: (0, 1 - c[0])
    q_shape = jax.ShapeDtypeStruct((tokens_here, q_cols), queries.dtype)
    kv_shape = jax.ShapeDtypeStruct((tokens_here, 2 * k_cols), keys.dtype)
    grid_spec = pltpu.PrefetchScalarGridSpec(
        num_scalar_prefetch=1,
        grid=(1,),
        in_specs=[
            pl.BlockSpec((tokens_here, q_cols), keep_map),
            pl.BlockSpec((tokens_here, k_cols), keep_map),
            pl.BlockSpec((tokens_here, k_cols), keep_map),
            pl.BlockSpec((tokens_here, q_cols), send_map),
            pl.BlockSpec((tokens_here, k_cols), send_map),
            pl.BlockSpec((tokens_here, k_cols), send_map),
        ],
        out_specs=[
            pl.BlockSpec((tokens_here, q_cols), lambda i, c: (0, 0)),
            pl.BlockSpec((tokens_here, 2 * k_cols), lambda i, c: (0, 0)),
        ]
        * 2,
    )
    return pl.pallas_call(
        split_kernel, grid_spec=grid_spec, out_shape=[q_shape, kv_shape] * 2
    )(core.reshape(1), queries, keys, values, queries, keys, values)


def delta_kernel(k_ref, v_ref, o_ref):
    for head in range(o_ref.shape[0]):
        lanes = slice(head * HD, (head + 1) * HD)
        key_feature = feature(k_ref[:, lanes].astype(jnp.float32))
        value_data = v_ref[:, lanes].astype(jnp.float32)
        o_ref[head, :HD, :] = jnp.dot(
            key_feature.T, value_data, precision=lax.Precision.HIGHEST,
            preferred_element_type=jnp.float32,
        )
        o_ref[head, HD:, :] = jnp.zeros((STATE_ROWS - HD, HD), jnp.float32)
        o_ref[head, HD : HD + 1, :] = jnp.sum(key_feature, axis=0, keepdims=True)


def local_deltas(keys, values):
    kv_heads = keys.shape[1] // HD
    return pl.pallas_call(
        delta_kernel,
        out_shape=jax.ShapeDtypeStruct((kv_heads, STATE_ROWS, HD), jnp.float32),
    )(keys, values)


def chip_states(keys, values, core, kv_group):
    total = local_deltas(keys, values)
    parts = lax.axis_size("head")
    keep = lax.dynamic_slice_in_dim(total, core * kv_group, kv_group)
    send = lax.dynamic_slice_in_dim(total, (1 - core) * kv_group, kv_group)
    total = keep + lax.ppermute(send, "head", [(p, p ^ 1) for p in range(parts)])
    steps = 2
    while steps < parts:
        total = total + lax.ppermute(total, "head", [(p, p ^ steps) for p in range(parts)])
        steps *= 2
    return total


def earlier_states(delta):
    count = lax.axis_size("seq")
    total = delta
    steps = 1
    while steps < count:
        total = total + shifted(total, "seq", steps)
        steps *= 2
    return total - delta


def online_step(q_ref, k_ref, v_ref, m_sc, l_sc, acc_sc, group_size, masked):
    block = q_ref.shape[0]
    score_scale = HD ** (-0.5)
    key_rows = k_ref[...]
    value_rows = jnp.concatenate([v_ref[...], jnp.ones((block, LANES), v_ref.dtype)], axis=1)
    if masked:
        rows = lax.broadcasted_iota(jnp.int32, (block, block), 0)
        cols = lax.broadcasted_iota(jnp.int32, (block, block), 1)
        allowed = cols <= rows
    for head in range(group_size):
        lanes = slice(head * HD, (head + 1) * HD)
        scores = lax.dot_general(
            q_ref[:, lanes], key_rows, (((1,), (1,)), ((), ())),
            preferred_element_type=jnp.float32,
        )
        if masked:
            scores = jnp.where(allowed, scores, -1e30)
        m_prev = m_sc[head]
        m_new = jnp.maximum(m_prev, jnp.max(scores, axis=-1, keepdims=True) * score_scale)
        probs = jnp.exp(scores * score_scale - m_new[:, :1])
        alpha = jnp.exp(m_prev - m_new)
        both = jnp.dot(probs.astype(jnp.bfloat16), value_rows, preferred_element_type=jnp.float32)
        l_sc[head] = alpha * l_sc[head] + both[:, HD:]
        acc_sc[:, lanes] = alpha * acc_sc[:, lanes] + both[:, :HD]
        m_sc[head] = m_new


def near_kernel(qs_ref, ks_ref, first_ref, diag_ref, q_keep, q_recv, k_keep, v_keep, k_recv,
                v_recv, acc_ref, ml_ref, m_sc, l_sc, acc_sc, *, group_size):
    step_at = pl.program_id(1)
    q_src = qs_ref[step_at]
    k_src = ks_ref[step_at]
    diag = diag_ref[step_at] == 1

    @pl.when(first_ref[step_at] == 1)
    def _init():
        m_sc[...] = jnp.full(m_sc.shape, -jnp.inf, jnp.float32)
        l_sc[...] = jnp.zeros(l_sc.shape, jnp.float32)
        acc_sc[...] = jnp.zeros(acc_sc.shape, jnp.float32)

    sources = ((q_keep, k_keep, v_keep), (q_recv, k_recv, v_recv))
    for q_at in range(2):
        for k_at in range(2):
            masked = q_at == k_at

            @pl.when((q_src == q_at) & (k_src == k_at) & (diag == masked))
            def _step():
                q_ref = sources[q_at][0]
                online_step(q_ref, sources[k_at][1], sources[k_at][2], m_sc, l_sc, acc_sc,
                            group_size, masked)

    @pl.when(diag)
    def _save():
        acc_ref[...] = acc_sc[...]
        lane = lax.broadcasted_iota(jnp.int32, ml_ref.shape, 1)
        packed = jnp.zeros(ml_ref.shape, jnp.float32)
        for head in range(group_size):
            packed = jnp.where(lane == head, m_sc[head], packed)
            packed = jnp.where(lane == group_size + head, l_sc[head], packed)
        ml_ref[...] = packed


def far_kernel(qp_ref, kp_ref, first_ref, last_ref, valid_ref, off_ref, gate_ref, q_keep, q_recv, k_ref,
               v_ref, s_ref, acc_in, ml_in, o_ref, m_sc, l_sc, acc_sc, *, group_size):
    kv_head = pl.program_id(0)
    step_at = pl.program_id(1)

    @pl.when(first_ref[step_at] == 1)
    def _init():
        packed = ml_in[...]
        for head in range(group_size):
            m_sc[head] = jnp.broadcast_to(packed[:, head : head + 1], m_sc.shape[1:])
            l_sc[head] = jnp.broadcast_to(
                packed[:, group_size + head : group_size + head + 1], l_sc.shape[1:]
            )
        acc_sc[...] = acc_in[...]

    for q_at, q_ref in enumerate((q_keep, q_recv)):
        chosen = qp_ref[step_at] == q_at

        @pl.when(chosen & (valid_ref[step_at] == 1))
        def _step():
            online_step(q_ref, k_ref, v_ref, m_sc, l_sc, acc_sc, group_size, False)

        @pl.when(chosen & (last_ref[step_at] == 1))
        def _last():
            finish(q_ref, s_ref, gate_ref, o_ref, acc_sc, l_sc, kv_head, group_size)


def finish(q_ref, s_ref, gate_ref, o_ref, acc_sc, l_sc, kv_head, group_size):
    memory = s_ref[:HD, :]
    normalizer = s_ref[HD : HD + 1, :]
    for head in range(group_size):
        lanes = slice(head * HD, (head + 1) * HD)
        local_part = acc_sc[:, lanes] / l_sc[head]
        query_feature = feature(q_ref[:, lanes].astype(jnp.float32))
        numerator = jnp.dot(
            query_feature, memory, precision=lax.Precision.HIGHEST,
            preferred_element_type=jnp.float32,
        )
        denominator = jnp.maximum(
            jnp.sum(query_feature * normalizer, axis=-1, keepdims=True), 1.0
        )
        mixing = gate_ref[kv_head * group_size + head]
        o_ref[:, lanes] = (
            mixing * (numerator / denominator) + (1.0 - mixing) * local_part
        ).astype(o_ref.dtype)


def near_tables(core):
    tables = np.array(
        [[[c, 1 ^ c, 1 ^ c], [c, c, 1 ^ c], [1, 1, 0], [1, 0, 1]] for c in range(2)], np.int32
    )
    return jnp.asarray(tables)[core]


def far_tables(chips, chip, core, source):
    per_block = max(1, 2 * (chips - 1))
    tables = np.zeros((chips, 2, 5, per_block), np.int32)
    for y in range(chips):
        for c in range(2):
            steps = []
            k_pos = 0
            for j in range(per_block):
                valid = int(j < 2 * y)
                if valid:
                    k_pos = 2 * (chips - 1 - y + j // 2) + ((j % 2) ^ c)
                steps.append((source, k_pos, int(j == 0), int(j == per_block - 1), valid))
            tables[y, c] = np.array(steps, np.int32).T
    return jnp.asarray(tables)[chip, core]


def attend(keep_q, recv_q, keep_kv, recv_kv, far_kv, state, mixing, chips, chip, core, group_size):
    block, q_cols = keep_q.shape
    kv_group = keep_kv.shape[-1] // (2 * HD)
    width = group_size * HD
    scratch = [
        pltpu.VMEM((group_size, block, LANES), jnp.float32),
        pltpu.VMEM((group_size, block, LANES), jnp.float32),
        pltpu.VMEM((block, width), jnp.float32),
    ]
    params = pltpu.CompilerParams(dimension_semantics=("arbitrary", "arbitrary"))
    near = near_tables(core)
    q_spec = pl.BlockSpec((block, width), lambda g, t, *_: (0, g))
    k_spec = pl.BlockSpec((block, HD), lambda g, t, *_: (0, g))
    v_spec = pl.BlockSpec((block, HD), lambda g, t, *_: (0, kv_group + g))
    near_spec = pltpu.PrefetchScalarGridSpec(
        num_scalar_prefetch=4,
        grid=(kv_group, near.shape[-1]),
        in_specs=[q_spec, q_spec, k_spec, v_spec, k_spec, v_spec],
        out_specs=[
            pl.BlockSpec((None, block, width), lambda g, t, qs, ks, f, d: (qs[t], 0, g)),
            pl.BlockSpec((None, None, block, LANES), lambda g, t, qs, ks, f, d: (g, qs[t], 0, 0)),
        ],
        scratch_shapes=scratch,
    )
    pair_flops = 4 * block * block * HD * group_size * kv_group
    pair_exps = block * block * group_size * kv_group
    acc, ml = pl.pallas_call(
        functools.partial(near_kernel, group_size=group_size),
        grid_spec=near_spec,
        cost_estimate=pl.CostEstimate(
            flops=3 * pair_flops, transcendentals=3 * pair_exps,
            bytes_accessed=int(keep_q.size * 12 + keep_kv.size * 4),
        ),
        out_shape=[
            jax.ShapeDtypeStruct((2, block, q_cols), jnp.float32),
            jax.ShapeDtypeStruct((kv_group, 2, block, LANES), jnp.float32),
        ],
        compiler_params=params,
    )(*[near[i] for i in range(4)], keep_q, recv_q, keep_kv, keep_kv, recv_kv, recv_kv)
    far_pairs = max(1, 2 * (chips - 1))

    def far_call(source, out_cols, col_offset):
        far = far_tables(chips, chip, core, source)
        offset = jnp.reshape(col_offset, (1,)).astype(jnp.int32)
        far_spec = pltpu.PrefetchScalarGridSpec(
            num_scalar_prefetch=6,
            grid=(kv_group, far.shape[-1]),
            in_specs=[
                pl.BlockSpec(memory_space=pltpu.SMEM),
                q_spec,
                q_spec,
                pl.BlockSpec((None, block, HD), lambda g, t, qp, kp, f, l, v, o: (kp[t], 0, g)),
                pl.BlockSpec(
                    (None, block, HD), lambda g, t, qp, kp, f, l, v, o: (kp[t], 0, kv_group + g)
                ),
                pl.BlockSpec((None, STATE_ROWS, HD), lambda g, t, qp, kp, f, l, v, o: (g, 0, 0)),
                pl.BlockSpec((None, block, width), lambda g, t, qp, kp, f, l, v, o: (qp[t], 0, g)),
                pl.BlockSpec(
                    (None, None, block, LANES), lambda g, t, qp, kp, f, l, v, o: (g, qp[t], 0, 0)
                ),
            ],
            out_specs=pl.BlockSpec((block, width), lambda g, t, qp, kp, f, l, v, o: (0, o[0] + g)),
            scratch_shapes=scratch,
        )
        return pl.pallas_call(
            functools.partial(far_kernel, group_size=group_size),
            grid_spec=far_spec,
            cost_estimate=pl.CostEstimate(
                flops=far_pairs * pair_flops // 2, transcendentals=far_pairs * pair_exps // 2,
                bytes_accessed=int(keep_q.size * 8 + far_kv.size * 2),
            ),
            out_shape=jax.ShapeDtypeStruct((block, out_cols), jnp.bfloat16),
            compiler_params=params,
        )(*[far[i] for i in range(5)], offset, mixing, keep_q, recv_q, far_kv, far_kv, state, acc, ml)

    sibling_part = far_call(1, q_cols, 0)
    back = lax.ppermute(sibling_part, "head", [(p, p ^ 1) for p in range(lax.axis_size("head"))])
    own_part = far_call(0, 2 * q_cols, core * kv_group)
    return own_part, back


def place_kernel(col_ref, full_ref, back_ref, o_ref):
    o_ref[...] = back_ref[...]


def place_back(own_part, back, core, kv_group):
    tokens_here, q_cols = back.shape
    width = q_cols // kv_group
    other = jnp.reshape((1 - core) * kv_group, (1,)).astype(jnp.int32)
    grid_spec = pltpu.PrefetchScalarGridSpec(
        num_scalar_prefetch=1,
        grid=(kv_group,),
        in_specs=[
            pl.BlockSpec(memory_space=pl.ANY),
            pl.BlockSpec((tokens_here, width), lambda g, c: (0, g)),
        ],
        out_specs=pl.BlockSpec((tokens_here, width), lambda g, c: (0, c[0] + g)),
    )
    return pl.pallas_call(
        place_kernel,
        grid_spec=grid_spec,
        out_shape=jax.ShapeDtypeStruct(own_part.shape, own_part.dtype),
        input_output_aliases={1: 0},
    )(other, own_part, back)


def body(queries, keys, values, gate_logit):
    parts = lax.axis_size("head")
    chips = parts // 2
    place = lax.axis_index("head")
    chip = place // 2
    core = place % 2
    k_cols = keys.shape[1] // 2
    kv_group = k_cols // HD
    group_size = queries.shape[1] // keys.shape[1]
    sibling = [(p, p ^ 1) for p in range(parts)]

    delta = chip_states(keys, values, core, kv_group)
    keep_q, keep_kv, send_q, send_kv = split_inputs(queries, keys, values, core)
    recv_q = lax.ppermute(send_q, "head", sibling)
    recv_kv = lax.ppermute(send_kv, "head", sibling)
    delta, keep_kv, send_kv, recv_q, recv_kv = lax.optimization_barrier(
        (delta, keep_kv, send_kv, recv_q, recv_kv)
    )
    state = earlier_states(delta)
    kv_parts = []
    for s in range(chips - 1, 0, -1):
        kv_parts.append(lax.ppermute(keep_kv, "head", [(p, p + 2 * s) for p in range(parts - 2 * s)]))
        kv_parts.append(
            lax.ppermute(send_kv, "head", [(p, (p + 2 * s) ^ 1) for p in range(parts - 2 * s)])
        )
    far_kv = jnp.stack(kv_parts) if kv_parts else jnp.stack([keep_kv, recv_kv])
    gate_here = lax.dynamic_slice_in_dim(gate_logit, core * kv_group * group_size, kv_group * group_size)
    mixing = jax.nn.sigmoid(gate_here)
    own_part, back = attend(
        keep_q, recv_q, keep_kv, recv_kv, far_kv, state, mixing, chips, chip, core, group_size
    )
    return place_back(own_part, back, core, kv_group)


def solution(mesh):
    in_specs = (P(("seq", "head"), None), P(("seq", "head"), None), P(("seq", "head"), None), P())
    out_specs = P(("seq", "head"), None)
    return jax.shard_map(body, mesh=mesh, in_specs=in_specs, out_specs=out_specs, check_vma=False)
```

```python
import functools

import jax
import jax.numpy as jnp
import numpy as np
from jax import lax
from jax.experimental import pallas as pl
from jax.experimental.pallas import tpu as pltpu
from jax.sharding import PartitionSpec as P

HQ = 32
KVH = 8
HD = 128
SEG = 2048
LANES = 128
STATE_ROWS = HD + 8


def feature(inputs):
    return jnp.where(inputs > 0, inputs + 1.0, jnp.exp(jnp.minimum(inputs, 0.0)))


def shifted(value, axis, steps):
    count = lax.axis_size(axis)
    return lax.ppermute(value, axis, [(source, source + steps) for source in range(count - steps)])


def split_kernel(core_ref, q_keep, k_keep, v_keep, q_send, k_send, v_send, *out_refs):
    k_cols = k_keep.shape[-1]
    keep_q, keep_kv, send_q, send_kv = out_refs
    keep_q[...] = q_keep[...]
    keep_kv[:, :k_cols] = k_keep[...]
    keep_kv[:, k_cols:] = v_keep[...]
    send_q[...] = q_send[...]
    send_kv[:, :k_cols] = k_send[...]
    send_kv[:, k_cols:] = v_send[...]


def split_inputs(queries, keys, values, core):
    tokens_here, q_all = queries.shape
    q_cols = q_all // 2
    k_cols = keys.shape[1] // 2
    keep_map = lambda i, c: (0, c[0])
    send_map = lambda i, c: (0, 1 - c[0])
    q_shape = jax.ShapeDtypeStruct((tokens_here, q_cols), queries.dtype)
    kv_shape = jax.ShapeDtypeStruct((tokens_here, 2 * k_cols), keys.dtype)
    grid_spec = pltpu.PrefetchScalarGridSpec(
        num_scalar_prefetch=1,
        grid=(1,),
        in_specs=[
            pl.BlockSpec((tokens_here, q_cols), keep_map),
            pl.BlockSpec((tokens_here, k_cols), keep_map),
            pl.BlockSpec((tokens_here, k_cols), keep_map),
            pl.BlockSpec((tokens_here, q_cols), send_map),
            pl.BlockSpec((tokens_here, k_cols), send_map),
            pl.BlockSpec((tokens_here, k_cols), send_map),
        ],
        out_specs=[
            pl.BlockSpec((tokens_here, q_cols), lambda i, c: (0, 0)),
            pl.BlockSpec((tokens_here, 2 * k_cols), lambda i, c: (0, 0)),
        ]
        * 2,
    )
    return pl.pallas_call(
        split_kernel, grid_spec=grid_spec, out_shape=[q_shape, kv_shape] * 2
    )(core.reshape(1), queries, keys, values, queries, keys, values)


def delta_kernel(k_ref, v_ref, o_ref):
    for head in range(o_ref.shape[0]):
        lanes = slice(head * HD, (head + 1) * HD)
        key_feature = feature(k_ref[:, lanes].astype(jnp.float32))
        value_data = v_ref[:, lanes].astype(jnp.float32)
        o_ref[head, :HD, :] = jnp.dot(
            key_feature.T, value_data, precision=lax.Precision.HIGHEST,
            preferred_element_type=jnp.float32,
        )
        o_ref[head, HD:, :] = jnp.zeros((STATE_ROWS - HD, HD), jnp.float32)
        o_ref[head, HD : HD + 1, :] = jnp.sum(key_feature, axis=0, keepdims=True)


def local_deltas(keys, values):
    kv_heads = keys.shape[1] // HD
    return pl.pallas_call(
        delta_kernel,
        out_shape=jax.ShapeDtypeStruct((kv_heads, STATE_ROWS, HD), jnp.float32),
    )(keys, values)


def chip_states(keys, values, core, kv_group):
    total = local_deltas(keys, values)
    parts = lax.axis_size("head")
    keep = lax.dynamic_slice_in_dim(total, core * kv_group, kv_group)
    send = lax.dynamic_slice_in_dim(total, (1 - core) * kv_group, kv_group)
    total = keep + lax.ppermute(send.astype(jnp.bfloat16), "head", [(p, p ^ 1) for p in range(parts)])
    steps = 2
    while steps < parts:
        across = lax.ppermute(total.astype(jnp.bfloat16), "head", [(p, p ^ steps) for p in range(parts)])
        total = total + across
        steps *= 2
    return total


def earlier_states(delta):
    count = lax.axis_size("seq")
    total = delta
    steps = 1
    while steps < count:
        total = total + shifted(total.astype(jnp.bfloat16), "seq", steps)
        steps *= 2
    return total - delta


def online_step(q_ref, k_ref, v_ref, m_sc, l_sc, acc_sc, group_size, masked):
    block = q_ref.shape[0]
    score_scale = HD ** (-0.5)
    key_rows = k_ref[...]
    value_rows = jnp.concatenate([v_ref[...], jnp.ones((block, LANES), v_ref.dtype)], axis=1)
    if masked:
        rows = lax.broadcasted_iota(jnp.int32, (block, block), 0)
        cols = lax.broadcasted_iota(jnp.int32, (block, block), 1)
        allowed = cols <= rows
    for head in range(group_size):
        lanes = slice(head * HD, (head + 1) * HD)
        scores = lax.dot_general(
            q_ref[:, lanes], key_rows, (((1,), (1,)), ((), ())),
            preferred_element_type=jnp.float32,
        )
        if masked:
            scores = jnp.where(allowed, scores, -1e30)
        m_prev = m_sc[head]
        m_new = jnp.maximum(m_prev, jnp.max(scores, axis=-1, keepdims=True) * score_scale)
        probs = jnp.exp(scores * score_scale - m_new[:, :1])
        alpha = jnp.exp(m_prev - m_new)
        both = jnp.dot(probs.astype(jnp.bfloat16), value_rows, preferred_element_type=jnp.float32)
        l_sc[head] = alpha * l_sc[head] + both[:, HD:]
        acc_sc[:, lanes] = alpha * acc_sc[:, lanes] + both[:, :HD]
        m_sc[head] = m_new


def near_kernel(qs_ref, ks_ref, first_ref, diag_ref, q_keep, q_recv, k_keep, v_keep, k_recv,
                v_recv, acc_ref, ml_ref, m_sc, l_sc, acc_sc, *, group_size):
    step_at = pl.program_id(1)
    q_src = qs_ref[step_at]
    k_src = ks_ref[step_at]
    diag = diag_ref[step_at] == 1

    @pl.when(first_ref[step_at] == 1)
    def _init():
        m_sc[...] = jnp.full(m_sc.shape, -jnp.inf, jnp.float32)
        l_sc[...] = jnp.zeros(l_sc.shape, jnp.float32)
        acc_sc[...] = jnp.zeros(acc_sc.shape, jnp.float32)

    sources = ((q_keep, k_keep, v_keep), (q_recv, k_recv, v_recv))
    for q_at in range(2):
        for k_at in range(2):
            masked = q_at == k_at

            @pl.when((q_src == q_at) & (k_src == k_at) & (diag == masked))
            def _step():
                q_ref = sources[q_at][0]
                online_step(q_ref, sources[k_at][1], sources[k_at][2], m_sc, l_sc, acc_sc,
                            group_size, masked)

    @pl.when(diag)
    def _save():
        acc_ref[...] = acc_sc[...]
        lane = lax.broadcasted_iota(jnp.int32, ml_ref.shape, 1)
        packed = jnp.zeros(ml_ref.shape, jnp.float32)
        for head in range(group_size):
            packed = jnp.where(lane == head, m_sc[head], packed)
            packed = jnp.where(lane == group_size + head, l_sc[head], packed)
        ml_ref[...] = packed


def far_kernel(qp_ref, kp_ref, first_ref, last_ref, valid_ref, off_ref, gate_ref, q_keep, q_recv, k_ref,
               v_ref, s_ref, acc_in, ml_in, o_ref, m_sc, l_sc, acc_sc, *, group_size):
    kv_head = pl.program_id(0)
    step_at = pl.program_id(1)

    @pl.when(first_ref[step_at] == 1)
    def _init():
        packed = ml_in[...]
        for head in range(group_size):
            m_sc[head] = jnp.broadcast_to(packed[:, head : head + 1], m_sc.shape[1:])
            l_sc[head] = jnp.broadcast_to(
                packed[:, group_size + head : group_size + head + 1], l_sc.shape[1:]
            )
        acc_sc[...] = acc_in[...]

    for q_at, q_ref in enumerate((q_keep, q_recv)):
        chosen = qp_ref[step_at] == q_at

        @pl.when(chosen & (valid_ref[step_at] == 1))
        def _step():
            online_step(q_ref, k_ref, v_ref, m_sc, l_sc, acc_sc, group_size, False)

        @pl.when(chosen & (last_ref[step_at] == 1))
        def _last():
            finish(q_ref, s_ref, gate_ref, o_ref, acc_sc, l_sc, kv_head, group_size)


def finish(q_ref, s_ref, gate_ref, o_ref, acc_sc, l_sc, kv_head, group_size):
    memory = s_ref[:HD, :]
    normalizer = s_ref[HD : HD + 1, :]
    for head in range(group_size):
        lanes = slice(head * HD, (head + 1) * HD)
        local_part = acc_sc[:, lanes] / l_sc[head]
        query_feature = feature(q_ref[:, lanes].astype(jnp.float32))
        numerator = jnp.dot(
            query_feature, memory, precision=lax.Precision.HIGHEST,
            preferred_element_type=jnp.float32,
        )
        denominator = jnp.maximum(
            jnp.sum(query_feature * normalizer, axis=-1, keepdims=True), 1.0
        )
        mixing = gate_ref[kv_head * group_size + head]
        o_ref[:, lanes] = (
            mixing * (numerator / denominator) + (1.0 - mixing) * local_part
        ).astype(o_ref.dtype)


def near_tables(core):
    tables = np.array(
        [[[c, 1 ^ c, 1 ^ c], [c, c, 1 ^ c], [1, 1, 0], [1, 0, 1]] for c in range(2)], np.int32
    )
    return jnp.asarray(tables)[core]


def far_tables(chips, chip, core, source):
    per_block = max(1, 2 * (chips - 1))
    tables = np.zeros((chips, 2, 5, per_block), np.int32)
    for y in range(chips):
        for c in range(2):
            steps = []
            k_pos = 0
            for j in range(per_block):
                valid = int(j < 2 * y)
                if valid:
                    k_pos = 2 * (chips - 1 - y + j // 2) + ((j % 2) ^ c)
                steps.append((source, k_pos, int(j == 0), int(j == per_block - 1), valid))
            tables[y, c] = np.array(steps, np.int32).T
    return jnp.asarray(tables)[chip, core]


def attend(keep_q, recv_q, keep_kv, recv_kv, far_kv, state, mixing, chips, chip, core, group_size):
    block, q_cols = keep_q.shape
    kv_group = keep_kv.shape[-1] // (2 * HD)
    width = group_size * HD
    scratch = [
        pltpu.VMEM((group_size, block, LANES), jnp.float32),
        pltpu.VMEM((group_size, block, LANES), jnp.float32),
        pltpu.VMEM((block, width), jnp.float32),
    ]
    params = pltpu.CompilerParams(dimension_semantics=("arbitrary", "arbitrary"))
    near = near_tables(core)
    q_spec = pl.BlockSpec((block, width), lambda g, t, *_: (0, g))
    k_spec = pl.BlockSpec((block, HD), lambda g, t, *_: (0, g))
    v_spec = pl.BlockSpec((block, HD), lambda g, t, *_: (0, kv_group + g))
    near_spec = pltpu.PrefetchScalarGridSpec(
        num_scalar_prefetch=4,
        grid=(kv_group, near.shape[-1]),
        in_specs=[q_spec, q_spec, k_spec, v_spec, k_spec, v_spec],
        out_specs=[
            pl.BlockSpec((None, block, width), lambda g, t, qs, ks, f, d: (qs[t], 0, g)),
            pl.BlockSpec((None, None, block, LANES), lambda g, t, qs, ks, f, d: (g, qs[t], 0, 0)),
        ],
        scratch_shapes=scratch,
    )
    pair_flops = 4 * block * block * HD * group_size * kv_group
    pair_exps = block * block * group_size * kv_group
    acc, ml = pl.pallas_call(
        functools.partial(near_kernel, group_size=group_size),
        grid_spec=near_spec,
        cost_estimate=pl.CostEstimate(
            flops=3 * pair_flops, transcendentals=3 * pair_exps,
            bytes_accessed=int(keep_q.size * 12 + keep_kv.size * 4),
        ),
        out_shape=[
            jax.ShapeDtypeStruct((2, block, q_cols), jnp.float32),
            jax.ShapeDtypeStruct((kv_group, 2, block, LANES), jnp.float32),
        ],
        compiler_params=params,
    )(*[near[i] for i in range(4)], keep_q, recv_q, keep_kv, keep_kv, recv_kv, recv_kv)
    far_pairs = max(1, 2 * (chips - 1))

    def far_call(source, out_cols, col_offset):
        far = far_tables(chips, chip, core, source)
        offset = jnp.reshape(col_offset, (1,)).astype(jnp.int32)
        far_spec = pltpu.PrefetchScalarGridSpec(
            num_scalar_prefetch=6,
            grid=(kv_group, far.shape[-1]),
            in_specs=[
                pl.BlockSpec(memory_space=pltpu.SMEM),
                q_spec,
                q_spec,
                pl.BlockSpec((None, block, HD), lambda g, t, qp, kp, f, l, v, o: (kp[t], 0, g)),
                pl.BlockSpec(
                    (None, block, HD), lambda g, t, qp, kp, f, l, v, o: (kp[t], 0, kv_group + g)
                ),
                pl.BlockSpec((None, STATE_ROWS, HD), lambda g, t, qp, kp, f, l, v, o: (g, 0, 0)),
                pl.BlockSpec((None, block, width), lambda g, t, qp, kp, f, l, v, o: (qp[t], 0, g)),
                pl.BlockSpec(
                    (None, None, block, LANES), lambda g, t, qp, kp, f, l, v, o: (g, qp[t], 0, 0)
                ),
            ],
            out_specs=pl.BlockSpec((block, width), lambda g, t, qp, kp, f, l, v, o: (0, o[0] + g)),
            scratch_shapes=scratch,
        )
        return pl.pallas_call(
            functools.partial(far_kernel, group_size=group_size),
            grid_spec=far_spec,
            cost_estimate=pl.CostEstimate(
                flops=far_pairs * pair_flops // 2, transcendentals=far_pairs * pair_exps // 2,
                bytes_accessed=int(keep_q.size * 8 + far_kv.size * 2),
            ),
            out_shape=jax.ShapeDtypeStruct((block, out_cols), jnp.bfloat16),
            compiler_params=params,
        )(*[far[i] for i in range(5)], offset, mixing, keep_q, recv_q, far_kv, far_kv, state, acc, ml)

    sibling_part = far_call(1, q_cols, 0)
    back = lax.ppermute(sibling_part, "head", [(p, p ^ 1) for p in range(lax.axis_size("head"))])
    own_part = far_call(0, 2 * q_cols, core * kv_group)
    return own_part, back


def place_kernel(col_ref, full_ref, back_ref, o_ref):
    o_ref[...] = back_ref[...]


def place_back(own_part, back, core, kv_group):
    tokens_here, q_cols = back.shape
    width = q_cols // kv_group
    other = jnp.reshape((1 - core) * kv_group, (1,)).astype(jnp.int32)
    grid_spec = pltpu.PrefetchScalarGridSpec(
        num_scalar_prefetch=1,
        grid=(kv_group,),
        in_specs=[
            pl.BlockSpec(memory_space=pl.ANY),
            pl.BlockSpec((tokens_here, width), lambda g, c: (0, g)),
        ],
        out_specs=pl.BlockSpec((tokens_here, width), lambda g, c: (0, c[0] + g)),
    )
    return pl.pallas_call(
        place_kernel,
        grid_spec=grid_spec,
        out_shape=jax.ShapeDtypeStruct(own_part.shape, own_part.dtype),
        input_output_aliases={1: 0},
    )(other, own_part, back)


def body(queries, keys, values, gate_logit):
    parts = lax.axis_size("head")
    chips = parts // 2
    place = lax.axis_index("head")
    chip = place // 2
    core = place % 2
    k_cols = keys.shape[1] // 2
    kv_group = k_cols // HD
    group_size = queries.shape[1] // keys.shape[1]
    sibling = [(p, p ^ 1) for p in range(parts)]

    delta = chip_states(keys, values, core, kv_group)
    keep_q, keep_kv, send_q, send_kv = split_inputs(queries, keys, values, core)
    recv_q = lax.ppermute(send_q, "head", sibling)
    recv_kv = lax.ppermute(send_kv, "head", sibling)
    delta, keep_kv, send_kv, recv_q, recv_kv = lax.optimization_barrier(
        (delta, keep_kv, send_kv, recv_q, recv_kv)
    )
    state = earlier_states(delta)
    kv_parts = []
    for s in range(chips - 1, 0, -1):
        kv_parts.append(lax.ppermute(keep_kv, "head", [(p, p + 2 * s) for p in range(parts - 2 * s)]))
        kv_parts.append(
            lax.ppermute(send_kv, "head", [(p, (p + 2 * s) ^ 1) for p in range(parts - 2 * s)])
        )
    far_kv = jnp.stack(kv_parts) if kv_parts else jnp.stack([keep_kv, recv_kv])
    gate_here = lax.dynamic_slice_in_dim(gate_logit, core * kv_group * group_size, kv_group * group_size)
    mixing = jax.nn.sigmoid(gate_here)
    own_part, back = attend(
        keep_q, recv_q, keep_kv, recv_kv, far_kv, state, mixing, chips, chip, core, group_size
    )
    return place_back(own_part, back, core, kv_group)


def solution(mesh):
    in_specs = (P(("seq", "head"), None), P(("seq", "head"), None), P(("seq", "head"), None), P())
    out_specs = P(("seq", "head"), None)
    return jax.shard_map(body, mesh=mesh, in_specs=in_specs, out_specs=out_specs, check_vma=False)
```

```python
import functools

import jax
import jax.numpy as jnp
import numpy as np
from jax import lax
from jax.experimental import pallas as pl
from jax.experimental.pallas import tpu as pltpu
from jax.sharding import PartitionSpec as P

HQ = 32
KVH = 8
HD = 128
SEG = 2048
LANES = 128
STATE_ROWS = HD + 8


def feature(inputs):
    return jnp.where(inputs > 0, inputs + 1.0, jnp.exp(jnp.minimum(inputs, 0.0)))


def shifted(value, axis, steps):
    count = lax.axis_size(axis)
    return lax.ppermute(value, axis, [(source, source + steps) for source in range(count - steps)])


def split_kernel(core_ref, q_keep, k_keep, v_keep, q_send, k_send, v_send, *out_refs):
    k_cols = k_keep.shape[-1]
    keep_q, keep_kv, send_q, send_kv = out_refs
    keep_q[...] = q_keep[...]
    keep_kv[:, :k_cols] = k_keep[...]
    keep_kv[:, k_cols:] = v_keep[...]
    send_q[...] = q_send[...]
    send_kv[:, :k_cols] = k_send[...]
    send_kv[:, k_cols:] = v_send[...]


def split_inputs(queries, keys, values, core):
    tokens_here, q_all = queries.shape
    q_cols = q_all // 2
    k_cols = keys.shape[1] // 2
    keep_map = lambda i, c: (0, c[0])
    send_map = lambda i, c: (0, 1 - c[0])
    q_shape = jax.ShapeDtypeStruct((tokens_here, q_cols), queries.dtype)
    kv_shape = jax.ShapeDtypeStruct((tokens_here, 2 * k_cols), keys.dtype)
    grid_spec = pltpu.PrefetchScalarGridSpec(
        num_scalar_prefetch=1,
        grid=(1,),
        in_specs=[
            pl.BlockSpec((tokens_here, q_cols), keep_map),
            pl.BlockSpec((tokens_here, k_cols), keep_map),
            pl.BlockSpec((tokens_here, k_cols), keep_map),
            pl.BlockSpec((tokens_here, q_cols), send_map),
            pl.BlockSpec((tokens_here, k_cols), send_map),
            pl.BlockSpec((tokens_here, k_cols), send_map),
        ],
        out_specs=[
            pl.BlockSpec((tokens_here, q_cols), lambda i, c: (0, 0)),
            pl.BlockSpec((tokens_here, 2 * k_cols), lambda i, c: (0, 0)),
        ]
        * 2,
    )
    return pl.pallas_call(
        split_kernel, grid_spec=grid_spec, out_shape=[q_shape, kv_shape] * 2
    )(core.reshape(1), queries, keys, values, queries, keys, values)


def delta_kernel(k_ref, v_ref, o_ref):
    for head in range(o_ref.shape[0]):
        lanes = slice(head * HD, (head + 1) * HD)
        key_feature = feature(k_ref[:, lanes].astype(jnp.float32))
        value_data = v_ref[:, lanes].astype(jnp.float32)
        o_ref[head, :HD, :] = jnp.dot(
            key_feature.T, value_data, precision=lax.Precision.HIGHEST,
            preferred_element_type=jnp.float32,
        )
        o_ref[head, HD:, :] = jnp.zeros((STATE_ROWS - HD, HD), jnp.float32)
        o_ref[head, HD : HD + 1, :] = jnp.sum(key_feature, axis=0, keepdims=True)


def local_deltas(keys, values):
    kv_heads = keys.shape[1] // HD
    return pl.pallas_call(
        delta_kernel,
        out_shape=jax.ShapeDtypeStruct((kv_heads, STATE_ROWS, HD), jnp.float32),
    )(keys, values)


def chip_states(keys, values, core, kv_group):
    total = local_deltas(keys, values)
    parts = lax.axis_size("head")
    keep = lax.dynamic_slice_in_dim(total, core * kv_group, kv_group)
    send = lax.dynamic_slice_in_dim(total, (1 - core) * kv_group, kv_group)
    total = keep + lax.ppermute(send.astype(jnp.bfloat16), "head", [(p, p ^ 1) for p in range(parts)])
    steps = 2
    while steps < parts:
        across = lax.ppermute(total.astype(jnp.bfloat16), "head", [(p, p ^ steps) for p in range(parts)])
        total = total + across
        steps *= 2
    return total


def earlier_states(delta):
    count = lax.axis_size("seq")
    total = delta
    steps = 1
    while steps < count:
        total = total + shifted(total.astype(jnp.bfloat16), "seq", steps)
        steps *= 2
    return total - delta


def online_step(q_ref, k_ref, v_ref, m_sc, l_sc, acc_sc, group_size, masked):
    block = q_ref.shape[0]
    score_scale = HD ** (-0.5)
    key_rows = k_ref[...]
    value_rows = jnp.concatenate([v_ref[...], jnp.ones((block, LANES), v_ref.dtype)], axis=1)
    if masked:
        rows = lax.broadcasted_iota(jnp.int32, (block, block), 0)
        cols = lax.broadcasted_iota(jnp.int32, (block, block), 1)
        allowed = cols <= rows
    for head in range(group_size):
        lanes = slice(head * HD, (head + 1) * HD)
        scores = lax.dot_general(
            q_ref[:, lanes], key_rows, (((1,), (1,)), ((), ())),
            preferred_element_type=jnp.float32,
        )
        if masked:
            scores = jnp.where(allowed, scores, -1e30)
        m_prev = m_sc[head]
        m_new = jnp.maximum(m_prev, jnp.max(scores, axis=-1, keepdims=True) * score_scale)
        probs = jnp.exp(scores * score_scale - m_new[:, :1])
        alpha = jnp.exp(m_prev - m_new)
        both = jnp.dot(probs.astype(jnp.bfloat16), value_rows, preferred_element_type=jnp.float32)
        l_sc[head] = alpha * l_sc[head] + both[:, HD:]
        acc_sc[:, lanes] = alpha * acc_sc[:, lanes] + both[:, :HD]
        m_sc[head] = m_new


def near_kernel(qs_ref, ks_ref, first_ref, diag_ref, q_keep, q_recv, k_keep, v_keep, k_recv,
                v_recv, acc_ref, ml_ref, m_sc, l_sc, acc_sc, *, group_size):
    step_at = pl.program_id(1)
    q_src = qs_ref[step_at]
    k_src = ks_ref[step_at]
    diag = diag_ref[step_at] == 1

    @pl.when(first_ref[step_at] == 1)
    def _init():
        m_sc[...] = jnp.full(m_sc.shape, -jnp.inf, jnp.float32)
        l_sc[...] = jnp.zeros(l_sc.shape, jnp.float32)
        acc_sc[...] = jnp.zeros(acc_sc.shape, jnp.float32)

    sources = ((q_keep, k_keep, v_keep), (q_recv, k_recv, v_recv))
    for q_at in range(2):
        for k_at in range(2):
            masked = q_at == k_at

            @pl.when((q_src == q_at) & (k_src == k_at) & (diag == masked))
            def _step():
                q_ref = sources[q_at][0]
                online_step(q_ref, sources[k_at][1], sources[k_at][2], m_sc, l_sc, acc_sc,
                            group_size, masked)

    @pl.when(diag)
    def _save():
        acc_ref[...] = acc_sc[...]
        lane = lax.broadcasted_iota(jnp.int32, ml_ref.shape, 1)
        packed = jnp.zeros(ml_ref.shape, jnp.float32)
        for head in range(group_size):
            packed = jnp.where(lane == head, m_sc[head], packed)
            packed = jnp.where(lane == group_size + head, l_sc[head], packed)
        ml_ref[...] = packed


def far_kernel(qp_ref, kp_ref, first_ref, last_ref, valid_ref, off_ref, gate_ref, q_ref, *refs,
               group_size):
    kv_refs = refs[:-7]
    s_ref, acc_in, ml_in, o_ref, m_sc, l_sc, acc_sc = refs[-7:]
    kv_head = pl.program_id(0)
    step_at = pl.program_id(1)

    @pl.when(first_ref[step_at] == 1)
    def _init():
        packed = ml_in[...]
        for head in range(group_size):
            m_sc[head] = jnp.broadcast_to(packed[:, head : head + 1], m_sc.shape[1:])
            l_sc[head] = jnp.broadcast_to(
                packed[:, group_size + head : group_size + head + 1], l_sc.shape[1:]
            )
        acc_sc[...] = acc_in[...]

    for part in range(len(kv_refs) // 2):
        @pl.when((kp_ref[step_at] == part) & (valid_ref[step_at] == 1))
        def _step():
            online_step(q_ref, kv_refs[2 * part], kv_refs[2 * part + 1], m_sc, l_sc, acc_sc,
                        group_size, False)

    @pl.when(last_ref[step_at] == 1)
    def _last():
        finish(q_ref, s_ref, gate_ref, o_ref, acc_sc, l_sc, kv_head, group_size)


def finish(q_ref, s_ref, gate_ref, o_ref, acc_sc, l_sc, kv_head, group_size):
    memory = s_ref[:HD, :]
    normalizer = s_ref[HD : HD + 1, :]
    for head in range(group_size):
        lanes = slice(head * HD, (head + 1) * HD)
        local_part = acc_sc[:, lanes] / l_sc[head]
        query_feature = feature(q_ref[:, lanes].astype(jnp.float32))
        numerator = jnp.dot(
            query_feature, memory, precision=lax.Precision.HIGHEST,
            preferred_element_type=jnp.float32,
        )
        denominator = jnp.maximum(
            jnp.sum(query_feature * normalizer, axis=-1, keepdims=True), 1.0
        )
        mixing = gate_ref[kv_head * group_size + head]
        o_ref[:, lanes] = (
            mixing * (numerator / denominator) + (1.0 - mixing) * local_part
        ).astype(o_ref.dtype)


def near_tables(core):
    tables = np.array(
        [[[c, 1 ^ c, 1 ^ c], [c, c, 1 ^ c], [1, 1, 0], [1, 0, 1]] for c in range(2)], np.int32
    )
    return jnp.asarray(tables)[core]


def far_tables(chips, chip, core, source):
    per_block = max(1, 2 * (chips - 1))
    tables = np.zeros((chips, 2, 5, per_block), np.int32)
    for y in range(chips):
        for c in range(2):
            steps = []
            k_pos = 0
            for j in range(per_block):
                valid = int(j < 2 * y)
                if valid:
                    k_pos = 2 * (chips - 1 - y + j // 2) + ((j % 2) ^ c)
                steps.append((source, k_pos, int(j == 0), int(j == per_block - 1), valid))
            tables[y, c] = np.array(steps, np.int32).T
    return jnp.asarray(tables)[chip, core]


def attend(keep_q, recv_q, keep_kv, recv_kv, far_kv, state, mixing, chips, chip, core, group_size):
    block, q_cols = keep_q.shape
    kv_group = keep_kv.shape[-1] // (2 * HD)
    width = group_size * HD
    scratch = [
        pltpu.VMEM((group_size, block, LANES), jnp.float32),
        pltpu.VMEM((group_size, block, LANES), jnp.float32),
        pltpu.VMEM((block, width), jnp.float32),
    ]
    params = pltpu.CompilerParams(dimension_semantics=("arbitrary", "arbitrary"))
    near = near_tables(core)
    q_spec = pl.BlockSpec((block, width), lambda g, t, *_: (0, g))
    k_spec = pl.BlockSpec((block, HD), lambda g, t, *_: (0, g))
    v_spec = pl.BlockSpec((block, HD), lambda g, t, *_: (0, kv_group + g))
    near_spec = pltpu.PrefetchScalarGridSpec(
        num_scalar_prefetch=4,
        grid=(kv_group, near.shape[-1]),
        in_specs=[q_spec, q_spec, k_spec, v_spec, k_spec, v_spec],
        out_specs=[
            pl.BlockSpec((None, block, width), lambda g, t, qs, ks, f, d: (qs[t], 0, g)),
            pl.BlockSpec((None, None, block, LANES), lambda g, t, qs, ks, f, d: (g, qs[t], 0, 0)),
        ],
        scratch_shapes=scratch,
    )
    pair_flops = 4 * block * block * HD * group_size * kv_group
    pair_exps = block * block * group_size * kv_group
    acc, ml = pl.pallas_call(
        functools.partial(near_kernel, group_size=group_size),
        grid_spec=near_spec,
        cost_estimate=pl.CostEstimate(
            flops=3 * pair_flops, transcendentals=3 * pair_exps,
            bytes_accessed=int(keep_q.size * 12 + keep_kv.size * 4),
        ),
        out_shape=[
            jax.ShapeDtypeStruct((2, block, q_cols), jnp.float32),
            jax.ShapeDtypeStruct((kv_group, 2, block, LANES), jnp.float32),
        ],
        compiler_params=params,
    )(*[near[i] for i in range(4)], keep_q, recv_q, keep_kv, keep_kv, recv_kv, recv_kv)
    far_pairs = max(1, 2 * (chips - 1))

    def far_call(source, out_cols, col_offset):
        far = far_tables(chips, chip, core, source)
        offset = jnp.reshape(col_offset, (1,)).astype(jnp.int32)
        part_specs = []
        for _ in far_kv:
            part_specs += [k_spec, v_spec]
        far_spec = pltpu.PrefetchScalarGridSpec(
            num_scalar_prefetch=6,
            grid=(kv_group, far.shape[-1]),
            in_specs=[pl.BlockSpec(memory_space=pltpu.SMEM), q_spec]
            + part_specs
            + [
                pl.BlockSpec((None, STATE_ROWS, HD), lambda g, t, qp, kp, f, l, v, o: (g, 0, 0)),
                pl.BlockSpec((None, block, width), lambda g, t, qp, kp, f, l, v, o: (qp[t], 0, g)),
                pl.BlockSpec(
                    (None, None, block, LANES), lambda g, t, qp, kp, f, l, v, o: (g, qp[t], 0, 0)
                ),
            ],
            out_specs=pl.BlockSpec((block, width), lambda g, t, qp, kp, f, l, v, o: (0, o[0] + g)),
            scratch_shapes=scratch,
        )
        kv_args = []
        for part in far_kv:
            kv_args += [part, part]
        return pl.pallas_call(
            functools.partial(far_kernel, group_size=group_size),
            grid_spec=far_spec,
            cost_estimate=pl.CostEstimate(
                flops=far_pairs * pair_flops // 2, transcendentals=far_pairs * pair_exps // 2,
                bytes_accessed=int(keep_q.size * 8 + keep_kv.size * 2 * len(far_kv)),
            ),
            out_shape=jax.ShapeDtypeStruct((block, out_cols), jnp.bfloat16),
            compiler_params=params,
        )(*[far[i] for i in range(5)], offset, mixing, (keep_q, recv_q)[source], *kv_args, state,
          acc, ml)

    sibling_part = far_call(1, q_cols, 0)
    back = lax.ppermute(sibling_part, "head", [(p, p ^ 1) for p in range(lax.axis_size("head"))])
    own_part = far_call(0, 2 * q_cols, core * kv_group)
    return own_part, back


def place_kernel(col_ref, full_ref, back_ref, o_ref):
    o_ref[...] = back_ref[...]


def place_back(own_part, back, core, kv_group):
    tokens_here, q_cols = back.shape
    width = q_cols // kv_group
    other = jnp.reshape((1 - core) * kv_group, (1,)).astype(jnp.int32)
    grid_spec = pltpu.PrefetchScalarGridSpec(
        num_scalar_prefetch=1,
        grid=(kv_group,),
        in_specs=[
            pl.BlockSpec(memory_space=pl.ANY),
            pl.BlockSpec((tokens_here, width), lambda g, c: (0, g)),
        ],
        out_specs=pl.BlockSpec((tokens_here, width), lambda g, c: (0, c[0] + g)),
    )
    return pl.pallas_call(
        place_kernel,
        grid_spec=grid_spec,
        out_shape=jax.ShapeDtypeStruct(own_part.shape, own_part.dtype),
        input_output_aliases={1: 0},
    )(other, own_part, back)


def body(queries, keys, values, gate_logit):
    parts = lax.axis_size("head")
    chips = parts // 2
    place = lax.axis_index("head")
    chip = place // 2
    core = place % 2
    k_cols = keys.shape[1] // 2
    kv_group = k_cols // HD
    group_size = queries.shape[1] // keys.shape[1]
    sibling = [(p, p ^ 1) for p in range(parts)]

    delta = chip_states(keys, values, core, kv_group)
    keep_q, keep_kv, send_q, send_kv = split_inputs(queries, keys, values, core)
    recv_q = lax.ppermute(send_q, "head", sibling)
    recv_kv = lax.ppermute(send_kv, "head", sibling)
    delta, keep_kv, send_kv, recv_q, recv_kv = lax.optimization_barrier(
        (delta, keep_kv, send_kv, recv_q, recv_kv)
    )
    state = earlier_states(delta)
    kv_parts = []
    for s in range(chips - 1, 0, -1):
        kv_parts.append(lax.ppermute(keep_kv, "head", [(p, p + 2 * s) for p in range(parts - 2 * s)]))
        kv_parts.append(
            lax.ppermute(send_kv, "head", [(p, (p + 2 * s) ^ 1) for p in range(parts - 2 * s)])
        )
    far_kv = kv_parts if kv_parts else [keep_kv, recv_kv]
    gate_here = lax.dynamic_slice_in_dim(gate_logit, core * kv_group * group_size, kv_group * group_size)
    mixing = jax.nn.sigmoid(gate_here)
    own_part, back = attend(
        keep_q, recv_q, keep_kv, recv_kv, far_kv, state, mixing, chips, chip, core, group_size
    )
    return place_back(own_part, back, core, kv_group)


def solution(mesh):
    in_specs = (P(("seq", "head"), None), P(("seq", "head"), None), P(("seq", "head"), None), P())
    out_specs = P(("seq", "head"), None)
    return jax.shard_map(body, mesh=mesh, in_specs=in_specs, out_specs=out_specs, check_vma=False)
```

```python
import functools

import jax
import jax.numpy as jnp
import numpy as np
from jax import lax
from jax.experimental import pallas as pl
from jax.experimental.pallas import tpu as pltpu
from jax.sharding import PartitionSpec as P

HQ = 32
KVH = 8
HD = 128
SEG = 2048
LANES = 128
STATE_ROWS = HD + 8


def feature(inputs):
    return jnp.where(inputs > 0, inputs + 1.0, jnp.exp(jnp.minimum(inputs, 0.0)))


def shifted(value, axis, steps):
    count = lax.axis_size(axis)
    return lax.ppermute(value, axis, [(source, source + steps) for source in range(count - steps)])


def split_kernel(core_ref, q_keep, k_keep, v_keep, q_send, k_send, v_send, *out_refs):
    k_cols = k_keep.shape[-1]
    keep_q, keep_kv, send_q, send_kv = out_refs
    keep_q[...] = q_keep[...]
    keep_kv[:, :k_cols] = k_keep[...]
    keep_kv[:, k_cols:] = v_keep[...]
    send_q[...] = q_send[...]
    send_kv[:, :k_cols] = k_send[...]
    send_kv[:, k_cols:] = v_send[...]


def split_inputs(queries, keys, values, core):
    tokens_here, q_all = queries.shape
    q_cols = q_all // 2
    k_cols = keys.shape[1] // 2
    keep_map = lambda i, c: (0, c[0])
    send_map = lambda i, c: (0, 1 - c[0])
    q_shape = jax.ShapeDtypeStruct((tokens_here, q_cols), queries.dtype)
    kv_shape = jax.ShapeDtypeStruct((tokens_here, 2 * k_cols), keys.dtype)
    grid_spec = pltpu.PrefetchScalarGridSpec(
        num_scalar_prefetch=1,
        grid=(1,),
        in_specs=[
            pl.BlockSpec((tokens_here, q_cols), keep_map),
            pl.BlockSpec((tokens_here, k_cols), keep_map),
            pl.BlockSpec((tokens_here, k_cols), keep_map),
            pl.BlockSpec((tokens_here, q_cols), send_map),
            pl.BlockSpec((tokens_here, k_cols), send_map),
            pl.BlockSpec((tokens_here, k_cols), send_map),
        ],
        out_specs=[
            pl.BlockSpec((tokens_here, q_cols), lambda i, c: (0, 0)),
            pl.BlockSpec((tokens_here, 2 * k_cols), lambda i, c: (0, 0)),
        ]
        * 2,
    )
    return pl.pallas_call(
        split_kernel, grid_spec=grid_spec, out_shape=[q_shape, kv_shape] * 2
    )(core.reshape(1), queries, keys, values, queries, keys, values)


def delta_kernel(k_ref, v_ref, o_ref):
    for head in range(o_ref.shape[0]):
        lanes = slice(head * HD, (head + 1) * HD)
        key_feature = feature(k_ref[:, lanes].astype(jnp.float32))
        value_data = v_ref[:, lanes].astype(jnp.float32)
        o_ref[head, :HD, :] = jnp.dot(
            key_feature.T, value_data, precision=lax.Precision.HIGHEST,
            preferred_element_type=jnp.float32,
        )
        o_ref[head, HD:, :] = jnp.zeros((STATE_ROWS - HD, HD), jnp.float32)
        o_ref[head, HD : HD + 1, :] = jnp.sum(key_feature, axis=0, keepdims=True)


def local_deltas(keys, values):
    kv_heads = keys.shape[1] // HD
    return pl.pallas_call(
        delta_kernel,
        out_shape=jax.ShapeDtypeStruct((kv_heads, STATE_ROWS, HD), jnp.float32),
    )(keys, values)


def chip_states(keys, values, core, kv_group):
    total = local_deltas(keys, values)
    parts = lax.axis_size("head")
    keep = lax.dynamic_slice_in_dim(total, core * kv_group, kv_group)
    send = lax.dynamic_slice_in_dim(total, (1 - core) * kv_group, kv_group)
    total = keep + lax.ppermute(send.astype(jnp.bfloat16), "head", [(p, p ^ 1) for p in range(parts)])
    steps = 2
    while steps < parts:
        across = lax.ppermute(total.astype(jnp.bfloat16), "head", [(p, p ^ steps) for p in range(parts)])
        total = total + across
        steps *= 2
    return total


def earlier_states(delta):
    count = lax.axis_size("seq")
    total = delta
    steps = 1
    while steps < count:
        total = total + shifted(total.astype(jnp.bfloat16), "seq", steps)
        steps *= 2
    return total - delta


def online_step(q_ref, k_ref, v_ref, m_sc, l_sc, acc_sc, group_size, masked):
    block = q_ref.shape[0]
    score_scale = HD ** (-0.5)
    key_rows = k_ref[...]
    value_rows = jnp.concatenate([v_ref[...], jnp.ones((block, LANES), v_ref.dtype)], axis=1)
    if masked:
        rows = lax.broadcasted_iota(jnp.int32, (block, block), 0)
        cols = lax.broadcasted_iota(jnp.int32, (block, block), 1)
        allowed = cols <= rows
    for head in range(group_size):
        lanes = slice(head * HD, (head + 1) * HD)
        scores = lax.dot_general(
            q_ref[:, lanes], key_rows, (((1,), (1,)), ((), ())),
            preferred_element_type=jnp.float32,
        )
        if masked:
            scores = jnp.where(allowed, scores, -1e30)
        m_prev = m_sc[head]
        m_new = jnp.maximum(m_prev, jnp.max(scores, axis=-1, keepdims=True) * score_scale)
        probs = jnp.exp(scores * score_scale - m_new[:, :1])
        alpha = jnp.exp(m_prev - m_new)
        both = jnp.dot(probs.astype(jnp.bfloat16), value_rows, preferred_element_type=jnp.float32)
        l_sc[head] = alpha * l_sc[head] + both[:, HD:]
        acc_sc[:, lanes] = alpha * acc_sc[:, lanes] + both[:, :HD]
        m_sc[head] = m_new


def near_kernel(qs_ref, ks_ref, first_ref, diag_ref, q_keep, q_recv, k_keep, v_keep, k_recv,
                v_recv, acc_ref, ml_ref, m_sc, l_sc, acc_sc, *, group_size):
    step_at = pl.program_id(1)
    q_src = qs_ref[step_at]
    k_src = ks_ref[step_at]
    diag = diag_ref[step_at] == 1

    @pl.when(first_ref[step_at] == 1)
    def _init():
        m_sc[...] = jnp.full(m_sc.shape, -jnp.inf, jnp.float32)
        l_sc[...] = jnp.zeros(l_sc.shape, jnp.float32)
        acc_sc[...] = jnp.zeros(acc_sc.shape, jnp.float32)

    sources = ((q_keep, k_keep, v_keep), (q_recv, k_recv, v_recv))
    for q_at in range(2):
        for k_at in range(2):
            masked = q_at == k_at

            @pl.when((q_src == q_at) & (k_src == k_at) & (diag == masked))
            def _step():
                q_ref = sources[q_at][0]
                online_step(q_ref, sources[k_at][1], sources[k_at][2], m_sc, l_sc, acc_sc,
                            group_size, masked)

    @pl.when(diag)
    def _save():
        acc_ref[...] = acc_sc[...]
        lane = lax.broadcasted_iota(jnp.int32, ml_ref.shape, 1)
        packed = jnp.zeros(ml_ref.shape, jnp.float32)
        for head in range(group_size):
            packed = jnp.where(lane == head, m_sc[head], packed)
            packed = jnp.where(lane == group_size + head, l_sc[head], packed)
        ml_ref[...] = packed


def far_kernel(qp_ref, kp_ref, first_ref, last_ref, valid_ref, off_ref, gate_ref, q_ref, *refs,
               group_size):
    kv_refs = refs[:-7]
    s_ref, acc_in, ml_in, o_ref, m_sc, l_sc, acc_sc = refs[-7:]
    kv_head = pl.program_id(0)
    step_at = pl.program_id(1)

    @pl.when(first_ref[step_at] == 1)
    def _init():
        packed = ml_in[...]
        for head in range(group_size):
            m_sc[head] = jnp.broadcast_to(packed[:, head : head + 1], m_sc.shape[1:])
            l_sc[head] = jnp.broadcast_to(
                packed[:, group_size + head : group_size + head + 1], l_sc.shape[1:]
            )
        acc_sc[...] = acc_in[...]

    for part in range(len(kv_refs) // 2):
        @pl.when((kp_ref[step_at] == part) & (valid_ref[step_at] == 1))
        def _step():
            online_step(q_ref, kv_refs[2 * part], kv_refs[2 * part + 1], m_sc, l_sc, acc_sc,
                        group_size, False)

    @pl.when(last_ref[step_at] == 1)
    def _last():
        finish(q_ref, s_ref, gate_ref, o_ref, acc_sc, l_sc, kv_head, group_size)


def finish(q_ref, s_ref, gate_ref, o_ref, acc_sc, l_sc, kv_head, group_size):
    memory = s_ref[:HD, :]
    normalizer = s_ref[HD : HD + 1, :]
    for head in range(group_size):
        lanes = slice(head * HD, (head + 1) * HD)
        local_part = acc_sc[:, lanes] / l_sc[head]
        query_feature = feature(q_ref[:, lanes].astype(jnp.float32))
        numerator = jnp.dot(
            query_feature, memory, precision=lax.Precision.HIGHEST,
            preferred_element_type=jnp.float32,
        )
        denominator = jnp.maximum(
            jnp.sum(query_feature * normalizer, axis=-1, keepdims=True), 1.0
        )
        mixing = gate_ref[kv_head * group_size + head]
        o_ref[:, lanes] = (
            mixing * (numerator / denominator) + (1.0 - mixing) * local_part
        ).astype(o_ref.dtype)


def near_tables(core):
    tables = np.array(
        [[[c, 1 ^ c, 1 ^ c], [c, c, 1 ^ c], [1, 1, 0], [1, 0, 1]] for c in range(2)], np.int32
    )
    return jnp.asarray(tables)[core]


def far_tables(chips, chip, core, source):
    per_block = max(1, 2 * (chips - 1))
    tables = np.zeros((chips, 2, 5, per_block), np.int32)
    for y in range(chips):
        for c in range(2):
            steps = []
            k_pos = 0
            for j in range(per_block):
                valid = int(j < 2 * y)
                if valid:
                    k_pos = 2 * (chips - 1 - y + j // 2) + ((j % 2) ^ c)
                steps.append((source, k_pos, int(j == 0), int(j == per_block - 1), valid))
            tables[y, c] = np.array(steps, np.int32).T
    return jnp.asarray(tables)[chip, core]


def attend(keep_q, recv_q, keep_kv, recv_kv, far_kv, state, mixing, chips, chip, core, group_size):
    block, q_cols = keep_q.shape
    kv_group = keep_kv.shape[-1] // (2 * HD)
    width = group_size * HD
    scratch = [
        pltpu.VMEM((group_size, block, LANES), jnp.float32),
        pltpu.VMEM((group_size, block, LANES), jnp.float32),
        pltpu.VMEM((block, width), jnp.float32),
    ]
    params = pltpu.CompilerParams(dimension_semantics=("arbitrary", "arbitrary"))
    near = near_tables(core)
    q_spec = pl.BlockSpec((block, width), lambda g, t, *_: (0, g))
    k_spec = pl.BlockSpec((block, HD), lambda g, t, *_: (0, g))
    v_spec = pl.BlockSpec((block, HD), lambda g, t, *_: (0, kv_group + g))
    near_spec = pltpu.PrefetchScalarGridSpec(
        num_scalar_prefetch=4,
        grid=(kv_group, near.shape[-1]),
        in_specs=[q_spec, q_spec, k_spec, v_spec, k_spec, v_spec],
        out_specs=[
            pl.BlockSpec((None, block, width), lambda g, t, qs, ks, f, d: (qs[t], 0, g)),
            pl.BlockSpec((None, None, block, LANES), lambda g, t, qs, ks, f, d: (g, qs[t], 0, 0)),
        ],
        scratch_shapes=scratch,
    )
    pair_flops = 4 * block * block * HD * group_size * kv_group
    pair_exps = block * block * group_size * kv_group
    acc, ml = pl.pallas_call(
        functools.partial(near_kernel, group_size=group_size),
        grid_spec=near_spec,
        cost_estimate=pl.CostEstimate(
            flops=3 * pair_flops, transcendentals=3 * pair_exps,
            bytes_accessed=int(keep_q.size * 12 + keep_kv.size * 4),
        ),
        out_shape=[
            jax.ShapeDtypeStruct((2, block, q_cols), jnp.float32),
            jax.ShapeDtypeStruct((kv_group, 2, block, LANES), jnp.float32),
        ],
        compiler_params=params,
    )(*[near[i] for i in range(4)], keep_q, recv_q, keep_kv, keep_kv, recv_kv, recv_kv)
    far_pairs = max(1, 2 * (chips - 1))

    def far_call(source, out_cols, col_offset):
        far = far_tables(chips, chip, core, source)
        offset = jnp.reshape(col_offset, (1,)).astype(jnp.int32)
        part_specs = []
        for _ in far_kv:
            part_specs += [k_spec, v_spec]
        far_spec = pltpu.PrefetchScalarGridSpec(
            num_scalar_prefetch=6,
            grid=(kv_group, far.shape[-1]),
            in_specs=[pl.BlockSpec(memory_space=pltpu.SMEM), q_spec]
            + part_specs
            + [
                pl.BlockSpec((None, STATE_ROWS, HD), lambda g, t, qp, kp, f, l, v, o: (g, 0, 0)),
                pl.BlockSpec((None, block, width), lambda g, t, qp, kp, f, l, v, o: (qp[t], 0, g)),
                pl.BlockSpec(
                    (None, None, block, LANES), lambda g, t, qp, kp, f, l, v, o: (g, qp[t], 0, 0)
                ),
            ],
            out_specs=pl.BlockSpec((block, width), lambda g, t, qp, kp, f, l, v, o: (0, o[0] + g)),
            scratch_shapes=scratch,
        )
        kv_args = []
        for part in far_kv:
            kv_args += [part, part]
        return pl.pallas_call(
            functools.partial(far_kernel, group_size=group_size),
            grid_spec=far_spec,
            cost_estimate=pl.CostEstimate(
                flops=far_pairs * pair_flops // 2, transcendentals=far_pairs * pair_exps // 2,
                bytes_accessed=int(keep_q.size * 8 + keep_kv.size * 2 * len(far_kv)),
            ),
            out_shape=jax.ShapeDtypeStruct((block, out_cols), jnp.bfloat16),
            compiler_params=params,
        )(*[far[i] for i in range(5)], offset, mixing, (keep_q, recv_q)[source], *kv_args, state,
          acc, ml)

    sibling_part = far_call(1, q_cols, 0)
    back = lax.ppermute(sibling_part, "head", [(p, p ^ 1) for p in range(lax.axis_size("head"))])
    own_part = far_call(0, 2 * q_cols, core * kv_group)
    return own_part, back


def place_kernel(col_ref, full_ref, back_ref, o_ref):
    o_ref[...] = back_ref[...]


def place_back(own_part, back, core, kv_group):
    tokens_here, q_cols = back.shape
    other = jnp.reshape(1 - core, (1,)).astype(jnp.int32)
    grid_spec = pltpu.PrefetchScalarGridSpec(
        num_scalar_prefetch=1,
        grid=(1,),
        in_specs=[
            pl.BlockSpec(memory_space=pl.ANY),
            pl.BlockSpec((tokens_here, q_cols), lambda i, c: (0, 0)),
        ],
        out_specs=pl.BlockSpec((tokens_here, q_cols), lambda i, c: (0, c[0])),
    )
    return pl.pallas_call(
        place_kernel,
        grid_spec=grid_spec,
        out_shape=jax.ShapeDtypeStruct(own_part.shape, own_part.dtype),
        input_output_aliases={1: 0},
    )(other, own_part, back)


def body(queries, keys, values, gate_logit):
    parts = lax.axis_size("head")
    chips = parts // 2
    place = lax.axis_index("head")
    chip = place // 2
    core = place % 2
    k_cols = keys.shape[1] // 2
    kv_group = k_cols // HD
    group_size = queries.shape[1] // keys.shape[1]
    sibling = [(p, p ^ 1) for p in range(parts)]

    delta = chip_states(keys, values, core, kv_group)
    keep_q, keep_kv, send_q, send_kv = split_inputs(queries, keys, values, core)
    recv_q = lax.ppermute(send_q, "head", sibling)
    recv_kv = lax.ppermute(send_kv, "head", sibling)
    delta, keep_kv, send_kv, recv_q, recv_kv = lax.optimization_barrier(
        (delta, keep_kv, send_kv, recv_q, recv_kv)
    )
    state = earlier_states(delta)
    kv_parts = []
    for s in range(chips - 1, 0, -1):
        kv_parts.append(lax.ppermute(keep_kv, "head", [(p, p + 2 * s) for p in range(parts - 2 * s)]))
        kv_parts.append(
            lax.ppermute(send_kv, "head", [(p, (p + 2 * s) ^ 1) for p in range(parts - 2 * s)])
        )
    far_kv = kv_parts if kv_parts else [keep_kv, recv_kv]
    gate_here = lax.dynamic_slice_in_dim(gate_logit, core * kv_group * group_size, kv_group * group_size)
    mixing = jax.nn.sigmoid(gate_here)
    own_part, back = attend(
        keep_q, recv_q, keep_kv, recv_kv, far_kv, state, mixing, chips, chip, core, group_size
    )
    return place_back(own_part, back, core, kv_group)


def solution(mesh):
    in_specs = (P(("seq", "head"), None), P(("seq", "head"), None), P(("seq", "head"), None), P())
    out_specs = P(("seq", "head"), None)
    return jax.shard_map(body, mesh=mesh, in_specs=in_specs, out_specs=out_specs, check_vma=False)
```

```python
import functools

import jax
import jax.numpy as jnp
import numpy as np
from jax import lax
from jax.experimental import pallas as pl
from jax.experimental.pallas import tpu as pltpu
from jax.sharding import PartitionSpec as P

HQ = 32
KVH = 8
HD = 128
SEG = 2048
LANES = 128
STATE_ROWS = HD + 8


def feature(inputs):
    return jnp.where(inputs > 0, inputs + 1.0, jnp.exp(jnp.minimum(inputs, 0.0)))


def shifted(value, axis, steps):
    count = lax.axis_size(axis)
    return lax.ppermute(value, axis, [(source, source + steps) for source in range(count - steps)])


def split_kernel(core_ref, k_keep, v_keep, q_send, k_send, v_send, *out_refs):
    k_cols = k_keep.shape[-1]
    keep_kv, send_q, send_kv = out_refs
    keep_kv[:, :k_cols] = k_keep[...]
    keep_kv[:, k_cols:] = v_keep[...]
    send_q[...] = q_send[...]
    send_kv[:, :k_cols] = k_send[...]
    send_kv[:, k_cols:] = v_send[...]


def split_inputs(queries, keys, values, core):
    tokens_here, q_all = queries.shape
    q_cols = q_all // 2
    k_cols = keys.shape[1] // 2
    keep_map = lambda i, c: (0, c[0])
    send_map = lambda i, c: (0, 1 - c[0])
    q_shape = jax.ShapeDtypeStruct((tokens_here, q_cols), queries.dtype)
    kv_shape = jax.ShapeDtypeStruct((tokens_here, 2 * k_cols), keys.dtype)
    grid_spec = pltpu.PrefetchScalarGridSpec(
        num_scalar_prefetch=1,
        grid=(1,),
        in_specs=[
            pl.BlockSpec((tokens_here, k_cols), keep_map),
            pl.BlockSpec((tokens_here, k_cols), keep_map),
            pl.BlockSpec((tokens_here, q_cols), send_map),
            pl.BlockSpec((tokens_here, k_cols), send_map),
            pl.BlockSpec((tokens_here, k_cols), send_map),
        ],
        out_specs=[
            pl.BlockSpec((tokens_here, 2 * k_cols), lambda i, c: (0, 0)),
            pl.BlockSpec((tokens_here, q_cols), lambda i, c: (0, 0)),
            pl.BlockSpec((tokens_here, 2 * k_cols), lambda i, c: (0, 0)),
        ],
    )
    return pl.pallas_call(
        split_kernel, grid_spec=grid_spec, out_shape=[kv_shape, q_shape, kv_shape]
    )(core.reshape(1), keys, values, queries, keys, values)


def delta_kernel(k_ref, v_ref, o_ref):
    for head in range(o_ref.shape[0]):
        lanes = slice(head * HD, (head + 1) * HD)
        key_feature = feature(k_ref[:, lanes].astype(jnp.float32))
        value_data = v_ref[:, lanes].astype(jnp.float32)
        o_ref[head, :HD, :] = jnp.dot(
            key_feature.T, value_data, precision=lax.Precision.HIGHEST,
            preferred_element_type=jnp.float32,
        )
        o_ref[head, HD:, :] = jnp.zeros((STATE_ROWS - HD, HD), jnp.float32)
        o_ref[head, HD : HD + 1, :] = jnp.sum(key_feature, axis=0, keepdims=True)


def local_deltas(keys, values):
    kv_heads = keys.shape[1] // HD
    return pl.pallas_call(
        delta_kernel,
        out_shape=jax.ShapeDtypeStruct((kv_heads, STATE_ROWS, HD), jnp.float32),
    )(keys, values)


def chip_states(keys, values, core, kv_group):
    total = local_deltas(keys, values)
    parts = lax.axis_size("head")
    keep = lax.dynamic_slice_in_dim(total, core * kv_group, kv_group)
    send = lax.dynamic_slice_in_dim(total, (1 - core) * kv_group, kv_group)
    total = keep + lax.ppermute(send.astype(jnp.bfloat16), "head", [(p, p ^ 1) for p in range(parts)])
    steps = 2
    while steps < parts:
        across = lax.ppermute(total.astype(jnp.bfloat16), "head", [(p, p ^ steps) for p in range(parts)])
        total = total + across
        steps *= 2
    return total


def earlier_states(delta):
    count = lax.axis_size("seq")
    total = delta
    steps = 1
    while steps < count:
        total = total + shifted(total.astype(jnp.bfloat16), "seq", steps)
        steps *= 2
    return total - delta


def online_step(q_ref, k_ref, v_ref, m_sc, l_sc, acc_sc, group_size, masked):
    block = q_ref.shape[0]
    score_scale = HD ** (-0.5)
    key_rows = k_ref[...]
    value_rows = jnp.concatenate([v_ref[...], jnp.ones((block, LANES), v_ref.dtype)], axis=1)
    if masked:
        rows = lax.broadcasted_iota(jnp.int32, (block, block), 0)
        cols = lax.broadcasted_iota(jnp.int32, (block, block), 1)
        allowed = cols <= rows
    for head in range(group_size):
        lanes = slice(head * HD, (head + 1) * HD)
        scores = lax.dot_general(
            q_ref[:, lanes], key_rows, (((1,), (1,)), ((), ())),
            preferred_element_type=jnp.float32,
        )
        if masked:
            scores = jnp.where(allowed, scores, -1e30)
        m_prev = m_sc[head]
        m_new = jnp.maximum(m_prev, jnp.max(scores, axis=-1, keepdims=True) * score_scale)
        probs = jnp.exp(scores * score_scale - m_new[:, :1])
        alpha = jnp.exp(m_prev - m_new)
        both = jnp.dot(probs.astype(jnp.bfloat16), value_rows, preferred_element_type=jnp.float32)
        l_sc[head] = alpha * l_sc[head] + both[:, HD:]
        acc_sc[:, lanes] = alpha * acc_sc[:, lanes] + both[:, :HD]
        m_sc[head] = m_new


def near_kernel(qs_ref, ks_ref, first_ref, diag_ref, off_ref, q_keep, q_recv, k_keep, v_keep, k_recv,
                v_recv, acc_ref, ml_ref, m_sc, l_sc, acc_sc, *, group_size):
    step_at = pl.program_id(1)
    q_src = qs_ref[step_at]
    k_src = ks_ref[step_at]
    diag = diag_ref[step_at] == 1

    @pl.when(first_ref[step_at] == 1)
    def _init():
        m_sc[...] = jnp.full(m_sc.shape, -jnp.inf, jnp.float32)
        l_sc[...] = jnp.zeros(l_sc.shape, jnp.float32)
        acc_sc[...] = jnp.zeros(acc_sc.shape, jnp.float32)

    sources = ((q_keep, k_keep, v_keep), (q_recv, k_recv, v_recv))
    for q_at in range(2):
        for k_at in range(2):
            masked = q_at == k_at

            @pl.when((q_src == q_at) & (k_src == k_at) & (diag == masked))
            def _step():
                q_ref = sources[q_at][0]
                online_step(q_ref, sources[k_at][1], sources[k_at][2], m_sc, l_sc, acc_sc,
                            group_size, masked)

    @pl.when(diag)
    def _save():
        acc_ref[...] = acc_sc[...]
        lane = lax.broadcasted_iota(jnp.int32, ml_ref.shape, 1)
        packed = jnp.zeros(ml_ref.shape, jnp.float32)
        for head in range(group_size):
            packed = jnp.where(lane == head, m_sc[head], packed)
            packed = jnp.where(lane == group_size + head, l_sc[head], packed)
        ml_ref[...] = packed


def far_kernel(qp_ref, kp_ref, first_ref, last_ref, valid_ref, off_ref, gate_ref, q_ref, *refs,
               group_size):
    kv_refs = refs[:-7]
    s_ref, acc_in, ml_in, o_ref, m_sc, l_sc, acc_sc = refs[-7:]
    kv_head = pl.program_id(0)
    step_at = pl.program_id(1)

    @pl.when(first_ref[step_at] == 1)
    def _init():
        packed = ml_in[...]
        for head in range(group_size):
            m_sc[head] = jnp.broadcast_to(packed[:, head : head + 1], m_sc.shape[1:])
            l_sc[head] = jnp.broadcast_to(
                packed[:, group_size + head : group_size + head + 1], l_sc.shape[1:]
            )
        acc_sc[...] = acc_in[...]

    for part in range(len(kv_refs) // 2):
        @pl.when((kp_ref[step_at] == part) & (valid_ref[step_at] == 1))
        def _step():
            online_step(q_ref, kv_refs[2 * part], kv_refs[2 * part + 1], m_sc, l_sc, acc_sc,
                        group_size, False)

    @pl.when(last_ref[step_at] == 1)
    def _last():
        finish(q_ref, s_ref, gate_ref, o_ref, acc_sc, l_sc, kv_head, group_size)


def finish(q_ref, s_ref, gate_ref, o_ref, acc_sc, l_sc, kv_head, group_size):
    memory = s_ref[:HD, :]
    normalizer = s_ref[HD : HD + 1, :]
    for head in range(group_size):
        lanes = slice(head * HD, (head + 1) * HD)
        local_part = acc_sc[:, lanes] / l_sc[head]
        query_feature = feature(q_ref[:, lanes].astype(jnp.float32))
        numerator = jnp.dot(
            query_feature, memory, precision=lax.Precision.HIGHEST,
            preferred_element_type=jnp.float32,
        )
        denominator = jnp.maximum(
            jnp.sum(query_feature * normalizer, axis=-1, keepdims=True), 1.0
        )
        mixing = gate_ref[kv_head * group_size + head]
        o_ref[:, lanes] = (
            mixing * (numerator / denominator) + (1.0 - mixing) * local_part
        ).astype(o_ref.dtype)


def near_tables(core):
    tables = np.array(
        [[[c, 1 ^ c, 1 ^ c], [c, c, 1 ^ c], [1, 1, 0], [1, 0, 1]] for c in range(2)], np.int32
    )
    return jnp.asarray(tables)[core]


def far_tables(chips, chip, core, source):
    per_block = max(1, 2 * (chips - 1))
    tables = np.zeros((chips, 2, 5, per_block), np.int32)
    for y in range(chips):
        for c in range(2):
            steps = []
            k_pos = 0
            for j in range(per_block):
                valid = int(j < 2 * y)
                if valid:
                    k_pos = 2 * (chips - 1 - y + j // 2) + ((j % 2) ^ c)
                steps.append((source, k_pos, int(j == 0), int(j == per_block - 1), valid))
            tables[y, c] = np.array(steps, np.int32).T
    return jnp.asarray(tables)[chip, core]


def attend(queries, recv_q, keep_kv, recv_kv, far_kv, state, mixing, chips, chip, core, group_size):
    block, q_cols = recv_q.shape
    keep_q = queries
    kv_group = keep_kv.shape[-1] // (2 * HD)
    width = group_size * HD
    scratch = [
        pltpu.VMEM((group_size, block, LANES), jnp.float32),
        pltpu.VMEM((group_size, block, LANES), jnp.float32),
        pltpu.VMEM((block, width), jnp.float32),
    ]
    params = pltpu.CompilerParams(dimension_semantics=("arbitrary", "arbitrary"))
    near = near_tables(core)
    q_offset = jnp.reshape(core * kv_group, (1,)).astype(jnp.int32)
    q_spec = pl.BlockSpec((block, width), lambda g, t, *_: (0, g))
    own_q_spec = pl.BlockSpec((block, width), lambda g, t, *p: (0, p[-1][0] + g))
    k_spec = pl.BlockSpec((block, HD), lambda g, t, *_: (0, g))
    v_spec = pl.BlockSpec((block, HD), lambda g, t, *_: (0, kv_group + g))
    near_spec = pltpu.PrefetchScalarGridSpec(
        num_scalar_prefetch=5,
        grid=(kv_group, near.shape[-1]),
        in_specs=[own_q_spec, q_spec, k_spec, v_spec, k_spec, v_spec],
        out_specs=[
            pl.BlockSpec((None, block, width), lambda g, t, qs, ks, f, d, o: (qs[t], 0, g)),
            pl.BlockSpec(
                (None, None, block, LANES), lambda g, t, qs, ks, f, d, o: (g, qs[t], 0, 0)
            ),
        ],
        scratch_shapes=scratch,
    )
    pair_flops = 4 * block * block * HD * group_size * kv_group
    pair_exps = block * block * group_size * kv_group
    acc, ml = pl.pallas_call(
        functools.partial(near_kernel, group_size=group_size),
        grid_spec=near_spec,
        cost_estimate=pl.CostEstimate(
            flops=3 * pair_flops, transcendentals=3 * pair_exps,
            bytes_accessed=int(recv_q.size * 12 + keep_kv.size * 4),
        ),
        out_shape=[
            jax.ShapeDtypeStruct((2, block, q_cols), jnp.float32),
            jax.ShapeDtypeStruct((kv_group, 2, block, LANES), jnp.float32),
        ],
        compiler_params=params,
    )(*[near[i] for i in range(4)], q_offset, keep_q, recv_q, keep_kv, keep_kv, recv_kv, recv_kv)
    far_pairs = max(1, 2 * (chips - 1))

    def far_call(source, out_cols, col_offset):
        far = far_tables(chips, chip, core, source)
        offset = jnp.reshape(col_offset, (1,)).astype(jnp.int32)
        part_specs = []
        for _ in far_kv:
            part_specs += [k_spec, v_spec]
        far_spec = pltpu.PrefetchScalarGridSpec(
            num_scalar_prefetch=6,
            grid=(kv_group, far.shape[-1]),
            in_specs=[pl.BlockSpec(memory_space=pltpu.SMEM), own_q_spec]
            + part_specs
            + [
                pl.BlockSpec((None, STATE_ROWS, HD), lambda g, t, qp, kp, f, l, v, o: (g, 0, 0)),
                pl.BlockSpec((None, block, width), lambda g, t, qp, kp, f, l, v, o: (qp[t], 0, g)),
                pl.BlockSpec(
                    (None, None, block, LANES), lambda g, t, qp, kp, f, l, v, o: (g, qp[t], 0, 0)
                ),
            ],
            out_specs=pl.BlockSpec((block, width), lambda g, t, qp, kp, f, l, v, o: (0, o[0] + g)),
            scratch_shapes=scratch,
        )
        kv_args = []
        for part in far_kv:
            kv_args += [part, part]
        return pl.pallas_call(
            functools.partial(far_kernel, group_size=group_size),
            grid_spec=far_spec,
            cost_estimate=pl.CostEstimate(
                flops=far_pairs * pair_flops // 2, transcendentals=far_pairs * pair_exps // 2,
                bytes_accessed=int(recv_q.size * 8 + keep_kv.size * 2 * len(far_kv)),
            ),
            out_shape=jax.ShapeDtypeStruct((block, out_cols), jnp.bfloat16),
            compiler_params=params,
        )(*[far[i] for i in range(5)], offset, mixing, (keep_q, recv_q)[source], *kv_args, state,
          acc, ml)

    sibling_part = far_call(1, q_cols, 0)
    back = lax.ppermute(sibling_part, "head", [(p, p ^ 1) for p in range(lax.axis_size("head"))])
    own_part = far_call(0, 2 * q_cols, core * kv_group)
    return own_part, back


def place_kernel(col_ref, full_ref, back_ref, o_ref):
    o_ref[...] = back_ref[...]


def place_back(own_part, back, core, kv_group):
    tokens_here, q_cols = back.shape
    other = jnp.reshape(1 - core, (1,)).astype(jnp.int32)
    grid_spec = pltpu.PrefetchScalarGridSpec(
        num_scalar_prefetch=1,
        grid=(1,),
        in_specs=[
            pl.BlockSpec(memory_space=pl.ANY),
            pl.BlockSpec((tokens_here, q_cols), lambda i, c: (0, 0)),
        ],
        out_specs=pl.BlockSpec((tokens_here, q_cols), lambda i, c: (0, c[0])),
    )
    return pl.pallas_call(
        place_kernel,
        grid_spec=grid_spec,
        out_shape=jax.ShapeDtypeStruct(own_part.shape, own_part.dtype),
        input_output_aliases={1: 0},
    )(other, own_part, back)


def body(queries, keys, values, gate_logit):
    parts = lax.axis_size("head")
    chips = parts // 2
    place = lax.axis_index("head")
    chip = place // 2
    core = place % 2
    k_cols = keys.shape[1] // 2
    kv_group = k_cols // HD
    group_size = queries.shape[1] // keys.shape[1]
    sibling = [(p, p ^ 1) for p in range(parts)]

    delta = chip_states(keys, values, core, kv_group)
    keep_kv, send_q, send_kv = split_inputs(queries, keys, values, core)
    recv_q = lax.ppermute(send_q, "head", sibling)
    recv_kv = lax.ppermute(send_kv, "head", sibling)
    delta, keep_kv, send_kv, recv_q, recv_kv = lax.optimization_barrier(
        (delta, keep_kv, send_kv, recv_q, recv_kv)
    )
    state = earlier_states(delta)
    kv_parts = []
    for s in range(chips - 1, 0, -1):
        kv_parts.append(lax.ppermute(keep_kv, "head", [(p, p + 2 * s) for p in range(parts - 2 * s)]))
        kv_parts.append(
            lax.ppermute(send_kv, "head", [(p, (p + 2 * s) ^ 1) for p in range(parts - 2 * s)])
        )
    far_kv = kv_parts if kv_parts else [keep_kv, recv_kv]
    gate_here = lax.dynamic_slice_in_dim(gate_logit, core * kv_group * group_size, kv_group * group_size)
    mixing = jax.nn.sigmoid(gate_here)
    own_part, back = attend(
        queries, recv_q, keep_kv, recv_kv, far_kv, state, mixing, chips, chip, core, group_size
    )
    return place_back(own_part, back, core, kv_group)


def solution(mesh):
    in_specs = (P(("seq", "head"), None), P(("seq", "head"), None), P(("seq", "head"), None), P())
    out_specs = P(("seq", "head"), None)
    return jax.shard_map(body, mesh=mesh, in_specs=in_specs, out_specs=out_specs, check_vma=False)
```

```python
import functools

import jax
import jax.numpy as jnp
import numpy as np
from jax import lax
from jax.experimental import pallas as pl
from jax.experimental.pallas import tpu as pltpu
from jax.sharding import PartitionSpec as P

HQ = 32
KVH = 8
HD = 128
SEG = 2048
LANES = 128
STATE_ROWS = HD + 8


def feature(inputs):
    return jnp.where(inputs > 0, inputs + 1.0, jnp.exp(jnp.minimum(inputs, 0.0)))


def shifted(value, axis, steps):
    count = lax.axis_size(axis)
    return lax.ppermute(value, axis, [(source, source + steps) for source in range(count - steps)])


def head_sums(k_ref, v_ref, o_ref):
    for head in range(o_ref.shape[0]):
        lanes = slice(head * HD, (head + 1) * HD)
        key_feature = feature(k_ref[:, lanes].astype(jnp.float32))
        value_data = v_ref[:, lanes].astype(jnp.float32)
        o_ref[head, :HD, :] = jnp.dot(
            key_feature.T, value_data, precision=lax.Precision.HIGHEST,
            preferred_element_type=jnp.float32,
        )
        o_ref[head, HD:, :] = jnp.zeros((STATE_ROWS - HD, HD), jnp.float32)
        o_ref[head, HD : HD + 1, :] = jnp.sum(key_feature, axis=0, keepdims=True)


def split_kernel(core_ref, k_keep, v_keep, q_send, k_send, v_send, *out_refs):
    k_cols = k_keep.shape[-1]
    keep_kv, send_q, send_kv, keep_sums, send_sums = out_refs
    keep_kv[:, :k_cols] = k_keep[...]
    keep_kv[:, k_cols:] = v_keep[...]
    send_q[...] = q_send[...]
    send_kv[:, :k_cols] = k_send[...]
    send_kv[:, k_cols:] = v_send[...]
    head_sums(k_keep, v_keep, keep_sums)
    head_sums(k_send, v_send, send_sums)


def split_inputs(queries, keys, values, core):
    tokens_here, q_all = queries.shape
    q_cols = q_all // 2
    k_cols = keys.shape[1] // 2
    kv_group = k_cols // HD
    keep_map = lambda i, c: (0, c[0])
    send_map = lambda i, c: (0, 1 - c[0])
    q_shape = jax.ShapeDtypeStruct((tokens_here, q_cols), queries.dtype)
    kv_shape = jax.ShapeDtypeStruct((tokens_here, 2 * k_cols), keys.dtype)
    sums_shape = jax.ShapeDtypeStruct((kv_group, STATE_ROWS, HD), jnp.float32)
    grid_spec = pltpu.PrefetchScalarGridSpec(
        num_scalar_prefetch=1,
        grid=(1,),
        in_specs=[
            pl.BlockSpec((tokens_here, k_cols), keep_map),
            pl.BlockSpec((tokens_here, k_cols), keep_map),
            pl.BlockSpec((tokens_here, q_cols), send_map),
            pl.BlockSpec((tokens_here, k_cols), send_map),
            pl.BlockSpec((tokens_here, k_cols), send_map),
        ],
        out_specs=[
            pl.BlockSpec((tokens_here, 2 * k_cols), lambda i, c: (0, 0)),
            pl.BlockSpec((tokens_here, q_cols), lambda i, c: (0, 0)),
            pl.BlockSpec((tokens_here, 2 * k_cols), lambda i, c: (0, 0)),
            pl.BlockSpec((kv_group, STATE_ROWS, HD), lambda i, c: (0, 0, 0)),
            pl.BlockSpec((kv_group, STATE_ROWS, HD), lambda i, c: (0, 0, 0)),
        ],
    )
    return pl.pallas_call(
        split_kernel,
        grid_spec=grid_spec,
        out_shape=[kv_shape, q_shape, kv_shape, sums_shape, sums_shape],
    )(core.reshape(1), keys, values, queries, keys, values)


def chip_states(keep, send):
    parts = lax.axis_size("head")
    total = keep + lax.ppermute(send.astype(jnp.bfloat16), "head", [(p, p ^ 1) for p in range(parts)])
    steps = 2
    while steps < parts:
        across = lax.ppermute(total.astype(jnp.bfloat16), "head", [(p, p ^ steps) for p in range(parts)])
        total = total + across
        steps *= 2
    return total


def earlier_states(delta):
    count = lax.axis_size("seq")
    total = delta
    steps = 1
    while steps < count:
        total = total + shifted(total.astype(jnp.bfloat16), "seq", steps)
        steps *= 2
    return total - delta


def online_step(q_ref, k_ref, v_ref, m_sc, l_sc, acc_sc, group_size, masked):
    block = q_ref.shape[0]
    score_scale = HD ** (-0.5)
    key_rows = k_ref[...]
    value_rows = jnp.concatenate([v_ref[...], jnp.ones((block, LANES), v_ref.dtype)], axis=1)
    if masked:
        rows = lax.broadcasted_iota(jnp.int32, (block, block), 0)
        cols = lax.broadcasted_iota(jnp.int32, (block, block), 1)
        allowed = cols <= rows
    for head in range(group_size):
        lanes = slice(head * HD, (head + 1) * HD)
        scores = lax.dot_general(
            q_ref[:, lanes], key_rows, (((1,), (1,)), ((), ())),
            preferred_element_type=jnp.float32,
        )
        if masked:
            scores = jnp.where(allowed, scores, -1e30)
        m_prev = m_sc[head]
        m_new = jnp.maximum(m_prev, jnp.max(scores, axis=-1, keepdims=True) * score_scale)
        probs = jnp.exp(scores * score_scale - m_new[:, :1])
        alpha = jnp.exp(m_prev - m_new)
        both = jnp.dot(probs.astype(jnp.bfloat16), value_rows, preferred_element_type=jnp.float32)
        l_sc[head] = alpha * l_sc[head] + both[:, HD:]
        acc_sc[:, lanes] = alpha * acc_sc[:, lanes] + both[:, :HD]
        m_sc[head] = m_new


def near_kernel(qs_ref, ks_ref, first_ref, diag_ref, off_ref, q_keep, q_recv, k_keep, v_keep, k_recv,
                v_recv, acc_ref, ml_ref, m_sc, l_sc, acc_sc, *, group_size):
    step_at = pl.program_id(1)
    q_src = qs_ref[step_at]
    k_src = ks_ref[step_at]
    diag = diag_ref[step_at] == 1

    @pl.when(first_ref[step_at] == 1)
    def _init():
        m_sc[...] = jnp.full(m_sc.shape, -jnp.inf, jnp.float32)
        l_sc[...] = jnp.zeros(l_sc.shape, jnp.float32)
        acc_sc[...] = jnp.zeros(acc_sc.shape, jnp.float32)

    sources = ((q_keep, k_keep, v_keep), (q_recv, k_recv, v_recv))
    for q_at in range(2):
        for k_at in range(2):
            masked = q_at == k_at

            @pl.when((q_src == q_at) & (k_src == k_at) & (diag == masked))
            def _step():
                q_ref = sources[q_at][0]
                online_step(q_ref, sources[k_at][1], sources[k_at][2], m_sc, l_sc, acc_sc,
                            group_size, masked)

    @pl.when(diag)
    def _save():
        acc_ref[...] = acc_sc[...]
        lane = lax.broadcasted_iota(jnp.int32, ml_ref.shape, 1)
        packed = jnp.zeros(ml_ref.shape, jnp.float32)
        for head in range(group_size):
            packed = jnp.where(lane == head, m_sc[head], packed)
            packed = jnp.where(lane == group_size + head, l_sc[head], packed)
        ml_ref[...] = packed


def far_kernel(qp_ref, kp_ref, first_ref, last_ref, valid_ref, off_ref, gate_ref, q_ref, *refs,
               group_size):
    kv_refs = refs[:-7]
    s_ref, acc_in, ml_in, o_ref, m_sc, l_sc, acc_sc = refs[-7:]
    kv_head = pl.program_id(0)
    step_at = pl.program_id(1)

    @pl.when(first_ref[step_at] == 1)
    def _init():
        packed = ml_in[...]
        for head in range(group_size):
            m_sc[head] = jnp.broadcast_to(packed[:, head : head + 1], m_sc.shape[1:])
            l_sc[head] = jnp.broadcast_to(
                packed[:, group_size + head : group_size + head + 1], l_sc.shape[1:]
            )
        acc_sc[...] = acc_in[...]

    for part in range(len(kv_refs) // 2):
        @pl.when((kp_ref[step_at] == part) & (valid_ref[step_at] == 1))
        def _step():
            online_step(q_ref, kv_refs[2 * part], kv_refs[2 * part + 1], m_sc, l_sc, acc_sc,
                        group_size, False)

    @pl.when(last_ref[step_at] == 1)
    def _last():
        finish(q_ref, s_ref, gate_ref, o_ref, acc_sc, l_sc, kv_head, group_size)


def finish(q_ref, s_ref, gate_ref, o_ref, acc_sc, l_sc, kv_head, group_size):
    memory = s_ref[:HD, :]
    normalizer = s_ref[HD : HD + 1, :]
    for head in range(group_size):
        lanes = slice(head * HD, (head + 1) * HD)
        local_part = acc_sc[:, lanes] / l_sc[head]
        query_feature = feature(q_ref[:, lanes].astype(jnp.float32))
        numerator = jnp.dot(
            query_feature, memory, precision=lax.Precision.HIGHEST,
            preferred_element_type=jnp.float32,
        )
        denominator = jnp.maximum(
            jnp.sum(query_feature * normalizer, axis=-1, keepdims=True), 1.0
        )
        mixing = gate_ref[kv_head * group_size + head]
        o_ref[:, lanes] = (
            mixing * (numerator / denominator) + (1.0 - mixing) * local_part
        ).astype(o_ref.dtype)


def near_tables(core):
    tables = np.array(
        [[[c, 1 ^ c, 1 ^ c], [c, c, 1 ^ c], [1, 1, 0], [1, 0, 1]] for c in range(2)], np.int32
    )
    return jnp.asarray(tables)[core]


def far_tables(chips, chip, core, source):
    per_block = max(1, 2 * (chips - 1))
    tables = np.zeros((chips, 2, 5, per_block), np.int32)
    for y in range(chips):
        for c in range(2):
            steps = []
            k_pos = 0
            for j in range(per_block):
                valid = int(j < 2 * y)
                if valid:
                    k_pos = 2 * (chips - 1 - y + j // 2) + ((j % 2) ^ c)
                steps.append((source, k_pos, int(j == 0), int(j == per_block - 1), valid))
            tables[y, c] = np.array(steps, np.int32).T
    return jnp.asarray(tables)[chip, core]


def attend(queries, recv_q, keep_kv, recv_kv, far_kv, state, mixing, chips, chip, core, group_size):
    block, q_cols = recv_q.shape
    keep_q = queries
    kv_group = keep_kv.shape[-1] // (2 * HD)
    width = group_size * HD
    scratch = [
        pltpu.VMEM((group_size, block, LANES), jnp.float32),
        pltpu.VMEM((group_size, block, LANES), jnp.float32),
        pltpu.VMEM((block, width), jnp.float32),
    ]
    params = pltpu.CompilerParams(dimension_semantics=("arbitrary", "arbitrary"))
    near = near_tables(core)
    q_offset = jnp.reshape(core * kv_group, (1,)).astype(jnp.int32)
    q_spec = pl.BlockSpec((block, width), lambda g, t, *_: (0, g))
    own_q_spec = pl.BlockSpec((block, width), lambda g, t, *p: (0, p[-1][0] + g))
    k_spec = pl.BlockSpec((block, HD), lambda g, t, *_: (0, g))
    v_spec = pl.BlockSpec((block, HD), lambda g, t, *_: (0, kv_group + g))
    near_spec = pltpu.PrefetchScalarGridSpec(
        num_scalar_prefetch=5,
        grid=(kv_group, near.shape[-1]),
        in_specs=[own_q_spec, q_spec, k_spec, v_spec, k_spec, v_spec],
        out_specs=[
            pl.BlockSpec((None, block, width), lambda g, t, qs, ks, f, d, o: (qs[t], 0, g)),
            pl.BlockSpec(
                (None, None, block, LANES), lambda g, t, qs, ks, f, d, o: (g, qs[t], 0, 0)
            ),
        ],
        scratch_shapes=scratch,
    )
    pair_flops = 4 * block * block * HD * group_size * kv_group
    pair_exps = block * block * group_size * kv_group
    acc, ml = pl.pallas_call(
        functools.partial(near_kernel, group_size=group_size),
        grid_spec=near_spec,
        cost_estimate=pl.CostEstimate(
            flops=3 * pair_flops, transcendentals=3 * pair_exps,
            bytes_accessed=int(recv_q.size * 12 + keep_kv.size * 4),
        ),
        out_shape=[
            jax.ShapeDtypeStruct((2, block, q_cols), jnp.float32),
            jax.ShapeDtypeStruct((kv_group, 2, block, LANES), jnp.float32),
        ],
        compiler_params=params,
    )(*[near[i] for i in range(4)], q_offset, keep_q, recv_q, keep_kv, keep_kv, recv_kv, recv_kv)
    far_pairs = max(1, 2 * (chips - 1))

    def far_call(source, out_cols, col_offset):
        far = far_tables(chips, chip, core, source)
        offset = jnp.reshape(col_offset, (1,)).astype(jnp.int32)
        part_specs = []
        for _ in far_kv:
            part_specs += [k_spec, v_spec]
        far_spec = pltpu.PrefetchScalarGridSpec(
            num_scalar_prefetch=6,
            grid=(kv_group, far.shape[-1]),
            in_specs=[pl.BlockSpec(memory_space=pltpu.SMEM), own_q_spec]
            + part_specs
            + [
                pl.BlockSpec((None, STATE_ROWS, HD), lambda g, t, qp, kp, f, l, v, o: (g, 0, 0)),
                pl.BlockSpec((None, block, width), lambda g, t, qp, kp, f, l, v, o: (qp[t], 0, g)),
                pl.BlockSpec(
                    (None, None, block, LANES), lambda g, t, qp, kp, f, l, v, o: (g, qp[t], 0, 0)
                ),
            ],
            out_specs=pl.BlockSpec((block, width), lambda g, t, qp, kp, f, l, v, o: (0, o[0] + g)),
            scratch_shapes=scratch,
        )
        kv_args = []
        for part in far_kv:
            kv_args += [part, part]
        return pl.pallas_call(
            functools.partial(far_kernel, group_size=group_size),
            grid_spec=far_spec,
            cost_estimate=pl.CostEstimate(
                flops=far_pairs * pair_flops // 2, transcendentals=far_pairs * pair_exps // 2,
                bytes_accessed=int(recv_q.size * 8 + keep_kv.size * 2 * len(far_kv)),
            ),
            out_shape=jax.ShapeDtypeStruct((block, out_cols), jnp.bfloat16),
            compiler_params=params,
        )(*[far[i] for i in range(5)], offset, mixing, (keep_q, recv_q)[source], *kv_args, state,
          acc, ml)

    sibling_part = far_call(1, q_cols, 0)
    back = lax.ppermute(sibling_part, "head", [(p, p ^ 1) for p in range(lax.axis_size("head"))])
    own_part = far_call(0, 2 * q_cols, core * kv_group)
    return own_part, back


def place_kernel(col_ref, full_ref, back_ref, o_ref):
    o_ref[...] = back_ref[...]


def place_back(own_part, back, core, kv_group):
    tokens_here, q_cols = back.shape
    other = jnp.reshape(1 - core, (1,)).astype(jnp.int32)
    grid_spec = pltpu.PrefetchScalarGridSpec(
        num_scalar_prefetch=1,
        grid=(1,),
        in_specs=[
            pl.BlockSpec(memory_space=pl.ANY),
            pl.BlockSpec((tokens_here, q_cols), lambda i, c: (0, 0)),
        ],
        out_specs=pl.BlockSpec((tokens_here, q_cols), lambda i, c: (0, c[0])),
    )
    return pl.pallas_call(
        place_kernel,
        grid_spec=grid_spec,
        out_shape=jax.ShapeDtypeStruct(own_part.shape, own_part.dtype),
        input_output_aliases={1: 0},
    )(other, own_part, back)


def body(queries, keys, values, gate_logit):
    parts = lax.axis_size("head")
    chips = parts // 2
    place = lax.axis_index("head")
    chip = place // 2
    core = place % 2
    k_cols = keys.shape[1] // 2
    kv_group = k_cols // HD
    group_size = queries.shape[1] // keys.shape[1]
    sibling = [(p, p ^ 1) for p in range(parts)]

    keep_kv, send_q, send_kv, keep_sums, send_sums = split_inputs(queries, keys, values, core)
    delta = chip_states(keep_sums, send_sums)
    recv_q = lax.ppermute(send_q, "head", sibling)
    recv_kv = lax.ppermute(send_kv, "head", sibling)
    delta, keep_kv, send_kv, recv_q, recv_kv = lax.optimization_barrier(
        (delta, keep_kv, send_kv, recv_q, recv_kv)
    )
    state = earlier_states(delta)
    kv_parts = []
    for s in range(chips - 1, 0, -1):
        kv_parts.append(lax.ppermute(keep_kv, "head", [(p, p + 2 * s) for p in range(parts - 2 * s)]))
        kv_parts.append(
            lax.ppermute(send_kv, "head", [(p, (p + 2 * s) ^ 1) for p in range(parts - 2 * s)])
        )
    far_kv = kv_parts if kv_parts else [keep_kv, recv_kv]
    gate_here = lax.dynamic_slice_in_dim(gate_logit, core * kv_group * group_size, kv_group * group_size)
    mixing = jax.nn.sigmoid(gate_here)
    own_part, back = attend(
        queries, recv_q, keep_kv, recv_kv, far_kv, state, mixing, chips, chip, core, group_size
    )
    return place_back(own_part, back, core, kv_group)


def solution(mesh):
    in_specs = (P(("seq", "head"), None), P(("seq", "head"), None), P(("seq", "head"), None), P())
    out_specs = P(("seq", "head"), None)
    return jax.shard_map(body, mesh=mesh, in_specs=in_specs, out_specs=out_specs, check_vma=False)
```

```python
import functools

import jax
import jax.numpy as jnp
import numpy as np
from jax import lax
from jax.experimental import pallas as pl
from jax.experimental.pallas import tpu as pltpu
from jax.sharding import PartitionSpec as P

HQ = 32
KVH = 8
HD = 128
SEG = 2048
LANES = 128
STATE_ROWS = HD + 8


def feature(inputs):
    return jnp.where(inputs > 0, inputs + 1.0, jnp.exp(jnp.minimum(inputs, 0.0)))


def shifted(value, axis, steps):
    count = lax.axis_size(axis)
    return lax.ppermute(value, axis, [(source, source + steps) for source in range(count - steps)])


def head_sums(k_ref, v_ref, o_ref):
    for head in range(o_ref.shape[0]):
        lanes = slice(head * HD, (head + 1) * HD)
        key_feature = feature(k_ref[:, lanes].astype(jnp.float32))
        value_data = v_ref[:, lanes].astype(jnp.float32)
        o_ref[head, :HD, :] = jnp.dot(
            key_feature.T, value_data, precision=lax.Precision.HIGHEST,
            preferred_element_type=jnp.float32,
        )
        o_ref[head, HD:, :] = jnp.zeros((STATE_ROWS - HD, HD), jnp.float32)
        o_ref[head, HD : HD + 1, :] = jnp.sum(key_feature, axis=0, keepdims=True)


def split_kernel(core_ref, k_keep, v_keep, q_send, k_send, v_send, *out_refs):
    k_cols = k_keep.shape[-1]
    keep_kv, send_q, send_kv, keep_sums = out_refs
    keep_kv[:, :k_cols] = k_keep[...]
    keep_kv[:, k_cols:] = v_keep[...]
    send_q[...] = q_send[...]
    send_kv[:, :k_cols] = k_send[...]
    send_kv[:, k_cols:] = v_send[...]
    head_sums(k_keep, v_keep, keep_sums)


def split_inputs(queries, keys, values, core):
    tokens_here, q_all = queries.shape
    q_cols = q_all // 2
    k_cols = keys.shape[1] // 2
    kv_group = k_cols // HD
    keep_map = lambda i, c: (0, c[0])
    send_map = lambda i, c: (0, 1 - c[0])
    q_shape = jax.ShapeDtypeStruct((tokens_here, q_cols), queries.dtype)
    kv_shape = jax.ShapeDtypeStruct((tokens_here, 2 * k_cols), keys.dtype)
    sums_shape = jax.ShapeDtypeStruct((kv_group, STATE_ROWS, HD), jnp.float32)
    grid_spec = pltpu.PrefetchScalarGridSpec(
        num_scalar_prefetch=1,
        grid=(1,),
        in_specs=[
            pl.BlockSpec((tokens_here, k_cols), keep_map),
            pl.BlockSpec((tokens_here, k_cols), keep_map),
            pl.BlockSpec((tokens_here, q_cols), send_map),
            pl.BlockSpec((tokens_here, k_cols), send_map),
            pl.BlockSpec((tokens_here, k_cols), send_map),
        ],
        out_specs=[
            pl.BlockSpec((tokens_here, 2 * k_cols), lambda i, c: (0, 0)),
            pl.BlockSpec((tokens_here, q_cols), lambda i, c: (0, 0)),
            pl.BlockSpec((tokens_here, 2 * k_cols), lambda i, c: (0, 0)),
            pl.BlockSpec((kv_group, STATE_ROWS, HD), lambda i, c: (0, 0, 0)),
        ],
    )
    return pl.pallas_call(
        split_kernel,
        grid_spec=grid_spec,
        out_shape=[kv_shape, q_shape, kv_shape, sums_shape],
    )(core.reshape(1), keys, values, queries, keys, values)


def kv_sums_kernel(kv_ref, o_ref):
    k_cols = kv_ref.shape[-1] // 2
    for head in range(o_ref.shape[0]):
        key_feature = feature(kv_ref[:, head * HD : (head + 1) * HD].astype(jnp.float32))
        value_data = kv_ref[:, k_cols + head * HD : k_cols + (head + 1) * HD].astype(jnp.float32)
        o_ref[head, :HD, :] = jnp.dot(
            key_feature.T, value_data, precision=lax.Precision.HIGHEST,
            preferred_element_type=jnp.float32,
        )
        o_ref[head, HD:, :] = jnp.zeros((STATE_ROWS - HD, HD), jnp.float32)
        o_ref[head, HD : HD + 1, :] = jnp.sum(key_feature, axis=0, keepdims=True)


def kv_sums(kv_rows):
    kv_group = kv_rows.shape[-1] // (2 * HD)
    return pl.pallas_call(
        kv_sums_kernel,
        out_shape=jax.ShapeDtypeStruct((kv_group, STATE_ROWS, HD), jnp.float32),
    )(kv_rows)


def chip_states(keep, recv_kv):
    parts = lax.axis_size("head")
    total = keep + kv_sums(recv_kv)
    steps = 2
    while steps < parts:
        across = lax.ppermute(total.astype(jnp.bfloat16), "head", [(p, p ^ steps) for p in range(parts)])
        total = total + across
        steps *= 2
    return total


def earlier_states(delta):
    count = lax.axis_size("seq")
    total = delta
    steps = 1
    while steps < count:
        total = total + shifted(total.astype(jnp.bfloat16), "seq", steps)
        steps *= 2
    return total - delta


def online_step(q_ref, k_ref, v_ref, m_sc, l_sc, acc_sc, group_size, masked):
    block = q_ref.shape[0]
    score_scale = HD ** (-0.5)
    key_rows = k_ref[...]
    value_rows = jnp.concatenate([v_ref[...], jnp.ones((block, LANES), v_ref.dtype)], axis=1)
    if masked:
        rows = lax.broadcasted_iota(jnp.int32, (block, block), 0)
        cols = lax.broadcasted_iota(jnp.int32, (block, block), 1)
        allowed = cols <= rows
    for head in range(group_size):
        lanes = slice(head * HD, (head + 1) * HD)
        scores = lax.dot_general(
            q_ref[:, lanes], key_rows, (((1,), (1,)), ((), ())),
            preferred_element_type=jnp.float32,
        )
        if masked:
            scores = jnp.where(allowed, scores, -1e30)
        m_prev = m_sc[head]
        m_new = jnp.maximum(m_prev, jnp.max(scores, axis=-1, keepdims=True) * score_scale)
        probs = jnp.exp(scores * score_scale - m_new[:, :1])
        alpha = jnp.exp(m_prev - m_new)
        both = jnp.dot(probs.astype(jnp.bfloat16), value_rows, preferred_element_type=jnp.float32)
        l_sc[head] = alpha * l_sc[head] + both[:, HD:]
        acc_sc[:, lanes] = alpha * acc_sc[:, lanes] + both[:, :HD]
        m_sc[head] = m_new


def near_kernel(qs_ref, ks_ref, first_ref, diag_ref, off_ref, q_keep, q_recv, k_keep, v_keep, k_recv,
                v_recv, acc_ref, ml_ref, m_sc, l_sc, acc_sc, *, group_size):
    step_at = pl.program_id(1)
    q_src = qs_ref[step_at]
    k_src = ks_ref[step_at]
    diag = diag_ref[step_at] == 1

    @pl.when(first_ref[step_at] == 1)
    def _init():
        m_sc[...] = jnp.full(m_sc.shape, -jnp.inf, jnp.float32)
        l_sc[...] = jnp.zeros(l_sc.shape, jnp.float32)
        acc_sc[...] = jnp.zeros(acc_sc.shape, jnp.float32)

    sources = ((q_keep, k_keep, v_keep), (q_recv, k_recv, v_recv))
    for q_at in range(2):
        for k_at in range(2):
            masked = q_at == k_at

            @pl.when((q_src == q_at) & (k_src == k_at) & (diag == masked))
            def _step():
                q_ref = sources[q_at][0]
                online_step(q_ref, sources[k_at][1], sources[k_at][2], m_sc, l_sc, acc_sc,
                            group_size, masked)

    @pl.when(diag)
    def _save():
        acc_ref[...] = acc_sc[...]
        lane = lax.broadcasted_iota(jnp.int32, ml_ref.shape, 1)
        packed = jnp.zeros(ml_ref.shape, jnp.float32)
        for head in range(group_size):
            packed = jnp.where(lane == head, m_sc[head], packed)
            packed = jnp.where(lane == group_size + head, l_sc[head], packed)
        ml_ref[...] = packed


def far_kernel(qp_ref, kp_ref, first_ref, last_ref, valid_ref, off_ref, gate_ref, q_ref, *refs,
               group_size):
    kv_refs = refs[:-7]
    s_ref, acc_in, ml_in, o_ref, m_sc, l_sc, acc_sc = refs[-7:]
    kv_head = pl.program_id(0)
    step_at = pl.program_id(1)

    @pl.when(first_ref[step_at] == 1)
    def _init():
        packed = ml_in[...]
        for head in range(group_size):
            m_sc[head] = jnp.broadcast_to(packed[:, head : head + 1], m_sc.shape[1:])
            l_sc[head] = jnp.broadcast_to(
                packed[:, group_size + head : group_size + head + 1], l_sc.shape[1:]
            )
        acc_sc[...] = acc_in[...]

    for part in range(len(kv_refs) // 2):
        @pl.when((kp_ref[step_at] == part) & (valid_ref[step_at] == 1))
        def _step():
            online_step(q_ref, kv_refs[2 * part], kv_refs[2 * part + 1], m_sc, l_sc, acc_sc,
                        group_size, False)

    @pl.when(last_ref[step_at] == 1)
    def _last():
        finish(q_ref, s_ref, gate_ref, o_ref, acc_sc, l_sc, kv_head, group_size)


def finish(q_ref, s_ref, gate_ref, o_ref, acc_sc, l_sc, kv_head, group_size):
    memory = s_ref[:HD, :]
    normalizer = s_ref[HD : HD + 1, :]
    for head in range(group_size):
        lanes = slice(head * HD, (head + 1) * HD)
        local_part = acc_sc[:, lanes] / l_sc[head]
        query_feature = feature(q_ref[:, lanes].astype(jnp.float32))
        numerator = jnp.dot(
            query_feature, memory, precision=lax.Precision.HIGHEST,
            preferred_element_type=jnp.float32,
        )
        denominator = jnp.maximum(
            jnp.sum(query_feature * normalizer, axis=-1, keepdims=True), 1.0
        )
        mixing = gate_ref[kv_head * group_size + head]
        o_ref[:, lanes] = (
            mixing * (numerator / denominator) + (1.0 - mixing) * local_part
        ).astype(o_ref.dtype)


def near_tables(core):
    tables = np.array(
        [[[c, 1 ^ c, 1 ^ c], [c, c, 1 ^ c], [1, 1, 0], [1, 0, 1]] for c in range(2)], np.int32
    )
    return jnp.asarray(tables)[core]


def far_tables(chips, chip, core, source):
    per_block = max(1, 2 * (chips - 1))
    tables = np.zeros((chips, 2, 5, per_block), np.int32)
    for y in range(chips):
        for c in range(2):
            steps = []
            k_pos = 0
            for j in range(per_block):
                valid = int(j < 2 * y)
                if valid:
                    k_pos = 2 * (chips - 1 - y + j // 2) + ((j % 2) ^ c)
                steps.append((source, k_pos, int(j == 0), int(j == per_block - 1), valid))
            tables[y, c] = np.array(steps, np.int32).T
    return jnp.asarray(tables)[chip, core]


def attend(queries, recv_q, keep_kv, recv_kv, far_kv, state, mixing, chips, chip, core, group_size):
    block, q_cols = recv_q.shape
    keep_q = queries
    kv_group = keep_kv.shape[-1] // (2 * HD)
    width = group_size * HD
    scratch = [
        pltpu.VMEM((group_size, block, LANES), jnp.float32),
        pltpu.VMEM((group_size, block, LANES), jnp.float32),
        pltpu.VMEM((block, width), jnp.float32),
    ]
    params = pltpu.CompilerParams(dimension_semantics=("arbitrary", "arbitrary"))
    near = near_tables(core)
    q_offset = jnp.reshape(core * kv_group, (1,)).astype(jnp.int32)
    q_spec = pl.BlockSpec((block, width), lambda g, t, *_: (0, g))
    own_q_spec = pl.BlockSpec((block, width), lambda g, t, *p: (0, p[-1][0] + g))
    k_spec = pl.BlockSpec((block, HD), lambda g, t, *_: (0, g))
    v_spec = pl.BlockSpec((block, HD), lambda g, t, *_: (0, kv_group + g))
    near_spec = pltpu.PrefetchScalarGridSpec(
        num_scalar_prefetch=5,
        grid=(kv_group, near.shape[-1]),
        in_specs=[own_q_spec, q_spec, k_spec, v_spec, k_spec, v_spec],
        out_specs=[
            pl.BlockSpec((None, block, width), lambda g, t, qs, ks, f, d, o: (qs[t], 0, g)),
            pl.BlockSpec(
                (None, None, block, LANES), lambda g, t, qs, ks, f, d, o: (g, qs[t], 0, 0)
            ),
        ],
        scratch_shapes=scratch,
    )
    pair_flops = 4 * block * block * HD * group_size * kv_group
    pair_exps = block * block * group_size * kv_group
    acc, ml = pl.pallas_call(
        functools.partial(near_kernel, group_size=group_size),
        grid_spec=near_spec,
        cost_estimate=pl.CostEstimate(
            flops=3 * pair_flops, transcendentals=3 * pair_exps,
            bytes_accessed=int(recv_q.size * 12 + keep_kv.size * 4),
        ),
        out_shape=[
            jax.ShapeDtypeStruct((2, block, q_cols), jnp.float32),
            jax.ShapeDtypeStruct((kv_group, 2, block, LANES), jnp.float32),
        ],
        compiler_params=params,
    )(*[near[i] for i in range(4)], q_offset, keep_q, recv_q, keep_kv, keep_kv, recv_kv, recv_kv)
    far_pairs = max(1, 2 * (chips - 1))

    def far_call(source, out_cols, col_offset):
        far = far_tables(chips, chip, core, source)
        offset = jnp.reshape(col_offset, (1,)).astype(jnp.int32)
        part_specs = []
        for _ in far_kv:
            part_specs += [k_spec, v_spec]
        far_spec = pltpu.PrefetchScalarGridSpec(
            num_scalar_prefetch=6,
            grid=(kv_group, far.shape[-1]),
            in_specs=[pl.BlockSpec(memory_space=pltpu.SMEM), own_q_spec]
            + part_specs
            + [
                pl.BlockSpec((None, STATE_ROWS, HD), lambda g, t, qp, kp, f, l, v, o: (g, 0, 0)),
                pl.BlockSpec((None, block, width), lambda g, t, qp, kp, f, l, v, o: (qp[t], 0, g)),
                pl.BlockSpec(
                    (None, None, block, LANES), lambda g, t, qp, kp, f, l, v, o: (g, qp[t], 0, 0)
                ),
            ],
            out_specs=pl.BlockSpec((block, width), lambda g, t, qp, kp, f, l, v, o: (0, o[0] + g)),
            scratch_shapes=scratch,
        )
        kv_args = []
        for part in far_kv:
            kv_args += [part, part]
        return pl.pallas_call(
            functools.partial(far_kernel, group_size=group_size),
            grid_spec=far_spec,
            cost_estimate=pl.CostEstimate(
                flops=far_pairs * pair_flops // 2, transcendentals=far_pairs * pair_exps // 2,
                bytes_accessed=int(recv_q.size * 8 + keep_kv.size * 2 * len(far_kv)),
            ),
            out_shape=jax.ShapeDtypeStruct((block, out_cols), jnp.bfloat16),
            compiler_params=params,
        )(*[far[i] for i in range(5)], offset, mixing, (keep_q, recv_q)[source], *kv_args, state,
          acc, ml)

    sibling_part = far_call(1, q_cols, 0)
    back = lax.ppermute(sibling_part, "head", [(p, p ^ 1) for p in range(lax.axis_size("head"))])
    own_part = far_call(0, 2 * q_cols, core * kv_group)
    return own_part, back


def place_kernel(col_ref, full_ref, back_ref, o_ref):
    o_ref[...] = back_ref[...]


def place_back(own_part, back, core, kv_group):
    tokens_here, q_cols = back.shape
    other = jnp.reshape(1 - core, (1,)).astype(jnp.int32)
    grid_spec = pltpu.PrefetchScalarGridSpec(
        num_scalar_prefetch=1,
        grid=(1,),
        in_specs=[
            pl.BlockSpec(memory_space=pl.ANY),
            pl.BlockSpec((tokens_here, q_cols), lambda i, c: (0, 0)),
        ],
        out_specs=pl.BlockSpec((tokens_here, q_cols), lambda i, c: (0, c[0])),
    )
    return pl.pallas_call(
        place_kernel,
        grid_spec=grid_spec,
        out_shape=jax.ShapeDtypeStruct(own_part.shape, own_part.dtype),
        input_output_aliases={1: 0},
    )(other, own_part, back)


def body(queries, keys, values, gate_logit):
    parts = lax.axis_size("head")
    chips = parts // 2
    place = lax.axis_index("head")
    chip = place // 2
    core = place % 2
    k_cols = keys.shape[1] // 2
    kv_group = k_cols // HD
    group_size = queries.shape[1] // keys.shape[1]
    sibling = [(p, p ^ 1) for p in range(parts)]

    keep_kv, send_q, send_kv, keep_sums = split_inputs(queries, keys, values, core)
    recv_q = lax.ppermute(send_q, "head", sibling)
    recv_kv = lax.ppermute(send_kv, "head", sibling)
    delta = chip_states(keep_sums, recv_kv)
    delta, keep_kv, send_kv, recv_q, recv_kv = lax.optimization_barrier(
        (delta, keep_kv, send_kv, recv_q, recv_kv)
    )
    state = earlier_states(delta)
    kv_parts = []
    for s in range(chips - 1, 0, -1):
        kv_parts.append(lax.ppermute(keep_kv, "head", [(p, p + 2 * s) for p in range(parts - 2 * s)]))
        kv_parts.append(
            lax.ppermute(send_kv, "head", [(p, (p + 2 * s) ^ 1) for p in range(parts - 2 * s)])
        )
    far_kv = kv_parts if kv_parts else [keep_kv, recv_kv]
    gate_here = lax.dynamic_slice_in_dim(gate_logit, core * kv_group * group_size, kv_group * group_size)
    mixing = jax.nn.sigmoid(gate_here)
    own_part, back = attend(
        queries, recv_q, keep_kv, recv_kv, far_kv, state, mixing, chips, chip, core, group_size
    )
    return place_back(own_part, back, core, kv_group)


def solution(mesh):
    in_specs = (P(("seq", "head"), None), P(("seq", "head"), None), P(("seq", "head"), None), P())
    out_specs = P(("seq", "head"), None)
    return jax.shard_map(body, mesh=mesh, in_specs=in_specs, out_specs=out_specs, check_vma=False)
```

```python
import functools

import jax
import jax.numpy as jnp
import numpy as np
from jax import lax
from jax.experimental import pallas as pl
from jax.experimental.pallas import tpu as pltpu
from jax.sharding import PartitionSpec as P

HQ = 32
KVH = 8
HD = 128
SEG = 2048
LANES = 128
STATE_ROWS = HD + 8


def feature(inputs):
    return jnp.where(inputs > 0, inputs + 1.0, jnp.exp(jnp.minimum(inputs, 0.0)))


def shifted(value, axis, steps):
    count = lax.axis_size(axis)
    return lax.ppermute(value, axis, [(source, source + steps) for source in range(count - steps)])


def head_sums(k_ref, v_ref, o_ref):
    for head in range(o_ref.shape[0]):
        lanes = slice(head * HD, (head + 1) * HD)
        key_feature = feature(k_ref[:, lanes].astype(jnp.float32))
        value_data = v_ref[:, lanes].astype(jnp.float32)
        o_ref[head, :HD, :] = jnp.dot(
            key_feature.T, value_data, precision=lax.Precision.HIGH,
            preferred_element_type=jnp.float32,
        )
        o_ref[head, HD:, :] = jnp.zeros((STATE_ROWS - HD, HD), jnp.float32)
        o_ref[head, HD : HD + 1, :] = jnp.sum(key_feature, axis=0, keepdims=True)


def split_kernel(core_ref, k_keep, v_keep, q_send, k_send, v_send, *out_refs):
    k_cols = k_keep.shape[-1]
    keep_kv, send_q, send_kv, keep_sums, send_sums = out_refs
    keep_kv[:, :k_cols] = k_keep[...]
    keep_kv[:, k_cols:] = v_keep[...]
    send_q[...] = q_send[...]
    send_kv[:, :k_cols] = k_send[...]
    send_kv[:, k_cols:] = v_send[...]
    head_sums(k_keep, v_keep, keep_sums)
    head_sums(k_send, v_send, send_sums)


def split_inputs(queries, keys, values, core):
    tokens_here, q_all = queries.shape
    q_cols = q_all // 2
    k_cols = keys.shape[1] // 2
    kv_group = k_cols // HD
    keep_map = lambda i, c: (0, c[0])
    send_map = lambda i, c: (0, 1 - c[0])
    q_shape = jax.ShapeDtypeStruct((tokens_here, q_cols), queries.dtype)
    kv_shape = jax.ShapeDtypeStruct((tokens_here, 2 * k_cols), keys.dtype)
    sums_shape = jax.ShapeDtypeStruct((kv_group, STATE_ROWS, HD), jnp.float32)
    grid_spec = pltpu.PrefetchScalarGridSpec(
        num_scalar_prefetch=1,
        grid=(1,),
        in_specs=[
            pl.BlockSpec((tokens_here, k_cols), keep_map),
            pl.BlockSpec((tokens_here, k_cols), keep_map),
            pl.BlockSpec((tokens_here, q_cols), send_map),
            pl.BlockSpec((tokens_here, k_cols), send_map),
            pl.BlockSpec((tokens_here, k_cols), send_map),
        ],
        out_specs=[
            pl.BlockSpec((tokens_here, 2 * k_cols), lambda i, c: (0, 0)),
            pl.BlockSpec((tokens_here, q_cols), lambda i, c: (0, 0)),
            pl.BlockSpec((tokens_here, 2 * k_cols), lambda i, c: (0, 0)),
            pl.BlockSpec((kv_group, STATE_ROWS, HD), lambda i, c: (0, 0, 0)),
            pl.BlockSpec((kv_group, STATE_ROWS, HD), lambda i, c: (0, 0, 0)),
        ],
    )
    return pl.pallas_call(
        split_kernel,
        grid_spec=grid_spec,
        out_shape=[kv_shape, q_shape, kv_shape, sums_shape, sums_shape],
    )(core.reshape(1), keys, values, queries, keys, values)


def chip_states(keep, send):
    parts = lax.axis_size("head")
    total = keep + lax.ppermute(send.astype(jnp.bfloat16), "head", [(p, p ^ 1) for p in range(parts)])
    steps = 2
    while steps < parts:
        across = lax.ppermute(total.astype(jnp.bfloat16), "head", [(p, p ^ steps) for p in range(parts)])
        total = total + across
        steps *= 2
    return total


def earlier_states(delta):
    count = lax.axis_size("seq")
    total = delta
    steps = 1
    while steps < count:
        total = total + shifted(total.astype(jnp.bfloat16), "seq", steps)
        steps *= 2
    return total - delta


def online_step(q_ref, k_ref, v_ref, m_sc, l_sc, acc_sc, group_size, masked):
    block = q_ref.shape[0]
    score_scale = HD ** (-0.5)
    key_rows = k_ref[...]
    value_rows = jnp.concatenate([v_ref[...], jnp.ones((block, LANES), v_ref.dtype)], axis=1)
    if masked:
        rows = lax.broadcasted_iota(jnp.int32, (block, block), 0)
        cols = lax.broadcasted_iota(jnp.int32, (block, block), 1)
        allowed = cols <= rows
    for head in range(group_size):
        lanes = slice(head * HD, (head + 1) * HD)
        scores = lax.dot_general(
            q_ref[:, lanes], key_rows, (((1,), (1,)), ((), ())),
            preferred_element_type=jnp.float32,
        )
        if masked:
            scores = jnp.where(allowed, scores, -1e30)
        m_prev = m_sc[head]
        m_new = jnp.maximum(m_prev, jnp.max(scores, axis=-1, keepdims=True) * score_scale)
        probs = jnp.exp(scores * score_scale - m_new[:, :1])
        alpha = jnp.exp(m_prev - m_new)
        both = jnp.dot(probs.astype(jnp.bfloat16), value_rows, preferred_element_type=jnp.float32)
        l_sc[head] = alpha * l_sc[head] + both[:, HD:]
        acc_sc[:, lanes] = alpha * acc_sc[:, lanes] + both[:, :HD]
        m_sc[head] = m_new


def near_kernel(qs_ref, ks_ref, first_ref, diag_ref, off_ref, q_keep, q_recv, k_keep, v_keep, k_recv,
                v_recv, acc_ref, ml_ref, m_sc, l_sc, acc_sc, *, group_size):
    step_at = pl.program_id(1)
    q_src = qs_ref[step_at]
    k_src = ks_ref[step_at]
    diag = diag_ref[step_at] == 1

    @pl.when(first_ref[step_at] == 1)
    def _init():
        m_sc[...] = jnp.full(m_sc.shape, -jnp.inf, jnp.float32)
        l_sc[...] = jnp.zeros(l_sc.shape, jnp.float32)
        acc_sc[...] = jnp.zeros(acc_sc.shape, jnp.float32)

    sources = ((q_keep, k_keep, v_keep), (q_recv, k_recv, v_recv))
    for q_at in range(2):
        for k_at in range(2):
            masked = q_at == k_at

            @pl.when((q_src == q_at) & (k_src == k_at) & (diag == masked))
            def _step():
                q_ref = sources[q_at][0]
                online_step(q_ref, sources[k_at][1], sources[k_at][2], m_sc, l_sc, acc_sc,
                            group_size, masked)

    @pl.when(diag)
    def _save():
        acc_ref[...] = acc_sc[...]
        lane = lax.broadcasted_iota(jnp.int32, ml_ref.shape, 1)
        packed = jnp.zeros(ml_ref.shape, jnp.float32)
        for head in range(group_size):
            packed = jnp.where(lane == head, m_sc[head], packed)
            packed = jnp.where(lane == group_size + head, l_sc[head], packed)
        ml_ref[...] = packed


def far_kernel(qp_ref, kp_ref, first_ref, last_ref, valid_ref, off_ref, gate_ref, q_ref, *refs,
               group_size):
    kv_refs = refs[:-7]
    s_ref, acc_in, ml_in, o_ref, m_sc, l_sc, acc_sc = refs[-7:]
    kv_head = pl.program_id(0)
    step_at = pl.program_id(1)

    @pl.when(first_ref[step_at] == 1)
    def _init():
        packed = ml_in[...]
        for head in range(group_size):
            m_sc[head] = jnp.broadcast_to(packed[:, head : head + 1], m_sc.shape[1:])
            l_sc[head] = jnp.broadcast_to(
                packed[:, group_size + head : group_size + head + 1], l_sc.shape[1:]
            )
        acc_sc[...] = acc_in[...]

    for part in range(len(kv_refs) // 2):
        @pl.when((kp_ref[step_at] == part) & (valid_ref[step_at] == 1))
        def _step():
            online_step(q_ref, kv_refs[2 * part], kv_refs[2 * part + 1], m_sc, l_sc, acc_sc,
                        group_size, False)

    @pl.when(last_ref[step_at] == 1)
    def _last():
        finish(q_ref, s_ref, gate_ref, o_ref, acc_sc, l_sc, kv_head, group_size)


def finish(q_ref, s_ref, gate_ref, o_ref, acc_sc, l_sc, kv_head, group_size):
    memory = s_ref[:HD, :]
    normalizer = s_ref[HD : HD + 1, :]
    for head in range(group_size):
        lanes = slice(head * HD, (head + 1) * HD)
        local_part = acc_sc[:, lanes] / l_sc[head]
        query_feature = feature(q_ref[:, lanes].astype(jnp.float32))
        numerator = jnp.dot(
            query_feature, memory, precision=lax.Precision.HIGH,
            preferred_element_type=jnp.float32,
        )
        denominator = jnp.maximum(
            jnp.sum(query_feature * normalizer, axis=-1, keepdims=True), 1.0
        )
        mixing = gate_ref[kv_head * group_size + head]
        o_ref[:, lanes] = (
            mixing * (numerator / denominator) + (1.0 - mixing) * local_part
        ).astype(o_ref.dtype)


def near_tables(core):
    tables = np.array(
        [[[c, 1 ^ c, 1 ^ c], [c, c, 1 ^ c], [1, 1, 0], [1, 0, 1]] for c in range(2)], np.int32
    )
    return jnp.asarray(tables)[core]


def far_tables(chips, chip, core, source):
    per_block = max(1, 2 * (chips - 1))
    tables = np.zeros((chips, 2, 5, per_block), np.int32)
    for y in range(chips):
        for c in range(2):
            steps = []
            k_pos = 0
            for j in range(per_block):
                valid = int(j < 2 * y)
                if valid:
                    k_pos = 2 * (chips - 1 - y + j // 2) + ((j % 2) ^ c)
                steps.append((source, k_pos, int(j == 0), int(j == per_block - 1), valid))
            tables[y, c] = np.array(steps, np.int32).T
    return jnp.asarray(tables)[chip, core]


def attend(queries, recv_q, keep_kv, recv_kv, far_kv, state, mixing, chips, chip, core, group_size):
    block, q_cols = recv_q.shape
    keep_q = queries
    kv_group = keep_kv.shape[-1] // (2 * HD)
    width = group_size * HD
    scratch = [
        pltpu.VMEM((group_size, block, LANES), jnp.float32),
        pltpu.VMEM((group_size, block, LANES), jnp.float32),
        pltpu.VMEM((block, width), jnp.float32),
    ]
    params = pltpu.CompilerParams(dimension_semantics=("arbitrary", "arbitrary"))
    near = near_tables(core)
    q_offset = jnp.reshape(core * kv_group, (1,)).astype(jnp.int32)
    q_spec = pl.BlockSpec((block, width), lambda g, t, *_: (0, g))
    own_q_spec = pl.BlockSpec((block, width), lambda g, t, *p: (0, p[-1][0] + g))
    k_spec = pl.BlockSpec((block, HD), lambda g, t, *_: (0, g))
    v_spec = pl.BlockSpec((block, HD), lambda g, t, *_: (0, kv_group + g))
    near_spec = pltpu.PrefetchScalarGridSpec(
        num_scalar_prefetch=5,
        grid=(kv_group, near.shape[-1]),
        in_specs=[own_q_spec, q_spec, k_spec, v_spec, k_spec, v_spec],
        out_specs=[
            pl.BlockSpec((None, block, width), lambda g, t, qs, ks, f, d, o: (qs[t], 0, g)),
            pl.BlockSpec(
                (None, None, block, LANES), lambda g, t, qs, ks, f, d, o: (g, qs[t], 0, 0)
            ),
        ],
        scratch_shapes=scratch,
    )
    pair_flops = 4 * block * block * HD * group_size * kv_group
    pair_exps = block * block * group_size * kv_group
    acc, ml = pl.pallas_call(
        functools.partial(near_kernel, group_size=group_size),
        grid_spec=near_spec,
        cost_estimate=pl.CostEstimate(
            flops=3 * pair_flops, transcendentals=3 * pair_exps,
            bytes_accessed=int(recv_q.size * 12 + keep_kv.size * 4),
        ),
        out_shape=[
            jax.ShapeDtypeStruct((2, block, q_cols), jnp.float32),
            jax.ShapeDtypeStruct((kv_group, 2, block, LANES), jnp.float32),
        ],
        compiler_params=params,
    )(*[near[i] for i in range(4)], q_offset, keep_q, recv_q, keep_kv, keep_kv, recv_kv, recv_kv)
    far_pairs = max(1, 2 * (chips - 1))

    def far_call(source, out_cols, col_offset):
        far = far_tables(chips, chip, core, source)
        offset = jnp.reshape(col_offset, (1,)).astype(jnp.int32)
        part_specs = []
        for _ in far_kv:
            part_specs += [k_spec, v_spec]
        far_spec = pltpu.PrefetchScalarGridSpec(
            num_scalar_prefetch=6,
            grid=(kv_group, far.shape[-1]),
            in_specs=[pl.BlockSpec(memory_space=pltpu.SMEM), own_q_spec]
            + part_specs
            + [
                pl.BlockSpec((None, STATE_ROWS, HD), lambda g, t, qp, kp, f, l, v, o: (g, 0, 0)),
                pl.BlockSpec((None, block, width), lambda g, t, qp, kp, f, l, v, o: (qp[t], 0, g)),
                pl.BlockSpec(
                    (None, None, block, LANES), lambda g, t, qp, kp, f, l, v, o: (g, qp[t], 0, 0)
                ),
            ],
            out_specs=pl.BlockSpec((block, width), lambda g, t, qp, kp, f, l, v, o: (0, o[0] + g)),
            scratch_shapes=scratch,
        )
        kv_args = []
        for part in far_kv:
            kv_args += [part, part]
        return pl.pallas_call(
            functools.partial(far_kernel, group_size=group_size),
            grid_spec=far_spec,
            cost_estimate=pl.CostEstimate(
                flops=far_pairs * pair_flops // 2, transcendentals=far_pairs * pair_exps // 2,
                bytes_accessed=int(recv_q.size * 8 + keep_kv.size * 2 * len(far_kv)),
            ),
            out_shape=jax.ShapeDtypeStruct((block, out_cols), jnp.bfloat16),
            compiler_params=params,
        )(*[far[i] for i in range(5)], offset, mixing, (keep_q, recv_q)[source], *kv_args, state,
          acc, ml)

    sibling_part = far_call(1, q_cols, 0)
    back = lax.ppermute(sibling_part, "head", [(p, p ^ 1) for p in range(lax.axis_size("head"))])
    own_part = far_call(0, 2 * q_cols, core * kv_group)
    return own_part, back


def place_kernel(col_ref, full_ref, back_ref, o_ref):
    o_ref[...] = back_ref[...]


def place_back(own_part, back, core, kv_group):
    tokens_here, q_cols = back.shape
    other = jnp.reshape(1 - core, (1,)).astype(jnp.int32)
    grid_spec = pltpu.PrefetchScalarGridSpec(
        num_scalar_prefetch=1,
        grid=(1,),
        in_specs=[
            pl.BlockSpec(memory_space=pl.ANY),
            pl.BlockSpec((tokens_here, q_cols), lambda i, c: (0, 0)),
        ],
        out_specs=pl.BlockSpec((tokens_here, q_cols), lambda i, c: (0, c[0])),
    )
    return pl.pallas_call(
        place_kernel,
        grid_spec=grid_spec,
        out_shape=jax.ShapeDtypeStruct(own_part.shape, own_part.dtype),
        input_output_aliases={1: 0},
    )(other, own_part, back)


def body(queries, keys, values, gate_logit):
    parts = lax.axis_size("head")
    chips = parts // 2
    place = lax.axis_index("head")
    chip = place // 2
    core = place % 2
    k_cols = keys.shape[1] // 2
    kv_group = k_cols // HD
    group_size = queries.shape[1] // keys.shape[1]
    sibling = [(p, p ^ 1) for p in range(parts)]

    keep_kv, send_q, send_kv, keep_sums, send_sums = split_inputs(queries, keys, values, core)
    delta = chip_states(keep_sums, send_sums)
    recv_q = lax.ppermute(send_q, "head", sibling)
    recv_kv = lax.ppermute(send_kv, "head", sibling)
    delta, keep_kv, send_kv, recv_q, recv_kv = lax.optimization_barrier(
        (delta, keep_kv, send_kv, recv_q, recv_kv)
    )
    state = earlier_states(delta)
    kv_parts = []
    for s in range(chips - 1, 0, -1):
        kv_parts.append(lax.ppermute(keep_kv, "head", [(p, p + 2 * s) for p in range(parts - 2 * s)]))
        kv_parts.append(
            lax.ppermute(send_kv, "head", [(p, (p + 2 * s) ^ 1) for p in range(parts - 2 * s)])
        )
    far_kv = kv_parts if kv_parts else [keep_kv, recv_kv]
    gate_here = lax.dynamic_slice_in_dim(gate_logit, core * kv_group * group_size, kv_group * group_size)
    mixing = jax.nn.sigmoid(gate_here)
    own_part, back = attend(
        queries, recv_q, keep_kv, recv_kv, far_kv, state, mixing, chips, chip, core, group_size
    )
    return place_back(own_part, back, core, kv_group)


def solution(mesh):
    in_specs = (P(("seq", "head"), None), P(("seq", "head"), None), P(("seq", "head"), None), P())
    out_specs = P(("seq", "head"), None)
    return jax.shard_map(body, mesh=mesh, in_specs=in_specs, out_specs=out_specs, check_vma=False)
```
